32 devices in a mesh: sec: 2 (over x), ta: 4 (over z), sa: 4 (over y, core).
Axes of the slice: x: 2, y: 2, z: 4, core: 2. Of those that a mesh axis runs over, the one named last changes fastest.
Arguments:
- gauge_links: float32 [4, 3, 3, 2, 16, 16, 256], P(None, None, None, None, 'ta', 'sa'), may hold values from -2.5 to 2.5
- noise_slabs: float32 [8, 3, 2, 4, 16, 256], P('sec', None, None, 'ta', 'sa'), may hold values from -6 to 6
- offsets: int32 [8], replicated, may hold values from 0 to 3, as said below
- vectors: bfloat16 [16, 32, 3, 2, 16, 256], P('ta', 'sec', None, None, 'sa'), may hold values from -0.0390625 to 0.0390625
Outputs:
- perambulator: float32 [8, 4, 2, 16, 32], P('sec', None, None, 'ta', 'sa')
The draws below stay inside these ranges and needn't reach their ends.
Inputs may be any that keep to these rules, and one draw needn't show every extreme that they name: `offsets`: each value from 0 to 3 is the offset of exactly 2 right-hand sides.
All inputs are finite; a program needn't handle non-finite values.
Results may differ from the reference program's by a relative error of at most 0.003.
Values may be sent and summed in bfloat16 or wider, within the bound.
No kernel may reach another device: no remote copies, remote signals or barrier semaphores. Data moves between devices by JAX's collectives and lax.ppermute only.
A program may use at most 128 MiB of HBM per device.

```python
import jax
import jax.numpy as jnp
from jax import lax

NX = 32
NY = 8
NVEC = 32
TDIL = 4
ITERS = 2
NT = 16
NZ = 16
NYX = 256
NRHS = 8


def draw_offsets(key, part):
    order = jax.random.permutation(key, NRHS)
    return (order % TDIL).astype(jnp.int32)


def block_scale(stream_key, dims, split, smallest, largest):
    def one(axis_at, shards_of):
        heights = jax.random.uniform(jax.random.fold_in(jax.random.fold_in(stream_key, 6), axis_at), (shards_of,), jnp.float32, smallest / len(split), largest / len(split))
        return jnp.repeat(jnp.exp(heights), dims[axis_at] // shards_of).reshape((-1,) + (1,) * (len(dims) - axis_at - 1))

    gain = one(*split[0])
    for cut in split[1:]:
        gain = gain * one(*cut)
    return gain


def normal_values(stream_key, dims, spread, limit, cuts=(), kind=jnp.bfloat16):
    entries = jax.random.normal(stream_key, dims, jnp.float32) * spread
    if len(cuts) > 0:
        entries = block_scale(stream_key, dims, cuts, -0.22, 0.18) * entries
    return jnp.clip(entries, min=-limit, max=limit).astype(kind)


def setup_inputs(seed: int = 0) -> dict:
    key_list = jax.random.split(jax.random.key(seed), 5)
    return {
        "gauge_links": normal_values(key_list[0], (4, 3, 3, 2, NT, NZ, NYX), 6 ** -0.5, 2.5, ((4, 4), (5, 4)), jnp.float32),
        "noise_slabs": normal_values(key_list[1], (NRHS, 3, 2, NT // TDIL, NZ, NYX), 1.0, 6.0, ((0, 2), (3, 4), (4, 4)), jnp.float32),
        "offsets": draw_offsets(jax.random.fold_in(key_list[4], 71), 0),
        "vectors": normal_values(key_list[3], (NT, NVEC, 3, 2, NZ, NYX), (6 * NX * NY * NZ) ** -0.5, 0.0390625, ((0, 4), (1, 2), (4, 4))),
    }


kappa_hop = 0.12
GAMMA_PERM = ((3, 2, 1, 0), (3, 2, 1, 0), (2, 3, 0, 1), (2, 3, 0, 1))
GAMMA_REAL = ((0, 0, 0, 0), (-1, 1, 1, -1), (0, 0, 0, 0), (1, 1, 1, 1))
GAMMA_IMAG = ((1, 1, -1, -1), (0, 0, 0, 0), (1, -1, -1, 1), (0, 0, 0, 0))


def phase_times(operand, phase_real, phase_imag):
    if phase_imag == 0:
        return operand * float(phase_real)
    dim_reim = operand.ndim - 4
    real_part = lax.index_in_dim(operand, 0, dim_reim, False)
    imag_part = lax.index_in_dim(operand, 1, dim_reim, False)
    return jnp.stack([-float(phase_imag) * imag_part, float(phase_imag) * real_part], axis=dim_reim)


def spin_row(operand, index):
    return lax.index_in_dim(operand, index, operand.ndim - 6, False)


def spin_project(operand, direction, orient, row_count):
    row_list = []
    for s in range(row_count):
        partner = spin_row(operand, GAMMA_PERM[direction][s])
        row_list.append(spin_row(operand, s) + phase_times(partner, orient * GAMMA_REAL[direction][s], orient * GAMMA_IMAG[direction][s]))
    return jnp.stack(row_list, axis=operand.ndim - 6)


def colour_product(gauge_field, operand, dagger):
    dim_colour = operand.ndim - 5
    row_list = []
    for a in range(3):
        sum_real = None
        sum_imag = None
        for b in range(3):
            if dagger:
                link_real = gauge_field[b, a, 0]
                link_imag = -gauge_field[b, a, 1]
            else:
                link_real = gauge_field[a, b, 0]
                link_imag = gauge_field[a, b, 1]
            column = lax.index_in_dim(operand, b, dim_colour, False)
            column_real = lax.index_in_dim(column, 0, column.ndim - 4, False)
            column_imag = lax.index_in_dim(column, 1, column.ndim - 4, False)
            term_real = link_real * column_real - link_imag * column_imag
            term_imag = link_real * column_imag + link_imag * column_real
            sum_real = term_real if sum_real is None else sum_real + term_real
            sum_imag = term_imag if sum_imag is None else sum_imag + term_imag
        row_list.append(jnp.stack([sum_real, sum_imag], axis=sum_real.ndim - 3))
    return jnp.stack(row_list, axis=dim_colour)


def move_first(operand, stride):
    positions = jnp.arange(operand.shape[-1]) % NX
    if stride == 1:
        return jnp.where(positions == NX - 1, jnp.roll(operand, NX - 1, axis=-1), jnp.roll(operand, -1, axis=-1))
    return jnp.where(positions == 0, jnp.roll(operand, 1 - NX, axis=-1), jnp.roll(operand, 1, axis=-1))


def move_second(operand, stride):
    return jnp.roll(operand, -stride * NX, axis=-1)


def spatial_terms(spinor, gauge_links):
    movers = (move_first, move_second)
    summed = None
    for d in (0, 1):
        gauge_field = gauge_links[d]
        forward = spin_project(colour_product(gauge_field, movers[d](spinor, 1), False), d, -1.0, 4)
        backward = spin_project(colour_product(movers[d](gauge_field, -1), movers[d](spinor, -1), True), d, 1.0, 4)
        summed = forward + backward if summed is None else summed + forward + backward
    return summed


def global_move(operand, direction, stride, fermion):
    slab_axis = -2 if direction == 2 else -3
    shifted = jnp.roll(operand, -stride, axis=slab_axis)
    if fermion and direction == 3:
        edge_index = NT - 1 if stride == 1 else 0
        rim_sign = jnp.where(jnp.arange(NT) == edge_index, -1.0, 1.0).astype(jnp.float32)
        shifted = shifted * rim_sign[:, None, None]
    return shifted


def hopping(spinor, gauge_links):
    summed = spatial_terms(spinor, gauge_links)
    for d in (2, 3):
        gauge_field = gauge_links[d]
        summed = summed + spin_project(colour_product(gauge_field, global_move(spinor, d, 1, True), False), d, -1.0, 4)
        summed = summed + spin_project(colour_product(global_move(gauge_field, d, -1, False), global_move(spinor, d, -1, True), True), d, 1.0, 4)
    return summed


def reference(gauge_links, noise_slabs, offsets, vectors):
    vectors_wide = vectors.astype(jnp.float32)

    def solve_project(r):
        noise_one = lax.dynamic_index_in_dim(noise_slabs, r, 0, False)
        filled = jnp.repeat(noise_one, TDIL, axis=2)
        time_mask = (jnp.arange(NT).astype(jnp.int32) % TDIL == offsets[r]).astype(jnp.float32)
        spin_mask = (jnp.arange(4).astype(jnp.int32) == r % 4).astype(jnp.float32)
        source = spin_mask[:, None, None, None, None, None] * (filled * time_mask[:, None, None])[None]
        spinor = source
        for _ in range(ITERS):
            residual = source - (spinor - kappa_hop * hopping(spinor, gauge_links))
            spinor = spinor + residual
        rounded = lax.optimization_barrier(spinor.astype(jnp.bfloat16)).astype(jnp.float32)
        products = jnp.einsum("tvcazs,qcbtzs->qabtv", vectors_wide, rounded, precision=lax.Precision.HIGHEST)
        real_part = products[:, 0, 0] + products[:, 1, 1]
        imag_part = products[:, 0, 1] - products[:, 1, 0]
        return jnp.stack([real_part, imag_part], axis=1)

    return lax.map(solve_project, jnp.arange(NRHS).astype(jnp.int32))
```

```python
import functools

import jax
import jax.numpy as jnp
from jax import lax
from jax.experimental import pallas as pl
from jax.experimental.pallas import tpu as pltpu
from jax.sharding import PartitionSpec as P

NX = 32
TDIL = 4
ITERS = 2
INTERPRET = False


kappa_hop = 0.12
GAMMA_PERM = ((3, 2, 1, 0), (3, 2, 1, 0), (2, 3, 0, 1), (2, 3, 0, 1))
GAMMA_REAL = ((0, 0, 0, 0), (-1, 1, 1, -1), (0, 0, 0, 0), (1, 1, 1, 1))
GAMMA_IMAG = ((1, 1, -1, -1), (0, 0, 0, 0), (1, -1, -1, 1), (0, 0, 0, 0))


def passed_along(value, axis, steps):
    count = lax.axis_size(axis)
    pairs = [(source, (source + steps) % count) for source in range(count)]
    return lax.ppermute(value, axis, pairs)


def from_partner(x, axis, stride):
    return lax.ppermute(x, axis, [(i, i ^ 1 << stride) for i in range(lax.axis_size(axis))])


def times_phase(re, im, cr, ci):
    if ci == 0:
        if cr == 1:
            return re, im
        return -re, -im
    if ci == 1:
        return -im, re
    return im, -re


def move_first(operand, stride):
    positions = jnp.arange(operand.shape[-1]) % NX
    if stride == 1:
        return jnp.where(
            positions == NX - 1, jnp.roll(operand, NX - 1, axis=-1), jnp.roll(operand, -1, axis=-1)
        )
    return jnp.where(
        positions == 0, jnp.roll(operand, 1 - NX, axis=-1), jnp.roll(operand, 1, axis=-1)
    )


def move_second(operand, stride):
    return jnp.roll(operand, -stride * NX, axis=-1)


def hop_kernel(p_ref, u_ref, b_ref, src_ref, out_ref):
    T = out_ref.shape[3]
    Z = out_ref.shape[4]
    L = out_ref.shape[5]
    rows = p_ref.shape[4]
    xpos = lax.broadcasted_iota(jnp.int32, (Z, L), 1) % NX
    x_last = xpos == NX - 1
    x_first = xpos == 0

    def body(t, carry):
        acc = [[[None, None] for _ in range(3)] for _ in range(4)]

        def shifted(s, c, ri, mu, stride):
            if mu == 3:
                return p_ref[s, c, ri, t + 1 + stride, pl.ds(0, Z), :]
            if mu == 2:
                full = p_ref[s, c, ri, t + 1, :, :]
                full = pltpu.roll(full, rows - 1 if stride == 1 else 1, axis=0)
                return full[:Z]
            v = p_ref[s, c, ri, t + 1, pl.ds(0, Z), :]
            if mu == 1:
                return pltpu.roll(v, (L - NX) if stride == 1 else NX, axis=1)
            if stride == 1:
                return jnp.where(x_last, pltpu.roll(v, NX - 1, axis=1), pltpu.roll(v, L - 1, axis=1))
            return jnp.where(x_first, pltpu.roll(v, L - NX + 1, axis=1), pltpu.roll(v, 1, axis=1))

        for mu in range(4):
            perm = GAMMA_PERM[mu]
            heads = [0, 1]
            for stride in (1, -1):
                orient = -1 if stride == 1 else 1
                half = []
                for s in heads:
                    p = perm[s]
                    cr, ci = orient * GAMMA_REAL[mu][s], orient * GAMMA_IMAG[mu][s]
                    colours = []
                    for c in range(3):
                        sre = shifted(s, c, 0, mu, stride)
                        sim = shifted(s, c, 1, mu, stride)
                        pre, pim = times_phase(shifted(p, c, 0, mu, stride), shifted(p, c, 1, mu, stride), cr, ci)
                        colours.append((sre + pre, sim + pim))
                    half.append(colours)
                links = u_ref if stride == 1 else b_ref
                for k, s in enumerate(heads):
                    p = perm[s]
                    cpr, cpi = orient * GAMMA_REAL[mu][p], orient * GAMMA_IMAG[mu][p]
                    for a in range(3):
                        sum_re = None
                        sum_im = None
                        for b in range(3):
                            if stride == 1:
                                lre = links[mu, a, b, 0, t]
                                lim = links[mu, a, b, 1, t]
                                hre, him = half[k][b]
                                tre = lre * hre - lim * him
                                tim = lre * him + lim * hre
                            else:
                                lre = links[mu, b, a, 0, t]
                                lim = links[mu, b, a, 1, t]
                                hre, him = half[k][b]
                                tre = lre * hre + lim * him
                                tim = lre * him - lim * hre
                            sum_re = tre if sum_re is None else sum_re + tre
                            sum_im = tim if sum_im is None else sum_im + tim
                        for row, (vre, vim) in ((s, (sum_re, sum_im)), (p, times_phase(sum_re, sum_im, cpr, cpi))):
                            if acc[row][a][0] is None:
                                acc[row][a] = [vre, vim]
                            else:
                                acc[row][a] = [acc[row][a][0] + vre, acc[row][a][1] + vim]
        for s in range(4):
            for c in range(3):
                for ri in range(2):
                    psi = p_ref[s, c, ri, t + 1, pl.ds(0, Z), :]
                    src = src_ref[s, c, ri, t]
                    residual = src - (psi - kappa_hop * acc[s][c][ri])
                    out_ref[s, c, ri, t] = psi + residual
        return carry

    lax.fori_loop(0, T, body, 0)


def hopping_step(padded, links, back_links, source):
    R, S, C, RI, T, Z, L = source.shape
    rows = padded.shape[5]
    spinor_block = pl.BlockSpec((None, S, C, RI, T + 2, rows, L), lambda r: (r, 0, 0, 0, 0, 0, 0))
    link_block = pl.BlockSpec(links.shape, lambda r: (0,) * 7)
    site_block = pl.BlockSpec((None, S, C, RI, T, Z, L), lambda r: (r, 0, 0, 0, 0, 0, 0))
    return pl.pallas_call(
        hop_kernel,
        grid=(R,),
        in_specs=[spinor_block, link_block, link_block, site_block],
        out_specs=site_block,
        out_shape=jax.ShapeDtypeStruct(source.shape, jnp.float32),
        compiler_params=pltpu.CompilerParams(dimension_semantics=("arbitrary",)),
        interpret=INTERPRET,
    )(padded, links, back_links, source)


def padded_spinor(spinor, lower_sign, upper_sign):
    R, S, C, RI, T, Z, L = spinor.shape
    rows = -(-(Z + 2) // 8) * 8
    t_lo = passed_along(spinor[:, :, :, :, T - 1:, :, :], "ta", 1) * lower_sign
    t_hi = passed_along(spinor[:, :, :, :, :1, :, :], "ta", -1) * upper_sign
    z_lo = passed_along(spinor[:, :, :, :, :, Z - 1:, :], "sa", 1)
    z_hi = passed_along(spinor[:, :, :, :, :, :1, :], "sa", -1)
    gap = jnp.zeros((R, S, C, RI, T, rows - Z - 2, L), jnp.float32)
    middle = jnp.concatenate([spinor, z_hi, gap, z_lo], axis=5)
    t_pad = ((0, 0),) * 5 + ((0, rows - Z), (0, 0))
    return jnp.concatenate([jnp.pad(t_lo, t_pad), middle, jnp.pad(t_hi, t_pad)], axis=4)


def intersection_part(rounded, vector_piece):
    products = jnp.einsum(
        "tvcazs,rqcbtzs->rqabtv", vector_piece, rounded, preferred_element_type=jnp.float32
    )
    real_part = products[:, :, 0, 0] + products[:, :, 1, 1]
    imag_part = products[:, :, 0, 1] - products[:, :, 1, 0]
    return jnp.stack([real_part, imag_part], axis=2)


def local(gauge_links, noise_slabs, offsets, vectors):
    partner_vectors = from_partner(vectors, "sec", 0)
    batch_rows = noise_slabs.shape[0]
    slab_length = gauge_links.shape[4]
    section_index = lax.axis_index("sec")
    slab_index = lax.axis_index("ta")
    slab_count = lax.axis_size("ta")
    lower_sign = jnp.where(slab_index == 0, -1.0, 1.0).astype(jnp.float32)
    upper_sign = jnp.where(slab_index == slab_count - 1, -1.0, 1.0).astype(jnp.float32)
    filled = jnp.repeat(noise_slabs, TDIL, axis=3)
    global_time = slab_index * slab_length + jnp.arange(slab_length)
    own_offsets = lax.dynamic_slice_in_dim(offsets, section_index * batch_rows, batch_rows)
    time_mask = (global_time[None, :] % TDIL == own_offsets[:, None]).astype(jnp.float32)
    rhs_index = section_index * batch_rows + jnp.arange(batch_rows)
    spin_mask = (jnp.arange(4)[None, :] == rhs_index[:, None] % 4).astype(jnp.float32)
    source = (
        spin_mask[:, :, None, None, None, None, None]
        * (filled * time_mask[:, None, None, :, None, None])[:, None]
    )
    time_edge = passed_along(gauge_links[3, :, :, :, -1:, :, :], "ta", 1)
    space_edge = passed_along(gauge_links[2, :, :, :, :, -1:, :], "sa", 1)
    back_links = jnp.stack(
        [
            move_first(gauge_links[0], -1),
            move_second(gauge_links[1], -1),
            jnp.concatenate([space_edge, gauge_links[2, :, :, :, :, :-1, :]], axis=4),
            jnp.concatenate([time_edge, gauge_links[3, :, :, :, :-1, :, :]], axis=3),
        ]
    )
    spinor = source
    for _ in range(ITERS):
        padded = padded_spinor(spinor, lower_sign, upper_sign)
        spinor = hopping_step(padded, gauge_links, back_links, source)
    rounded = spinor.astype(jnp.bfloat16)
    own_part = intersection_part(rounded, vectors)
    partner_part = intersection_part(rounded, partner_vectors)
    lower_half = jnp.where(section_index == 0, own_part, partner_part)
    upper_half = jnp.where(section_index == 0, partner_part, own_part)
    partial_value = jnp.concatenate([lower_half, upper_half], axis=4)
    return lax.psum_scatter(partial_value, "sa", scatter_dimension=4, tiled=True)


def solution(mesh):
    in_specs = (
        P(None, None, None, None, "ta", "sa", None),
        P("sec", None, None, "ta", "sa", None),
        P(),
        P("ta", "sec", None, None, "sa", None),
    )
    out_specs = P("sec", None, None, "ta", "sa")
    return jax.shard_map(local, mesh=mesh, in_specs=in_specs, out_specs=out_specs, check_vma=False)
```

```python
import functools

import jax
import jax.numpy as jnp
from jax import lax
from jax.experimental import pallas as pl
from jax.experimental.pallas import tpu as pltpu
from jax.sharding import PartitionSpec as P

NX = 32
TDIL = 4
ITERS = 2
INTERPRET = False


kappa_hop = 0.12
GAMMA_PERM = ((3, 2, 1, 0), (3, 2, 1, 0), (2, 3, 0, 1), (2, 3, 0, 1))
GAMMA_REAL = ((0, 0, 0, 0), (-1, 1, 1, -1), (0, 0, 0, 0), (1, 1, 1, 1))
GAMMA_IMAG = ((1, 1, -1, -1), (0, 0, 0, 0), (1, -1, -1, 1), (0, 0, 0, 0))


def passed_along(value, axis, steps):
    count = lax.axis_size(axis)
    pairs = [(source, (source + steps) % count) for source in range(count)]
    return lax.ppermute(value, axis, pairs)


def from_partner(x, axis, stride):
    return lax.ppermute(x, axis, [(i, i ^ 1 << stride) for i in range(lax.axis_size(axis))])


def times_phase(re, im, cr, ci):
    if ci == 0:
        if cr == 1:
            return re, im
        return -re, -im
    if ci == 1:
        return -im, re
    return im, -re


def move_first(operand, stride):
    positions = jnp.arange(operand.shape[-1]) % NX
    if stride == 1:
        return jnp.where(
            positions == NX - 1, jnp.roll(operand, NX - 1, axis=-1), jnp.roll(operand, -1, axis=-1)
        )
    return jnp.where(
        positions == 0, jnp.roll(operand, 1 - NX, axis=-1), jnp.roll(operand, 1, axis=-1)
    )


def move_second(operand, stride):
    return jnp.roll(operand, -stride * NX, axis=-1)


def hop_kernel(sign_ref, psi_ref, tlo_ref, thi_ref, zlo_ref, zhi_ref, u_ref, b_ref, src_ref, *rest):
    out_ref = rest[0]
    halo_refs = rest[1:-1]
    pad_ref = rest[-1]
    S, C, RI, T, Z, L = out_ref.shape
    for s in range(S):
        for c in range(C):
            for ri in range(RI):
                pad_ref[s, c, ri, pl.ds(1, T)] = psi_ref[s, c, ri]
                pad_ref[s, c, ri, pl.ds(0, 1)] = tlo_ref[s, c, ri] * sign_ref[0]
                pad_ref[s, c, ri, pl.ds(T + 1, 1)] = thi_ref[s, c, ri] * sign_ref[1]
    xpos = lax.broadcasted_iota(jnp.int32, (Z, L), 1) % NX
    zpos = lax.broadcasted_iota(jnp.int32, (Z, L), 0)
    x_last = xpos == NX - 1
    x_first = xpos == 0
    z_last = zpos == Z - 1
    z_first = zpos == 0

    def body(t, carry):
        acc = [[[None, None] for _ in range(3)] for _ in range(4)]

        def shifted(s, c, ri, mu, stride):
            if mu == 3:
                return pad_ref[s, c, ri, t + 1 + stride]
            v = pad_ref[s, c, ri, t + 1]
            if mu == 2:
                if stride == 1:
                    halo = jnp.broadcast_to(zhi_ref[s, c, ri, t], (Z, L))
                    return jnp.where(z_last, halo, pltpu.roll(v, Z - 1, axis=0))
                halo = jnp.broadcast_to(zlo_ref[s, c, ri, t], (Z, L))
                return jnp.where(z_first, halo, pltpu.roll(v, 1, axis=0))
            if mu == 1:
                return pltpu.roll(v, (L - NX) if stride == 1 else NX, axis=1)
            if stride == 1:
                return jnp.where(x_last, pltpu.roll(v, NX - 1, axis=1), pltpu.roll(v, L - 1, axis=1))
            return jnp.where(x_first, pltpu.roll(v, L - NX + 1, axis=1), pltpu.roll(v, 1, axis=1))

        for mu in range(4):
            perm = GAMMA_PERM[mu]
            heads = [0, 1]
            for stride in (1, -1):
                orient = -1 if stride == 1 else 1
                half = []
                for s in heads:
                    p = perm[s]
                    cr, ci = orient * GAMMA_REAL[mu][s], orient * GAMMA_IMAG[mu][s]
                    colours = []
                    for c in range(3):
                        sre = shifted(s, c, 0, mu, stride)
                        sim = shifted(s, c, 1, mu, stride)
                        pre, pim = times_phase(shifted(p, c, 0, mu, stride), shifted(p, c, 1, mu, stride), cr, ci)
                        colours.append((sre + pre, sim + pim))
                    half.append(colours)
                links = u_ref if stride == 1 else b_ref
                for k, s in enumerate(heads):
                    p = perm[s]
                    cpr, cpi = orient * GAMMA_REAL[mu][p], orient * GAMMA_IMAG[mu][p]
                    for a in range(3):
                        sum_re = None
                        sum_im = None
                        for b in range(3):
                            hre, him = half[k][b]
                            if stride == 1:
                                lre = links[mu, a, b, 0, t]
                                lim = links[mu, a, b, 1, t]
                                tre = lre * hre - lim * him
                                tim = lre * him + lim * hre
                            else:
                                lre = links[mu, b, a, 0, t]
                                lim = links[mu, b, a, 1, t]
                                tre = lre * hre + lim * him
                                tim = lre * him - lim * hre
                            sum_re = tre if sum_re is None else sum_re + tre
                            sum_im = tim if sum_im is None else sum_im + tim
                        for row, (vre, vim) in ((s, (sum_re, sum_im)), (p, times_phase(sum_re, sum_im, cpr, cpi))):
                            if acc[row][a][0] is None:
                                acc[row][a] = [vre, vim]
                            else:
                                acc[row][a] = [acc[row][a][0] + vre, acc[row][a][1] + vim]
        for s in range(4):
            for c in range(3):
                for ri in range(2):
                    psi = pad_ref[s, c, ri, t + 1]
                    src = src_ref[s, c, ri, t]
                    residual = src - (psi - kappa_hop * acc[s][c][ri])
                    out_ref[s, c, ri, t] = psi + residual
        return carry

    lax.fori_loop(0, T, body, 0)
    if halo_refs:
        tfirst_ref, tlast_ref, zfirst_ref, zlast_ref = halo_refs
        for s in range(S):
            for c in range(C):
                for ri in range(RI):
                    tfirst_ref[s, c, ri] = out_ref[s, c, ri, pl.ds(0, 1)]
                    tlast_ref[s, c, ri] = out_ref[s, c, ri, pl.ds(T - 1, 1)]
                    zfirst_ref[s, c, ri] = out_ref[s, c, ri, :, pl.ds(0, 1), :]
                    zlast_ref[s, c, ri] = out_ref[s, c, ri, :, pl.ds(Z - 1, 1), :]


def hopping_step(signs, spinor, halos, links, back_links, source, emit_halos):
    R, S, C, RI, T, Z, L = source.shape
    index = lambda r: (r, 0, 0, 0, 0, 0, 0)
    site_block = pl.BlockSpec((None, S, C, RI, T, Z, L), index)
    t_block = pl.BlockSpec((None, S, C, RI, 1, Z, L), index)
    z_block = pl.BlockSpec((None, S, C, RI, T, 1, L), index)
    link_block = pl.BlockSpec(links.shape, lambda r: (0,) * 7)
    out_shape = [jax.ShapeDtypeStruct(source.shape, jnp.float32)]
    out_specs = [site_block]
    if emit_halos:
        t_shape = jax.ShapeDtypeStruct((R, S, C, RI, 1, Z, L), jnp.float32)
        z_shape = jax.ShapeDtypeStruct((R, S, C, RI, T, 1, L), jnp.float32)
        out_shape += [t_shape, t_shape, z_shape, z_shape]
        out_specs += [t_block, t_block, z_block, z_block]
    return pl.pallas_call(
        hop_kernel,
        grid=(R,),
        in_specs=[pl.BlockSpec(memory_space=pltpu.SMEM), site_block, t_block, t_block, z_block, z_block,
                  link_block, link_block, site_block],
        out_specs=out_specs,
        out_shape=out_shape,
        scratch_shapes=[pltpu.VMEM((S, C, RI, T + 2, Z, L), jnp.float32)],
        compiler_params=pltpu.CompilerParams(dimension_semantics=("arbitrary",)),
        interpret=INTERPRET,
    )(signs, spinor, *halos, links, back_links, source)


def reduce_scatter_sa(partial_value):
    n = lax.axis_size("sa")
    if n & (n - 1):
        return lax.psum_scatter(partial_value, "sa", scatter_dimension=4, tiled=True)
    lead = partial_value.shape[:-1]
    width = partial_value.shape[-1] // n
    x = jnp.moveaxis(partial_value.reshape(lead + (n, width)), -2, 0)
    me = lax.axis_index("sa")
    d = n // 2
    while d >= 1:
        upper_mine = (me // d) % 2 == 1
        keep = jnp.where(upper_mine, x[d:], x[:d])
        send = jnp.where(upper_mine, x[:d], x[d:])
        x = keep + lax.ppermute(send, "sa", [(j, j ^ d) for j in range(n)])
        d //= 2
    return x[0]


def intersection_part(rounded, vector_piece):
    products = jnp.einsum(
        "tvcazs,rqcbtzs->rqabtv", vector_piece, rounded, preferred_element_type=jnp.float32
    )
    real_part = products[:, :, 0, 0] + products[:, :, 1, 1]
    imag_part = products[:, :, 0, 1] - products[:, :, 1, 0]
    return jnp.stack([real_part, imag_part], axis=2)


def local(gauge_links, noise_slabs, offsets, vectors):
    partner_vectors = from_partner(vectors, "sec", 0)
    batch_rows = noise_slabs.shape[0]
    slab_length = gauge_links.shape[4]
    Z = gauge_links.shape[5]
    K = noise_slabs.shape[3]
    section_index = lax.axis_index("sec")
    slab_index = lax.axis_index("ta")
    slab_count = lax.axis_size("ta")
    lower_sign = jnp.where(slab_index == 0, -1.0, 1.0).astype(jnp.float32)
    upper_sign = jnp.where(slab_index == slab_count - 1, -1.0, 1.0).astype(jnp.float32)
    signs = jnp.stack([lower_sign, upper_sign])
    t_start = slab_index * slab_length
    global_time = t_start + jnp.arange(slab_length)
    own_offsets = lax.dynamic_slice_in_dim(offsets, section_index * batch_rows, batch_rows)
    rhs_index = section_index * batch_rows + jnp.arange(batch_rows)
    spin_mask = (jnp.arange(4)[None, :] == rhs_index[:, None] % 4).astype(jnp.float32)

    def make_source(noise_t, times):
        time_mask = (times[None, :] % TDIL == own_offsets[:, None]).astype(jnp.float32)
        return (
            spin_mask[:, :, None, None, None, None, None]
            * (noise_t * time_mask[:, None, None, :, None, None])[:, None]
        )

    source = make_source(jnp.repeat(noise_slabs, TDIL, axis=3), global_time)
    noise_t_lo = passed_along(noise_slabs[:, :, :, K - 1:], "ta", 1)
    noise_t_hi = passed_along(noise_slabs[:, :, :, :1], "ta", -1)
    noise_z_lo = passed_along(noise_slabs[:, :, :, :, Z - 1:], "sa", 1)
    noise_z_hi = passed_along(noise_slabs[:, :, :, :, :1], "sa", -1)
    halos = (
        make_source(noise_t_lo, t_start - 1 + jnp.arange(1)),
        make_source(noise_t_hi, t_start + slab_length + jnp.arange(1)),
        make_source(jnp.repeat(noise_z_lo, TDIL, axis=3), global_time),
        make_source(jnp.repeat(noise_z_hi, TDIL, axis=3), global_time),
    )
    time_edge = passed_along(gauge_links[3, :, :, :, -1:, :, :], "ta", 1)
    space_edge = passed_along(gauge_links[2, :, :, :, :, -1:, :], "sa", 1)
    back_links = jnp.stack(
        [
            move_first(gauge_links[0], -1),
            move_second(gauge_links[1], -1),
            jnp.concatenate([space_edge, gauge_links[2, :, :, :, :, :-1, :]], axis=4),
            jnp.concatenate([time_edge, gauge_links[3, :, :, :, :-1, :, :]], axis=3),
        ]
    )
    spinor = source
    for step in range(ITERS):
        last = step == ITERS - 1
        result = hopping_step(signs, spinor, halos, gauge_links, back_links, source, not last)
        spinor = result[0]
        if not last:
            t_first, t_last, z_first, z_last = result[1:]
            halos = (
                passed_along(t_last, "ta", 1),
                passed_along(t_first, "ta", -1),
                passed_along(z_last, "sa", 1),
                passed_along(z_first, "sa", -1),
            )
    rounded = spinor.astype(jnp.bfloat16)
    own_part = intersection_part(rounded, vectors)
    partner_part = intersection_part(rounded, partner_vectors)
    lower_half = jnp.where(section_index == 0, own_part, partner_part)
    upper_half = jnp.where(section_index == 0, partner_part, own_part)
    partial_value = jnp.concatenate([lower_half, upper_half], axis=4)
    return reduce_scatter_sa(partial_value)


def solution(mesh):
    in_specs = (
        P(None, None, None, None, "ta", "sa", None),
        P("sec", None, None, "ta", "sa", None),
        P(),
        P("ta", "sec", None, None, "sa", None),
    )
    out_specs = P("sec", None, None, "ta", "sa")
    return jax.shard_map(local, mesh=mesh, in_specs=in_specs, out_specs=out_specs, check_vma=False)
```

```python
import jax
import jax.numpy as jnp
from jax import lax
from jax.experimental import pallas as pl
from jax.experimental.pallas import tpu as pltpu
from jax.sharding import PartitionSpec as P


NX = 32
TDIL = 4
ITERS = 2
INTERPRET = False


kappa_hop = 0.12
GAMMA_PERM = ((3, 2, 1, 0), (3, 2, 1, 0), (2, 3, 0, 1), (2, 3, 0, 1))
GAMMA_REAL = ((0, 0, 0, 0), (-1, 1, 1, -1), (0, 0, 0, 0), (1, 1, 1, 1))
GAMMA_IMAG = ((1, 1, -1, -1), (0, 0, 0, 0), (1, -1, -1, 1), (0, 0, 0, 0))


def passed_along(value, axis, steps):
    count = lax.axis_size(axis)
    pairs = [(source, (source + steps) % count) for source in range(count)]
    return lax.ppermute(value, axis, pairs)


def from_partner(x, axis, stride):
    return lax.ppermute(x, axis, [(i, i ^ 1 << stride) for i in range(lax.axis_size(axis))])


def times_phase(re, im, cr, ci):
    if ci == 0:
        if cr == 1:
            return re, im
        return -re, -im
    if ci == 1:
        return -im, re
    return im, -re


def move_first(operand, stride):
    positions = jnp.arange(operand.shape[-1]) % NX
    if stride == 1:
        return jnp.where(
            positions == NX - 1, jnp.roll(operand, NX - 1, axis=-1), jnp.roll(operand, -1, axis=-1)
        )
    return jnp.where(
        positions == 0, jnp.roll(operand, 1 - NX, axis=-1), jnp.roll(operand, 1, axis=-1)
    )


def move_second(operand, stride):
    return jnp.roll(operand, -stride * NX, axis=-1)


def hop_kernel(sign_ref, psi_ref, tlo_ref, thi_ref, zlo_ref, zhi_ref, u_ref, b_ref, src_ref, *rest):
    out_ref = rest[0]
    halo_refs = rest[1:-1]
    pad_ref = rest[-1]
    S, C, RI, T, Z, L = out_ref.shape
    for s in range(S):
        for c in range(C):
            for ri in range(RI):
                pad_ref[s, c, ri, pl.ds(1, T)] = psi_ref[s, c, ri]
                pad_ref[s, c, ri, pl.ds(0, 1)] = tlo_ref[s, c, ri] * sign_ref[0]
                pad_ref[s, c, ri, pl.ds(T + 1, 1)] = thi_ref[s, c, ri] * sign_ref[1]
    xpos = lax.broadcasted_iota(jnp.int32, (Z, L), 1) % NX
    zpos = lax.broadcasted_iota(jnp.int32, (Z, L), 0)
    x_last = xpos == NX - 1
    x_first = xpos == 0
    z_last = zpos == Z - 1
    z_first = zpos == 0

    def body(t, carry):
        acc = [[[None, None] for _ in range(3)] for _ in range(4)]

        def shifted(s, c, ri, mu, stride):
            if mu == 3:
                return pad_ref[s, c, ri, t + 1 + stride]
            v = pad_ref[s, c, ri, t + 1]
            if mu == 2:
                if stride == 1:
                    halo = jnp.broadcast_to(zhi_ref[s, c, ri, t], (Z, L))
                    return jnp.where(z_last, halo, pltpu.roll(v, Z - 1, axis=0))
                halo = jnp.broadcast_to(zlo_ref[s, c, ri, t], (Z, L))
                return jnp.where(z_first, halo, pltpu.roll(v, 1, axis=0))
            if mu == 1:
                return pltpu.roll(v, (L - NX) if stride == 1 else NX, axis=1)
            if stride == 1:
                return jnp.where(x_last, pltpu.roll(v, NX - 1, axis=1), pltpu.roll(v, L - 1, axis=1))
            return jnp.where(x_first, pltpu.roll(v, L - NX + 1, axis=1), pltpu.roll(v, 1, axis=1))

        for mu in range(4):
            perm = GAMMA_PERM[mu]
            heads = [0, 1]
            for stride in (1, -1):
                orient = -1 if stride == 1 else 1
                half = []
                for s in heads:
                    p = perm[s]
                    cr, ci = orient * GAMMA_REAL[mu][s], orient * GAMMA_IMAG[mu][s]
                    colours = []
                    for c in range(3):
                        sre = shifted(s, c, 0, mu, stride)
                        sim = shifted(s, c, 1, mu, stride)
                        pre, pim = times_phase(shifted(p, c, 0, mu, stride), shifted(p, c, 1, mu, stride), cr, ci)
                        colours.append((sre + pre, sim + pim))
                    half.append(colours)
                links = u_ref if stride == 1 else b_ref
                for k, s in enumerate(heads):
                    p = perm[s]
                    cpr, cpi = orient * GAMMA_REAL[mu][p], orient * GAMMA_IMAG[mu][p]
                    for a in range(3):
                        sum_re = None
                        sum_im = None
                        for b in range(3):
                            hre, him = half[k][b]
                            if stride == 1:
                                lre = links[mu, a, b, 0, t]
                                lim = links[mu, a, b, 1, t]
                                tre = lre * hre - lim * him
                                tim = lre * him + lim * hre
                            else:
                                lre = links[mu, b, a, 0, t]
                                lim = links[mu, b, a, 1, t]
                                tre = lre * hre + lim * him
                                tim = lre * him - lim * hre
                            sum_re = tre if sum_re is None else sum_re + tre
                            sum_im = tim if sum_im is None else sum_im + tim
                        for row, (vre, vim) in ((s, (sum_re, sum_im)), (p, times_phase(sum_re, sum_im, cpr, cpi))):
                            if acc[row][a][0] is None:
                                acc[row][a] = [vre, vim]
                            else:
                                acc[row][a] = [acc[row][a][0] + vre, acc[row][a][1] + vim]
        for s in range(4):
            for c in range(3):
                for ri in range(2):
                    psi = pad_ref[s, c, ri, t + 1]
                    src = src_ref[s, c, ri, t]
                    residual = src - (psi - kappa_hop * acc[s][c][ri])
                    out_ref[s, c, ri, t] = psi + residual
        return carry

    lax.fori_loop(0, T, body, 0)
    if halo_refs:
        tfirst_ref, tlast_ref, zfirst_ref, zlast_ref = halo_refs
        for s in range(S):
            for c in range(C):
                for ri in range(RI):
                    tfirst_ref[s, c, ri] = out_ref[s, c, ri, pl.ds(0, 1)]
                    tlast_ref[s, c, ri] = out_ref[s, c, ri, pl.ds(T - 1, 1)]
                    zfirst_ref[s, c, ri] = out_ref[s, c, ri, :, pl.ds(0, 1), :]
                    zlast_ref[s, c, ri] = out_ref[s, c, ri, :, pl.ds(Z - 1, 1), :]


def hopping_step(signs, spinor, halos, links, back_links, source, emit_halos):
    R, S, C, RI, T, Z, L = source.shape
    index = lambda r: (r, 0, 0, 0, 0, 0, 0)
    site_block = pl.BlockSpec((None, S, C, RI, T, Z, L), index)
    t_block = pl.BlockSpec((None, S, C, RI, 1, Z, L), index)
    z_block = pl.BlockSpec((None, S, C, RI, T, 1, L), index)
    link_block = pl.BlockSpec(links.shape, lambda r: (0,) * 7)
    out_shape = [jax.ShapeDtypeStruct(source.shape, jnp.float32)]
    out_specs = [site_block]
    if emit_halos:
        t_shape = jax.ShapeDtypeStruct((R, S, C, RI, 1, Z, L), jnp.float32)
        z_shape = jax.ShapeDtypeStruct((R, S, C, RI, T, 1, L), jnp.float32)
        out_shape += [t_shape, t_shape, z_shape, z_shape]
        out_specs += [t_block, t_block, z_block, z_block]
    return pl.pallas_call(
        hop_kernel,
        grid=(R,),
        in_specs=[pl.BlockSpec(memory_space=pltpu.SMEM), site_block, t_block, t_block, z_block, z_block,
                  link_block, link_block, site_block],
        out_specs=out_specs,
        out_shape=out_shape,
        scratch_shapes=[pltpu.VMEM((S, C, RI, T + 2, Z, L), jnp.float32)],
        compiler_params=pltpu.CompilerParams(dimension_semantics=("arbitrary",)),
        interpret=INTERPRET,
    )(signs, spinor, *halos, links, back_links, source)


def reduce_scatter_sa(partial_value):
    n = lax.axis_size("sa")
    if n & (n - 1):
        return lax.psum_scatter(partial_value, "sa", scatter_dimension=4, tiled=True)
    lead = partial_value.shape[:-1]
    width = partial_value.shape[-1] // n
    x = jnp.moveaxis(partial_value.reshape(lead + (n, width)), -2, 0)
    me = lax.axis_index("sa")
    d = n // 2
    while d >= 1:
        upper_mine = (me // d) % 2 == 1
        keep = jnp.where(upper_mine, x[d:], x[:d])
        send = jnp.where(upper_mine, x[:d], x[d:])
        x = keep + lax.ppermute(send, "sa", [(j, j ^ d) for j in range(n)])
        d //= 2
    return x[0]


def intersection_part(rounded, vector_piece):
    products = jnp.einsum(
        "tvcazs,rqcbtzs->rqabtv", vector_piece, rounded, preferred_element_type=jnp.float32
    )
    real_part = products[:, :, 0, 0] + products[:, :, 1, 1]
    imag_part = products[:, :, 0, 1] - products[:, :, 1, 0]
    return jnp.stack([real_part, imag_part], axis=2)


def local_body(gauge_links, noise_slabs, offsets, vectors):
    partner_vectors = from_partner(vectors, "sec", 0)
    batch_rows = noise_slabs.shape[0]
    slab_length = gauge_links.shape[4]
    Z = gauge_links.shape[5]
    K = noise_slabs.shape[3]
    section_index = lax.axis_index("sec")
    slab_index = lax.axis_index("ta")
    slab_count = lax.axis_size("ta")
    lower_sign = jnp.where(slab_index == 0, -1.0, 1.0).astype(jnp.float32)
    upper_sign = jnp.where(slab_index == slab_count - 1, -1.0, 1.0).astype(jnp.float32)
    signs = jnp.stack([lower_sign, upper_sign])
    t_start = slab_index * slab_length
    global_time = t_start + jnp.arange(slab_length)
    own_offsets = lax.dynamic_slice_in_dim(offsets, section_index * batch_rows, batch_rows)
    rhs_index = section_index * batch_rows + jnp.arange(batch_rows)
    spin_mask = (jnp.arange(4)[None, :] == rhs_index[:, None] % 4).astype(jnp.float32)

    def make_source(noise_t, times):
        time_mask = (times[None, :] % TDIL == own_offsets[:, None]).astype(jnp.float32)
        return (
            spin_mask[:, :, None, None, None, None, None]
            * (noise_t * time_mask[:, None, None, :, None, None])[:, None]
        )

    source = make_source(jnp.repeat(noise_slabs, TDIL, axis=3), global_time)
    noise_t_lo = passed_along(noise_slabs[:, :, :, K - 1:], "ta", 1)
    noise_t_hi = passed_along(noise_slabs[:, :, :, :1], "ta", -1)
    noise_z_lo = passed_along(noise_slabs[:, :, :, :, Z - 1:], "sa", 1)
    noise_z_hi = passed_along(noise_slabs[:, :, :, :, :1], "sa", -1)
    halos = (
        make_source(noise_t_lo, t_start - 1 + jnp.arange(1)),
        make_source(noise_t_hi, t_start + slab_length + jnp.arange(1)),
        make_source(jnp.repeat(noise_z_lo, TDIL, axis=3), global_time),
        make_source(jnp.repeat(noise_z_hi, TDIL, axis=3), global_time),
    )
    time_edge = passed_along(gauge_links[3, :, :, :, -1:, :, :], "ta", 1)
    space_edge = passed_along(gauge_links[2, :, :, :, :, -1:, :], "sa", 1)
    back_links = jnp.stack(
        [
            move_first(gauge_links[0], -1),
            move_second(gauge_links[1], -1),
            jnp.concatenate([space_edge, gauge_links[2, :, :, :, :, :-1, :]], axis=4),
            jnp.concatenate([time_edge, gauge_links[3, :, :, :, :-1, :, :]], axis=3),
        ]
    )
    spinor = source
    for step in range(ITERS):
        last = step == ITERS - 1
        result = hopping_step(signs, spinor, halos, gauge_links, back_links, source, not last)
        spinor = result[0]
        if not last:
            t_first, t_last, z_first, z_last = result[1:]
            halos = tuple(
                passed_along(plane.astype(jnp.bfloat16), axis, steps).astype(jnp.float32)
                for plane, axis, steps in (
                    (t_last, "ta", 1),
                    (t_first, "ta", -1),
                    (z_last, "sa", 1),
                    (z_first, "sa", -1),
                )
            )
    rounded = spinor.astype(jnp.bfloat16)
    own_part = intersection_part(rounded, vectors)
    partner_part = intersection_part(rounded, partner_vectors)
    lower_half = jnp.where(section_index == 0, own_part, partner_part)
    upper_half = jnp.where(section_index == 0, partner_part, own_part)
    partial_value = jnp.concatenate([lower_half, upper_half], axis=4)
    return reduce_scatter_sa(partial_value)


def solution(mesh):
    in_specs = (
        P(None, None, None, None, "ta", "sa", None),
        P("sec", None, None, "ta", "sa", None),
        P(),
        P("ta", "sec", None, None, "sa", None),
    )
    out_specs = P("sec", None, None, "ta", "sa")
    return jax.shard_map(local_body, mesh=mesh, in_specs=in_specs, out_specs=out_specs, check_vma=False)
```

```python
import functools

import jax
import jax.numpy as jnp
from jax import lax
from jax.experimental import pallas as pl
from jax.experimental.pallas import tpu as pltpu
from jax.sharding import PartitionSpec as P


NX = 32
TDIL = 4
INTERPRET = False


kappa_hop = 0.12
GAMMA_PERM = ((3, 2, 1, 0), (3, 2, 1, 0), (2, 3, 0, 1), (2, 3, 0, 1))
GAMMA_REAL = ((0, 0, 0, 0), (-1, 1, 1, -1), (0, 0, 0, 0), (1, 1, 1, 1))
GAMMA_IMAG = ((1, 1, -1, -1), (0, 0, 0, 0), (1, -1, -1, 1), (0, 0, 0, 0))


def passed_along(value, axis, steps):
    count = lax.axis_size(axis)
    pairs = [(source, (source + steps) % count) for source in range(count)]
    return lax.ppermute(value, axis, pairs)


def from_partner(x, axis, stride):
    return lax.ppermute(x, axis, [(i, i ^ 1 << stride) for i in range(lax.axis_size(axis))])


def times_phase(re, im, cr, ci):
    if ci == 0:
        if cr == 1:
            return re, im
        return -re, -im
    if ci == 1:
        return -im, re
    return im, -re


def hop_kernel(first, *refs):
    (smask_ref, tmask_ref, sign_ref, noise_ref, ntlo_ref, nthi_ref, nzlo_ref, nzhi_ref,
     u_ref, utedge_ref, uzedge_ref) = refs[:11]
    rest = refs[11:]
    if first:
        out_ref, tfirst_ref, tlast_ref, zfirst_ref, zlast_ref = rest[:5]
        pad_ref, src_ref, zlo_s, zhi_s, ut_s = rest[5:]
        zlo_src, zhi_src = zlo_s, zhi_s
    else:
        psi_ref, tlo_ref, thi_ref, zlo_src, zhi_src = rest[:5]
        out_ref = rest[5]
        pad_ref, src_ref, ut_s = rest[6:]
    S, C, RI, T, Z, L = src_ref.shape
    K = noise_ref.shape[2]
    span = T // K
    r = pl.program_id(0)

    @pl.when(r == 0)
    def _():
        for a in range(3):
            for b in range(3):
                for ri in range(RI):
                    ut_s[a, b, ri, pl.ds(0, 1)] = utedge_ref[a, b, ri]
                    ut_s[a, b, ri, pl.ds(1, T)] = u_ref[3, a, b, ri]

    for s in range(S):
        fs = smask_ref[r * S + s]
        for c in range(C):
            for ri in range(RI):
                for t in range(T):
                    src_ref[s, c, ri, t] = noise_ref[c, ri, t // span] * (fs * tmask_ref[r * (T + 2) + t + 1])
                if first:
                    pad_ref[s, c, ri, pl.ds(1, T)] = src_ref[s, c, ri]
                    pad_ref[s, c, ri, 0] = ntlo_ref[c, ri, 0] * (fs * tmask_ref[r * (T + 2)] * sign_ref[0])
                    pad_ref[s, c, ri, T + 1] = nthi_ref[c, ri, 0] * (
                        fs * tmask_ref[r * (T + 2) + T + 1] * sign_ref[1])
                    for t in range(T):
                        f = fs * tmask_ref[r * (T + 2) + t + 1]
                        zlo_s[s, c, ri, t] = nzlo_ref[c, ri, t // span] * f
                        zhi_s[s, c, ri, t] = nzhi_ref[c, ri, t // span] * f
                else:
                    pad_ref[s, c, ri, pl.ds(1, T)] = psi_ref[s, c, ri]
                    pad_ref[s, c, ri, pl.ds(0, 1)] = tlo_ref[s, c, ri].astype(jnp.float32) * sign_ref[0]
                    pad_ref[s, c, ri, pl.ds(T + 1, 1)] = thi_ref[s, c, ri].astype(jnp.float32) * sign_ref[1]
    xpos = lax.broadcasted_iota(jnp.int32, (Z, L), 1) % NX
    zpos = lax.broadcasted_iota(jnp.int32, (Z, L), 0)
    x_last = xpos == NX - 1
    x_first = xpos == 0
    z_last = zpos == Z - 1
    z_first = zpos == 0

    def x_back(v):
        return jnp.where(x_first, pltpu.roll(v, L - NX + 1, axis=1), pltpu.roll(v, 1, axis=1))

    def body(t, carry):
        acc = [[[None, None] for _ in range(3)] for _ in range(4)]

        def shifted(s, c, ri, mu, stride):
            if mu == 3:
                return pad_ref[s, c, ri, t + 1 + stride]
            v = pad_ref[s, c, ri, t + 1]
            if mu == 2:
                if stride == 1:
                    halo = jnp.broadcast_to(zhi_src[s, c, ri, t], (Z, L))
                    return jnp.where(z_last, halo, pltpu.roll(v, Z - 1, axis=0))
                halo = jnp.broadcast_to(zlo_src[s, c, ri, t], (Z, L))
                return jnp.where(z_first, halo, pltpu.roll(v, 1, axis=0))
            if mu == 1:
                return pltpu.roll(v, (L - NX) if stride == 1 else NX, axis=1)
            if stride == 1:
                return jnp.where(x_last, pltpu.roll(v, NX - 1, axis=1), pltpu.roll(v, L - 1, axis=1))
            return x_back(v)

        def back_link(mu, a, b, ri):
            if mu == 3:
                return ut_s[a, b, ri, t]
            v = u_ref[mu, a, b, ri, t]
            if mu == 2:
                edge = jnp.broadcast_to(uzedge_ref[a, b, ri, t], (Z, L))
                return jnp.where(z_first, edge, pltpu.roll(v, 1, axis=0))
            if mu == 1:
                return pltpu.roll(v, NX, axis=1)
            return x_back(v)

        for mu in range(4):
            perm = GAMMA_PERM[mu]
            heads = [0, 1]
            for stride in (1, -1):
                orient = -1 if stride == 1 else 1
                half = []
                for s in heads:
                    p = perm[s]
                    cr, ci = orient * GAMMA_REAL[mu][s], orient * GAMMA_IMAG[mu][s]
                    colours = []
                    for c in range(3):
                        sre = shifted(s, c, 0, mu, stride)
                        sim = shifted(s, c, 1, mu, stride)
                        pre, pim = times_phase(shifted(p, c, 0, mu, stride), shifted(p, c, 1, mu, stride), cr, ci)
                        colours.append((sre + pre, sim + pim))
                    half.append(colours)
                if stride == 1:
                    links = [[(u_ref[mu, a, b, 0, t], u_ref[mu, a, b, 1, t]) for b in range(3)] for a in range(3)]
                else:
                    links = [[(back_link(mu, b, a, 0), back_link(mu, b, a, 1)) for b in range(3)] for a in range(3)]
                for k, s in enumerate(heads):
                    p = perm[s]
                    cpr, cpi = orient * GAMMA_REAL[mu][p], orient * GAMMA_IMAG[mu][p]
                    for a in range(3):
                        sum_re = None
                        sum_im = None
                        for b in range(3):
                            hre, him = half[k][b]
                            lre, lim = links[a][b]
                            if stride == 1:
                                tre = lre * hre - lim * him
                                tim = lre * him + lim * hre
                            else:
                                tre = lre * hre + lim * him
                                tim = lre * him - lim * hre
                            sum_re = tre if sum_re is None else sum_re + tre
                            sum_im = tim if sum_im is None else sum_im + tim
                        for row, (vre, vim) in ((s, (sum_re, sum_im)), (p, times_phase(sum_re, sum_im, cpr, cpi))):
                            if acc[row][a][0] is None:
                                acc[row][a] = [vre, vim]
                            else:
                                acc[row][a] = [acc[row][a][0] + vre, acc[row][a][1] + vim]
        for s in range(4):
            for c in range(3):
                for ri in range(2):
                    psi = pad_ref[s, c, ri, t + 1]
                    src = src_ref[s, c, ri, t]
                    residual = src - (psi - kappa_hop * acc[s][c][ri])
                    out_ref[s, c, ri, t] = (psi + residual).astype(out_ref.dtype)
        return carry

    lax.fori_loop(0, T, body, 0)
    if first:
        for s in range(S):
            for c in range(C):
                for ri in range(RI):
                    tfirst_ref[s, c, ri] = out_ref[s, c, ri, pl.ds(0, 1)].astype(tfirst_ref.dtype)
                    tlast_ref[s, c, ri] = out_ref[s, c, ri, pl.ds(T - 1, 1)].astype(tlast_ref.dtype)
                    zfirst_ref[s, c, ri] = out_ref[s, c, ri, :, pl.ds(0, 1), :]
                    zlast_ref[s, c, ri] = out_ref[s, c, ri, :, pl.ds(Z - 1, 1), :]


def hopping_step(first, scalars, noise_parts, link_parts, spinor_parts):
    R, C, RI, K, Z, L = noise_parts[0].shape
    T = link_parts[0].shape[4]
    S = 4
    index = lambda r: (r,) + (0,) * 6
    index6 = lambda r: (r,) + (0,) * 5
    whole = lambda x: pl.BlockSpec(x.shape, lambda r: (0,) * x.ndim)
    smem = pl.BlockSpec(memory_space=pltpu.SMEM)
    site_block = pl.BlockSpec((None, S, C, RI, T, Z, L), index)
    t_block = pl.BlockSpec((None, S, C, RI, 1, Z, L), index)
    z_block = pl.BlockSpec((None, S, C, RI, T, 1, L), index)
    noise_specs = [
        pl.BlockSpec((None, C, RI, K, Z, L), index6),
        pl.BlockSpec((None, C, RI, 1, Z, L), index6),
        pl.BlockSpec((None, C, RI, 1, Z, L), index6),
        pl.BlockSpec((None, C, RI, K, 1, L), index6),
        pl.BlockSpec((None, C, RI, K, 1, L), index6),
    ]
    in_specs = [smem, smem, smem] + noise_specs + [whole(x) for x in link_parts]
    scratch = [pltpu.VMEM((S, C, RI, T + 2, Z, L), jnp.float32), pltpu.VMEM((S, C, RI, T, Z, L), jnp.float32)]
    if first:
        t_shape = jax.ShapeDtypeStruct((R, S, C, RI, 1, Z, L), jnp.bfloat16)
        z_shape = jax.ShapeDtypeStruct((R, S, C, RI, T, 1, L), jnp.float32)
        out_shape = [jax.ShapeDtypeStruct((R, S, C, RI, T, Z, L), jnp.float32), t_shape, t_shape, z_shape, z_shape]
        out_specs = [site_block, t_block, t_block, z_block, z_block]
        scratch += [pltpu.VMEM((S, C, RI, T, 1, L), jnp.float32)] * 2
    else:
        in_specs += [site_block, t_block, t_block, z_block, z_block]
        out_shape = jax.ShapeDtypeStruct((R, S, C, RI, T, Z, L), jnp.bfloat16)
        out_specs = site_block
    scratch += [pltpu.VMEM((3, 3, RI, T + 1, Z, L), jnp.float32)]
    return pl.pallas_call(
        functools.partial(hop_kernel, first),
        grid=(R,),
        in_specs=in_specs,
        out_specs=out_specs,
        out_shape=out_shape,
        scratch_shapes=scratch,
        compiler_params=pltpu.CompilerParams(dimension_semantics=("arbitrary",)),
        interpret=INTERPRET,
    )(*scalars, *noise_parts, *link_parts, *spinor_parts)


def reduce_scatter_sa(partial_value):
    n = lax.axis_size("sa")
    if n & (n - 1):
        return lax.psum_scatter(partial_value, "sa", scatter_dimension=4, tiled=True)
    lead = partial_value.shape[:-1]
    width = partial_value.shape[-1] // n
    x = jnp.moveaxis(partial_value.reshape(lead + (n, width)), -2, 0)
    me = lax.axis_index("sa")
    d = n // 2
    while d >= 1:
        upper_mine = (me // d) % 2 == 1
        keep = jnp.where(upper_mine, x[d:], x[:d])
        send = jnp.where(upper_mine, x[:d], x[d:])
        x = keep + lax.ppermute(send, "sa", [(j, j ^ d) for j in range(n)])
        d //= 2
    return x[0]


def intersection_part(rounded, vector_piece):
    products = jnp.einsum(
        "tvcazs,rqcbtzs->rqabtv", vector_piece, rounded, preferred_element_type=jnp.float32
    )
    real_part = products[:, :, 0, 0] + products[:, :, 1, 1]
    imag_part = products[:, :, 0, 1] - products[:, :, 1, 0]
    return jnp.stack([real_part, imag_part], axis=2)


def local_body(gauge_links, noise_slabs, offsets, vectors):
    partner_vectors = from_partner(vectors, "sec", 0)
    batch_rows = noise_slabs.shape[0]
    slab_length = gauge_links.shape[4]
    Z = gauge_links.shape[5]
    K = noise_slabs.shape[3]
    section_index = lax.axis_index("sec")
    slab_index = lax.axis_index("ta")
    slab_count = lax.axis_size("ta")
    lower_sign = jnp.where(slab_index == 0, -1.0, 1.0).astype(jnp.float32)
    upper_sign = jnp.where(slab_index == slab_count - 1, -1.0, 1.0).astype(jnp.float32)
    signs = jnp.stack([lower_sign, upper_sign])
    t_start = slab_index * slab_length
    own_offsets = lax.dynamic_slice_in_dim(offsets, section_index * batch_rows, batch_rows)
    rhs_index = section_index * batch_rows + jnp.arange(batch_rows)
    spin_mask = (jnp.arange(4)[None, :] == rhs_index[:, None] % 4).astype(jnp.float32)
    times = t_start - 1 + jnp.arange(slab_length + 2)
    time_mask = (times[None, :] % TDIL == own_offsets[:, None]).astype(jnp.float32)
    scalars = (spin_mask.reshape(-1), time_mask.reshape(-1), signs)
    noise_parts = (
        noise_slabs,
        passed_along(noise_slabs[:, :, :, K - 1:], "ta", 1),
        passed_along(noise_slabs[:, :, :, :1], "ta", -1),
        passed_along(noise_slabs[:, :, :, :, Z - 1:], "sa", 1),
        passed_along(noise_slabs[:, :, :, :, :1], "sa", -1),
    )
    link_parts = (
        gauge_links,
        passed_along(gauge_links[3, :, :, :, -1:, :, :], "ta", 1),
        passed_along(gauge_links[2, :, :, :, :, -1:, :], "sa", 1),
    )
    spinor, t_first, t_last, z_first, z_last = hopping_step(True, scalars, noise_parts, link_parts, ())
    halos = (
        passed_along(t_last, "ta", 1),
        passed_along(t_first, "ta", -1),
        passed_along(z_last, "sa", 1),
        passed_along(z_first, "sa", -1),
    )
    rounded = hopping_step(False, scalars, noise_parts, link_parts, (spinor,) + halos)
    own_part = intersection_part(rounded, vectors)
    partner_part = intersection_part(rounded, partner_vectors)
    lower_half = jnp.where(section_index == 0, own_part, partner_part)
    upper_half = jnp.where(section_index == 0, partner_part, own_part)
    partial_value = jnp.concatenate([lower_half, upper_half], axis=4)
    return reduce_scatter_sa(partial_value)


def solution(mesh):
    in_specs = (
        P(None, None, None, None, "ta", "sa", None),
        P("sec", None, None, "ta", "sa", None),
        P(),
        P("ta", "sec", None, None, "sa", None),
    )
    out_specs = P("sec", None, None, "ta", "sa")
    return jax.shard_map(local_body, mesh=mesh, in_specs=in_specs, out_specs=out_specs, check_vma=False)
```

```python
import functools

import jax
import jax.numpy as jnp
from jax import lax
from jax.experimental import pallas as pl
from jax.experimental.pallas import tpu as pltpu
from jax.sharding import PartitionSpec as P


NX = 32
TDIL = 4
INTERPRET = False


kappa_hop = 0.12
GAMMA_PERM = ((3, 2, 1, 0), (3, 2, 1, 0), (2, 3, 0, 1), (2, 3, 0, 1))
GAMMA_REAL = ((0, 0, 0, 0), (-1, 1, 1, -1), (0, 0, 0, 0), (1, 1, 1, 1))
GAMMA_IMAG = ((1, 1, -1, -1), (0, 0, 0, 0), (1, -1, -1, 1), (0, 0, 0, 0))


def passed_along(value, axis, steps):
    count = lax.axis_size(axis)
    pairs = [(source, (source + steps) % count) for source in range(count)]
    return lax.ppermute(value, axis, pairs)


def from_partner(x, axis, stride):
    return lax.ppermute(x, axis, [(i, i ^ 1 << stride) for i in range(lax.axis_size(axis))])


def times_phase(re, im, cr, ci):
    if ci == 0:
        if cr == 1:
            return re, im
        return -re, -im
    if ci == 1:
        return -im, re
    return im, -re


def hop_kernel(first, *refs):
    (smask_ref, tmask_ref, sign_ref, noise_ref, ntlo_ref, nthi_ref, nzlo_ref, nzhi_ref,
     u_ref, utedge_ref, uzedge_ref) = refs[:11]
    rest = refs[11:]
    if first:
        out_ref, tfirst_ref, tlast_ref, zfirst_ref, zlast_ref = rest[:5]
        scratch = rest[5:]
    else:
        psi_ref, tlo_ref, thi_ref, zlo_ref, zhi_ref = rest[:5]
        out_ref = rest[5]
        scratch = rest[6:]
    pad_ref, src_ref, zlo_s, zhi_s, u8, ut8, uz8 = scratch
    S, C, RI, T, ROWS, L = src_ref.shape
    Z = ROWS // 2
    K = noise_ref.shape[3]
    span = T // K
    h = pl.program_id(0)
    lower = pl.ds(0, Z)
    upper = pl.ds(Z, Z)

    @pl.when(h == 0)
    def _():
        for a in range(3):
            for b in range(3):
                for ri in range(RI):
                    for half in (lower, upper):
                        ut8[a, b, ri, pl.ds(0, 1), half] = utedge_ref[a, b, ri]
                        ut8[a, b, ri, pl.ds(1, T), half] = u_ref[3, a, b, ri]
                        for t in range(T):
                            uz8[a, b, ri, t, half] = jnp.broadcast_to(uzedge_ref[a, b, ri, t], (Z, L))
                        for mu in range(4):
                            u8[mu, a, b, ri, :, half] = u_ref[mu, a, b, ri]

    for s in range(S):
        for c in range(C):
            for ri in range(RI):
                for g, half in ((0, lower), (1, upper)):
                    r = 2 * h + g
                    fs = smask_ref[r * S + s]
                    for t in range(T):
                        src_ref[s, c, ri, t, half] = noise_ref[g, c, ri, t // span] * (
                            fs * tmask_ref[r * (T + 2) + t + 1])
                    if first:
                        pad_ref[s, c, ri, 0, half] = ntlo_ref[g, c, ri, 0] * (
                            fs * tmask_ref[r * (T + 2)] * sign_ref[0])
                        pad_ref[s, c, ri, T + 1, half] = nthi_ref[g, c, ri, 0] * (
                            fs * tmask_ref[r * (T + 2) + T + 1] * sign_ref[1])
                        for t in range(T):
                            f = fs * tmask_ref[r * (T + 2) + t + 1]
                            zlo_s[s, c, ri, t, half] = jnp.broadcast_to(nzlo_ref[g, c, ri, t // span] * f, (Z, L))
                            zhi_s[s, c, ri, t, half] = jnp.broadcast_to(nzhi_ref[g, c, ri, t // span] * f, (Z, L))
                    else:
                        for t in range(T):
                            zlo_s[s, c, ri, t, half] = jnp.broadcast_to(zlo_ref[s, c, ri, t, pl.ds(g, 1)], (Z, L))
                            zhi_s[s, c, ri, t, half] = jnp.broadcast_to(zhi_ref[s, c, ri, t, pl.ds(g, 1)], (Z, L))
                if first:
                    pad_ref[s, c, ri, pl.ds(1, T)] = src_ref[s, c, ri]
                else:
                    pad_ref[s, c, ri, pl.ds(1, T)] = psi_ref[s, c, ri]
                    pad_ref[s, c, ri, pl.ds(0, 1)] = tlo_ref[s, c, ri].astype(jnp.float32) * sign_ref[0]
                    pad_ref[s, c, ri, pl.ds(T + 1, 1)] = thi_ref[s, c, ri].astype(jnp.float32) * sign_ref[1]
    xpos = lax.broadcasted_iota(jnp.int32, (ROWS, L), 1) % NX
    zpos = lax.broadcasted_iota(jnp.int32, (ROWS, L), 0) % Z
    x_last = xpos == NX - 1
    x_first = xpos == 0
    z_last = zpos == Z - 1
    z_first = zpos == 0

    def x_back(v):
        return jnp.where(x_first, pltpu.roll(v, L - NX + 1, axis=1), pltpu.roll(v, 1, axis=1))

    def body(t, carry):
        acc = [[[None, None] for _ in range(3)] for _ in range(4)]

        def shifted(s, c, ri, mu, stride):
            if mu == 3:
                return pad_ref[s, c, ri, t + 1 + stride]
            v = pad_ref[s, c, ri, t + 1]
            if mu == 2:
                if stride == 1:
                    return jnp.where(z_last, zhi_s[s, c, ri, t], pltpu.roll(v, ROWS - 1, axis=0))
                return jnp.where(z_first, zlo_s[s, c, ri, t], pltpu.roll(v, 1, axis=0))
            if mu == 1:
                return pltpu.roll(v, (L - NX) if stride == 1 else NX, axis=1)
            if stride == 1:
                return jnp.where(x_last, pltpu.roll(v, NX - 1, axis=1), pltpu.roll(v, L - 1, axis=1))
            return x_back(v)

        def back_link(mu, a, b, ri):
            if mu == 3:
                return ut8[a, b, ri, t]
            v = u8[mu, a, b, ri, t]
            if mu == 2:
                return jnp.where(z_first, uz8[a, b, ri, t], pltpu.roll(v, 1, axis=0))
            if mu == 1:
                return pltpu.roll(v, NX, axis=1)
            return x_back(v)

        for mu in range(4):
            perm = GAMMA_PERM[mu]
            heads = [0, 1]
            for stride in (1, -1):
                orient = -1 if stride == 1 else 1
                half = []
                for s in heads:
                    p = perm[s]
                    cr, ci = orient * GAMMA_REAL[mu][s], orient * GAMMA_IMAG[mu][s]
                    colours = []
                    for c in range(3):
                        sre = shifted(s, c, 0, mu, stride)
                        sim = shifted(s, c, 1, mu, stride)
                        pre, pim = times_phase(shifted(p, c, 0, mu, stride), shifted(p, c, 1, mu, stride), cr, ci)
                        colours.append((sre + pre, sim + pim))
                    half.append(colours)
                if stride == 1:
                    links = [[(u8[mu, a, b, 0, t], u8[mu, a, b, 1, t]) for b in range(3)] for a in range(3)]
                else:
                    links = [[(back_link(mu, b, a, 0), back_link(mu, b, a, 1)) for b in range(3)] for a in range(3)]
                for k, s in enumerate(heads):
                    p = perm[s]
                    cpr, cpi = orient * GAMMA_REAL[mu][p], orient * GAMMA_IMAG[mu][p]
                    for a in range(3):
                        sum_re = None
                        sum_im = None
                        for b in range(3):
                            hre, him = half[k][b]
                            lre, lim = links[a][b]
                            if stride == 1:
                                tre = lre * hre - lim * him
                                tim = lre * him + lim * hre
                            else:
                                tre = lre * hre + lim * him
                                tim = lre * him - lim * hre
                            sum_re = tre if sum_re is None else sum_re + tre
                            sum_im = tim if sum_im is None else sum_im + tim
                        for row, (vre, vim) in ((s, (sum_re, sum_im)), (p, times_phase(sum_re, sum_im, cpr, cpi))):
                            if acc[row][a][0] is None:
                                acc[row][a] = [vre, vim]
                            else:
                                acc[row][a] = [acc[row][a][0] + vre, acc[row][a][1] + vim]
        for s in range(4):
            for c in range(3):
                for ri in range(2):
                    psi = pad_ref[s, c, ri, t + 1]
                    src = src_ref[s, c, ri, t]
                    residual = src - (psi - kappa_hop * acc[s][c][ri])
                    out_ref[s, c, ri, t] = (psi + residual).astype(out_ref.dtype)
        return carry

    lax.fori_loop(0, T, body, 0)
    if first:
        for s in range(S):
            for c in range(C):
                for ri in range(RI):
                    tfirst_ref[s, c, ri] = out_ref[s, c, ri, pl.ds(0, 1)].astype(tfirst_ref.dtype)
                    tlast_ref[s, c, ri] = out_ref[s, c, ri, pl.ds(T - 1, 1)].astype(tlast_ref.dtype)
                    for g in range(2):
                        zfirst_ref[s, c, ri, :, pl.ds(g, 1), :] = out_ref[s, c, ri, :, pl.ds(g * Z, 1), :]
                        zlast_ref[s, c, ri, :, pl.ds(g, 1), :] = out_ref[s, c, ri, :, pl.ds(g * Z + Z - 1, 1), :]


def hopping_step(first, scalars, noise_parts, link_parts, spinor_parts):
    R, C, RI, K, Z, L = noise_parts[0].shape
    T = link_parts[0].shape[4]
    S = 4
    H = R // 2
    ROWS = 2 * Z
    index = lambda h: (h,) + (0,) * 6
    index6 = lambda h: (h,) + (0,) * 5
    whole = lambda x: pl.BlockSpec(x.shape, lambda h: (0,) * x.ndim)
    smem = pl.BlockSpec(memory_space=pltpu.SMEM)
    site_block = pl.BlockSpec((None, S, C, RI, T, ROWS, L), index)
    t_block = pl.BlockSpec((None, S, C, RI, 1, ROWS, L), index)
    z_block = pl.BlockSpec((None, S, C, RI, T, 2, L), index)
    noise_specs = [
        pl.BlockSpec((2, C, RI, K, Z, L), index6),
        pl.BlockSpec((2, C, RI, 1, Z, L), index6),
        pl.BlockSpec((2, C, RI, 1, Z, L), index6),
        pl.BlockSpec((2, C, RI, K, 1, L), index6),
        pl.BlockSpec((2, C, RI, K, 1, L), index6),
    ]
    in_specs = [smem, smem, smem] + noise_specs + [whole(x) for x in link_parts]
    site_shape = (H, S, C, RI, T, ROWS, L)
    if first:
        t_shape = jax.ShapeDtypeStruct((H, S, C, RI, 1, ROWS, L), jnp.bfloat16)
        z_shape = jax.ShapeDtypeStruct((H, S, C, RI, T, 2, L), jnp.float32)
        out_shape = [jax.ShapeDtypeStruct(site_shape, jnp.float32), t_shape, t_shape, z_shape, z_shape]
        out_specs = [site_block, t_block, t_block, z_block, z_block]
    else:
        in_specs += [site_block, t_block, t_block, z_block, z_block]
        out_shape = jax.ShapeDtypeStruct(site_shape, jnp.bfloat16)
        out_specs = site_block
    scratch = [
        pltpu.VMEM((S, C, RI, T + 2, ROWS, L), jnp.float32),
        pltpu.VMEM((S, C, RI, T, ROWS, L), jnp.float32),
        pltpu.VMEM((S, C, RI, T, ROWS, L), jnp.float32),
        pltpu.VMEM((S, C, RI, T, ROWS, L), jnp.float32),
        pltpu.VMEM((4, 3, 3, RI, T, ROWS, L), jnp.float32),
        pltpu.VMEM((3, 3, RI, T + 1, ROWS, L), jnp.float32),
        pltpu.VMEM((3, 3, RI, T, ROWS, L), jnp.float32),
    ]
    return pl.pallas_call(
        functools.partial(hop_kernel, first),
        grid=(H,),
        in_specs=in_specs,
        out_specs=out_specs,
        out_shape=out_shape,
        scratch_shapes=scratch,
        compiler_params=pltpu.CompilerParams(dimension_semantics=("arbitrary",)),
        interpret=INTERPRET,
    )(*scalars, *noise_parts, *link_parts, *spinor_parts)


def reduce_scatter_sa(partial_value):
    n = lax.axis_size("sa")
    if n & (n - 1):
        return lax.psum_scatter(partial_value, "sa", scatter_dimension=4, tiled=True)
    lead = partial_value.shape[:-1]
    width = partial_value.shape[-1] // n
    x = jnp.moveaxis(partial_value.reshape(lead + (n, width)), -2, 0)
    me = lax.axis_index("sa")
    d = n // 2
    while d >= 1:
        upper_mine = (me // d) % 2 == 1
        keep = jnp.where(upper_mine, x[d:], x[:d])
        send = jnp.where(upper_mine, x[:d], x[d:])
        x = keep + lax.ppermute(send, "sa", [(j, j ^ d) for j in range(n)])
        d //= 2
    return x[0]


def intersection_part(rounded, vector_piece):
    products = jnp.einsum(
        "tvcazs,rqcbtzs->rqabtv", vector_piece, rounded, preferred_element_type=jnp.float32
    )
    real_part = products[:, :, 0, 0] + products[:, :, 1, 1]
    imag_part = products[:, :, 0, 1] - products[:, :, 1, 0]
    return jnp.stack([real_part, imag_part], axis=2)


def local_body(gauge_links, noise_slabs, offsets, vectors):
    partner_vectors = from_partner(vectors, "sec", 0)
    batch_rows = noise_slabs.shape[0]
    slab_length = gauge_links.shape[4]
    Z = gauge_links.shape[5]
    K = noise_slabs.shape[3]
    section_index = lax.axis_index("sec")
    slab_index = lax.axis_index("ta")
    slab_count = lax.axis_size("ta")
    lower_sign = jnp.where(slab_index == 0, -1.0, 1.0).astype(jnp.float32)
    upper_sign = jnp.where(slab_index == slab_count - 1, -1.0, 1.0).astype(jnp.float32)
    signs = jnp.stack([lower_sign, upper_sign])
    t_start = slab_index * slab_length
    own_offsets = lax.dynamic_slice_in_dim(offsets, section_index * batch_rows, batch_rows)
    rhs_index = section_index * batch_rows + jnp.arange(batch_rows)
    spin_mask = (jnp.arange(4)[None, :] == rhs_index[:, None] % 4).astype(jnp.float32)
    times = t_start - 1 + jnp.arange(slab_length + 2)
    time_mask = (times[None, :] % TDIL == own_offsets[:, None]).astype(jnp.float32)
    scalars = (spin_mask.reshape(-1), time_mask.reshape(-1), signs)
    noise_parts = (
        noise_slabs,
        passed_along(noise_slabs[:, :, :, K - 1:], "ta", 1),
        passed_along(noise_slabs[:, :, :, :1], "ta", -1),
        passed_along(noise_slabs[:, :, :, :, Z - 1:], "sa", 1),
        passed_along(noise_slabs[:, :, :, :, :1], "sa", -1),
    )
    link_parts = (
        gauge_links,
        passed_along(gauge_links[3, :, :, :, -1:, :, :], "ta", 1),
        passed_along(gauge_links[2, :, :, :, :, -1:, :], "sa", 1),
    )
    spinor, t_first, t_last, z_first, z_last = hopping_step(True, scalars, noise_parts, link_parts, ())
    halos = (
        passed_along(t_last, "ta", 1),
        passed_along(t_first, "ta", -1),
        passed_along(z_last, "sa", 1),
        passed_along(z_first, "sa", -1),
    )
    rounded = hopping_step(False, scalars, noise_parts, link_parts, (spinor,) + halos)
    H, S, C, RI, T, ROWS, L = rounded.shape
    rounded = jnp.moveaxis(rounded.reshape(H, S, C, RI, T, 2, ROWS // 2, L), 5, 1).reshape(
        2 * H, S, C, RI, T, ROWS // 2, L)
    own_part = intersection_part(rounded, vectors)
    partner_part = intersection_part(rounded, partner_vectors)
    lower_half = jnp.where(section_index == 0, own_part, partner_part)
    upper_half = jnp.where(section_index == 0, partner_part, own_part)
    partial_value = jnp.concatenate([lower_half, upper_half], axis=4)
    return reduce_scatter_sa(partial_value)


def solution(mesh):
    in_specs = (
        P(None, None, None, None, "ta", "sa", None),
        P("sec", None, None, "ta", "sa", None),
        P(),
        P("ta", "sec", None, None, "sa", None),
    )
    out_specs = P("sec", None, None, "ta", "sa")
    return jax.shard_map(local_body, mesh=mesh, in_specs=in_specs, out_specs=out_specs, check_vma=False)
```

```python
import functools

import jax
import jax.numpy as jnp
from jax import lax
from jax.experimental import pallas as pl
from jax.experimental.pallas import tpu as pltpu
from jax.sharding import PartitionSpec as P


NX = 32
TDIL = 4
INTERPRET = False


kappa_hop = 0.12
GAMMA_PERM = ((3, 2, 1, 0), (3, 2, 1, 0), (2, 3, 0, 1), (2, 3, 0, 1))
GAMMA_REAL = ((0, 0, 0, 0), (-1, 1, 1, -1), (0, 0, 0, 0), (1, 1, 1, 1))
GAMMA_IMAG = ((1, 1, -1, -1), (0, 0, 0, 0), (1, -1, -1, 1), (0, 0, 0, 0))


def passed_along(value, axis, steps):
    count = lax.axis_size(axis)
    pairs = [(source, (source + steps) % count) for source in range(count)]
    return lax.ppermute(value, axis, pairs)


def from_partner(x, axis, stride):
    return lax.ppermute(x, axis, [(i, i ^ 1 << stride) for i in range(lax.axis_size(axis))])


def times_phase(re, im, cr, ci):
    if ci == 0:
        if cr == 1:
            return re, im
        return -re, -im
    if ci == 1:
        return -im, re
    return im, -re


def hop_kernel(first, *refs):
    (smask_ref, tmask_ref, sign_ref, noise_ref, ntlo_ref, nthi_ref, nzlo_ref, nzhi_ref,
     u_ref, utedge_ref, uzedge_ref) = refs[:11]
    rest = refs[11:]
    if first:
        out_ref, tfirst_ref, tlast_ref, zfirst_ref, zlast_ref = rest[:5]
        scratch = rest[5:]
    else:
        psi_ref, tlo_ref, thi_ref, zlo_ref, zhi_ref = rest[:5]
        out_ref = rest[5]
        scratch = rest[6:]
    pad_ref, src_ref, zlo_s, zhi_s, u8, ut8, uz8 = scratch
    S, C, RI, T, ROWS, L = src_ref.shape
    Z = ROWS // 2
    K = noise_ref.shape[3]
    span = T // K
    h = pl.program_id(0)
    lower = pl.ds(0, Z)
    upper = pl.ds(Z, Z)

    @pl.when(h == 0)
    def _():
        for a in range(3):
            for b in range(3):
                for ri in range(RI):
                    for half in (lower, upper):
                        ut8[a, b, ri, pl.ds(0, 1), half] = utedge_ref[a, b, ri]
                        ut8[a, b, ri, pl.ds(1, T), half] = u_ref[3, a, b, ri]
                        for t in range(T):
                            uz8[a, b, ri, t, half] = jnp.broadcast_to(uzedge_ref[a, b, ri, t], (Z, L))
                        for mu in range(4):
                            u8[mu, a, b, ri, :, half] = u_ref[mu, a, b, ri]

    for s in range(S):
        for c in range(C):
            for ri in range(RI):
                for g, half in ((0, lower), (1, upper)):
                    r = 2 * h + g
                    fs = smask_ref[r * S + s]
                    for t in range(T):
                        src_ref[s, c, ri, t, half] = noise_ref[g, c, ri, t // span] * (
                            fs * tmask_ref[r * (T + 2) + t + 1])
                    if first:
                        pad_ref[s, c, ri, 0, half] = ntlo_ref[g, c, ri, 0] * (
                            fs * tmask_ref[r * (T + 2)] * sign_ref[0])
                        pad_ref[s, c, ri, T + 1, half] = nthi_ref[g, c, ri, 0] * (
                            fs * tmask_ref[r * (T + 2) + T + 1] * sign_ref[1])
                        for t in range(T):
                            f = fs * tmask_ref[r * (T + 2) + t + 1]
                            zlo_s[s, c, ri, t, half] = jnp.broadcast_to(nzlo_ref[g, c, ri, t // span] * f, (Z, L))
                            zhi_s[s, c, ri, t, half] = jnp.broadcast_to(nzhi_ref[g, c, ri, t // span] * f, (Z, L))
                    else:
                        for t in range(T):
                            if s < 2:
                                zlo_s[s, c, ri, t, half] = jnp.broadcast_to(zlo_ref[s, c, ri, t, pl.ds(g, 1)], (Z, L))
                                zhi_s[s, c, ri, t, half] = jnp.broadcast_to(zhi_ref[s, c, ri, t, pl.ds(g, 1)], (Z, L))
                            else:
                                zlo_s[s, c, ri, t, half] = jnp.zeros((Z, L), jnp.float32)
                                zhi_s[s, c, ri, t, half] = jnp.zeros((Z, L), jnp.float32)
                if first:
                    pad_ref[s, c, ri, pl.ds(1, T)] = src_ref[s, c, ri]
                else:
                    pad_ref[s, c, ri, pl.ds(1, T)] = psi_ref[s, c, ri]
                    if s < 2:
                        pad_ref[s, c, ri, pl.ds(0, 1)] = tlo_ref[s, c, ri].astype(jnp.float32) * sign_ref[0]
                        pad_ref[s, c, ri, pl.ds(T + 1, 1)] = thi_ref[s, c, ri].astype(jnp.float32) * sign_ref[1]
                    else:
                        pad_ref[s, c, ri, pl.ds(0, 1)] = jnp.zeros((1, ROWS, L), jnp.float32)
                        pad_ref[s, c, ri, pl.ds(T + 1, 1)] = jnp.zeros((1, ROWS, L), jnp.float32)
    xpos = lax.broadcasted_iota(jnp.int32, (ROWS, L), 1) % NX
    zpos = lax.broadcasted_iota(jnp.int32, (ROWS, L), 0) % Z
    x_last = xpos == NX - 1
    x_first = xpos == 0
    z_last = zpos == Z - 1
    z_first = zpos == 0

    def x_back(v):
        return jnp.where(x_first, pltpu.roll(v, L - NX + 1, axis=1), pltpu.roll(v, 1, axis=1))

    def body(t, carry):
        acc = [[[None, None] for _ in range(3)] for _ in range(4)]

        def shifted(s, c, ri, mu, stride):
            if mu == 3:
                return pad_ref[s, c, ri, t + 1 + stride]
            v = pad_ref[s, c, ri, t + 1]
            if mu == 2:
                if stride == 1:
                    return jnp.where(z_last, zhi_s[s, c, ri, t], pltpu.roll(v, ROWS - 1, axis=0))
                return jnp.where(z_first, zlo_s[s, c, ri, t], pltpu.roll(v, 1, axis=0))
            if mu == 1:
                return pltpu.roll(v, (L - NX) if stride == 1 else NX, axis=1)
            if stride == 1:
                return jnp.where(x_last, pltpu.roll(v, NX - 1, axis=1), pltpu.roll(v, L - 1, axis=1))
            return x_back(v)

        def back_link(mu, a, b, ri):
            if mu == 3:
                return ut8[a, b, ri, t]
            v = u8[mu, a, b, ri, t]
            if mu == 2:
                return jnp.where(z_first, uz8[a, b, ri, t], pltpu.roll(v, 1, axis=0))
            if mu == 1:
                return pltpu.roll(v, NX, axis=1)
            return x_back(v)

        for mu in range(4):
            perm = GAMMA_PERM[mu]
            heads = [0, 1]
            for stride in (1, -1):
                orient = -1 if stride == 1 else 1
                half = []
                for s in heads:
                    p = perm[s]
                    cr, ci = orient * GAMMA_REAL[mu][s], orient * GAMMA_IMAG[mu][s]
                    colours = []
                    for c in range(3):
                        sre = shifted(s, c, 0, mu, stride)
                        sim = shifted(s, c, 1, mu, stride)
                        pre, pim = times_phase(shifted(p, c, 0, mu, stride), shifted(p, c, 1, mu, stride), cr, ci)
                        colours.append((sre + pre, sim + pim))
                    half.append(colours)
                if stride == 1:
                    links = [[(u8[mu, a, b, 0, t], u8[mu, a, b, 1, t]) for b in range(3)] for a in range(3)]
                else:
                    links = [[(back_link(mu, b, a, 0), back_link(mu, b, a, 1)) for b in range(3)] for a in range(3)]
                for k, s in enumerate(heads):
                    p = perm[s]
                    cpr, cpi = orient * GAMMA_REAL[mu][p], orient * GAMMA_IMAG[mu][p]
                    for a in range(3):
                        sum_re = None
                        sum_im = None
                        for b in range(3):
                            hre, him = half[k][b]
                            lre, lim = links[a][b]
                            if stride == 1:
                                tre = lre * hre - lim * him
                                tim = lre * him + lim * hre
                            else:
                                tre = lre * hre + lim * him
                                tim = lre * him - lim * hre
                            sum_re = tre if sum_re is None else sum_re + tre
                            sum_im = tim if sum_im is None else sum_im + tim
                        for row, (vre, vim) in ((s, (sum_re, sum_im)), (p, times_phase(sum_re, sum_im, cpr, cpi))):
                            if acc[row][a][0] is None:
                                acc[row][a] = [vre, vim]
                            else:
                                acc[row][a] = [acc[row][a][0] + vre, acc[row][a][1] + vim]
        for s in range(4):
            for c in range(3):
                for ri in range(2):
                    psi = pad_ref[s, c, ri, t + 1]
                    src = src_ref[s, c, ri, t]
                    residual = src - (psi - kappa_hop * acc[s][c][ri])
                    out_ref[s, c, ri, t] = (psi + residual).astype(out_ref.dtype)
        return carry

    lax.fori_loop(0, T, body, 0)
    if first:
        for mu, stride, target, pick in (
            (3, 1, tfirst_ref, lambda s, c, ri: out_ref[s, c, ri, pl.ds(0, 1)]),
            (3, -1, tlast_ref, lambda s, c, ri: out_ref[s, c, ri, pl.ds(T - 1, 1)]),
        ):
            for k, (re, im) in enumerate(half_spinor(pick, mu, stride)):
                for c in range(C):
                    target[k, c, 0] = re[c].astype(target.dtype)
                    target[k, c, 1] = im[c].astype(target.dtype)
        for g in range(2):
            for mu, stride, target, row in ((2, 1, zfirst_ref, g * Z), (2, -1, zlast_ref, g * Z + Z - 1)):
                pick = lambda s, c, ri: out_ref[s, c, ri, :, pl.ds(row, 1), :]
                for k, (re, im) in enumerate(half_spinor(pick, mu, stride)):
                    for c in range(C):
                        target[k, c, 0, :, pl.ds(g, 1), :] = re[c]
                        target[k, c, 1, :, pl.ds(g, 1), :] = im[c]


def half_spinor(pick, mu, stride):
    orient = -1 if stride == 1 else 1
    rows = []
    for s in (0, 1):
        p = GAMMA_PERM[mu][s]
        cr, ci = orient * GAMMA_REAL[mu][s], orient * GAMMA_IMAG[mu][s]
        res, ims = [], []
        for c in range(3):
            pre, pim = times_phase(pick(p, c, 0), pick(p, c, 1), cr, ci)
            res.append(pick(s, c, 0) + pre)
            ims.append(pick(s, c, 1) + pim)
        rows.append((res, ims))
    return rows


def hopping_step(first, scalars, noise_parts, link_parts, spinor_parts):
    R, C, RI, K, Z, L = noise_parts[0].shape
    T = link_parts[0].shape[4]
    S = 4
    H = R // 2
    ROWS = 2 * Z
    index = lambda h: (h,) + (0,) * 6
    index6 = lambda h: (h,) + (0,) * 5
    whole = lambda x: pl.BlockSpec(x.shape, lambda h: (0,) * x.ndim)
    smem = pl.BlockSpec(memory_space=pltpu.SMEM)
    site_block = pl.BlockSpec((None, S, C, RI, T, ROWS, L), index)
    t_block = pl.BlockSpec((None, 2, C, RI, 1, ROWS, L), index)
    z_block = pl.BlockSpec((None, 2, C, RI, T, 2, L), index)
    noise_specs = [
        pl.BlockSpec((2, C, RI, K, Z, L), index6),
        pl.BlockSpec((2, C, RI, 1, Z, L), index6),
        pl.BlockSpec((2, C, RI, 1, Z, L), index6),
        pl.BlockSpec((2, C, RI, K, 1, L), index6),
        pl.BlockSpec((2, C, RI, K, 1, L), index6),
    ]
    in_specs = [smem, smem, smem] + noise_specs + [whole(x) for x in link_parts]
    site_shape = (H, S, C, RI, T, ROWS, L)
    if first:
        t_shape = jax.ShapeDtypeStruct((H, 2, C, RI, 1, ROWS, L), jnp.bfloat16)
        z_shape = jax.ShapeDtypeStruct((H, 2, C, RI, T, 2, L), jnp.float32)
        out_shape = [jax.ShapeDtypeStruct(site_shape, jnp.float32), t_shape, t_shape, z_shape, z_shape]
        out_specs = [site_block, t_block, t_block, z_block, z_block]
    else:
        in_specs += [site_block, t_block, t_block, z_block, z_block]
        out_shape = jax.ShapeDtypeStruct(site_shape, jnp.bfloat16)
        out_specs = site_block
    scratch = [
        pltpu.VMEM((S, C, RI, T + 2, ROWS, L), jnp.float32),
        pltpu.VMEM((S, C, RI, T, ROWS, L), jnp.float32),
        pltpu.VMEM((S, C, RI, T, ROWS, L), jnp.float32),
        pltpu.VMEM((S, C, RI, T, ROWS, L), jnp.float32),
        pltpu.VMEM((4, 3, 3, RI, T, ROWS, L), jnp.float32),
        pltpu.VMEM((3, 3, RI, T + 1, ROWS, L), jnp.float32),
        pltpu.VMEM((3, 3, RI, T, ROWS, L), jnp.float32),
    ]
    return pl.pallas_call(
        functools.partial(hop_kernel, first),
        grid=(H,),
        in_specs=in_specs,
        out_specs=out_specs,
        out_shape=out_shape,
        scratch_shapes=scratch,
        compiler_params=pltpu.CompilerParams(dimension_semantics=("arbitrary",)),
        interpret=INTERPRET,
    )(*scalars, *noise_parts, *link_parts, *spinor_parts)


def reduce_scatter_sa(partial_value):
    n = lax.axis_size("sa")
    if n & (n - 1):
        return lax.psum_scatter(partial_value, "sa", scatter_dimension=4, tiled=True)
    lead = partial_value.shape[:-1]
    width = partial_value.shape[-1] // n
    x = jnp.moveaxis(partial_value.reshape(lead + (n, width)), -2, 0)
    me = lax.axis_index("sa")
    d = n // 2
    while d >= 1:
        upper_mine = (me // d) % 2 == 1
        keep = jnp.where(upper_mine, x[d:], x[:d])
        send = jnp.where(upper_mine, x[:d], x[d:])
        x = keep + lax.ppermute(send, "sa", [(j, j ^ d) for j in range(n)])
        d //= 2
    return x[0]


def intersection_part(rounded, vector_piece):
    products = jnp.einsum(
        "tvcazs,hqcbtgzs->hgqabtv", vector_piece, rounded, preferred_element_type=jnp.float32
    )
    products = products.reshape((-1,) + products.shape[2:])
    real_part = products[:, :, 0, 0] + products[:, :, 1, 1]
    imag_part = products[:, :, 0, 1] - products[:, :, 1, 0]
    return jnp.stack([real_part, imag_part], axis=2)


def local_body(gauge_links, noise_slabs, offsets, vectors):
    partner_vectors = from_partner(vectors, "sec", 0)
    batch_rows = noise_slabs.shape[0]
    slab_length = gauge_links.shape[4]
    Z = gauge_links.shape[5]
    K = noise_slabs.shape[3]
    section_index = lax.axis_index("sec")
    slab_index = lax.axis_index("ta")
    slab_count = lax.axis_size("ta")
    lower_sign = jnp.where(slab_index == 0, -1.0, 1.0).astype(jnp.float32)
    upper_sign = jnp.where(slab_index == slab_count - 1, -1.0, 1.0).astype(jnp.float32)
    signs = jnp.stack([lower_sign, upper_sign])
    t_start = slab_index * slab_length
    own_offsets = lax.dynamic_slice_in_dim(offsets, section_index * batch_rows, batch_rows)
    rhs_index = section_index * batch_rows + jnp.arange(batch_rows)
    spin_mask = (jnp.arange(4)[None, :] == rhs_index[:, None] % 4).astype(jnp.float32)
    times = t_start - 1 + jnp.arange(slab_length + 2)
    time_mask = (times[None, :] % TDIL == own_offsets[:, None]).astype(jnp.float32)
    scalars = (spin_mask.reshape(-1), time_mask.reshape(-1), signs)
    noise_parts = (
        noise_slabs,
        passed_along(noise_slabs[:, :, :, K - 1:], "ta", 1),
        passed_along(noise_slabs[:, :, :, :1], "ta", -1),
        passed_along(noise_slabs[:, :, :, :, Z - 1:], "sa", 1),
        passed_along(noise_slabs[:, :, :, :, :1], "sa", -1),
    )
    link_parts = (
        gauge_links,
        passed_along(gauge_links[3, :, :, :, -1:, :, :], "ta", 1),
        passed_along(gauge_links[2, :, :, :, :, -1:, :], "sa", 1),
    )
    spinor, t_first, t_last, z_first, z_last = hopping_step(True, scalars, noise_parts, link_parts, ())
    halos = (
        passed_along(t_last, "ta", 1),
        passed_along(t_first, "ta", -1),
        passed_along(z_last, "sa", 1),
        passed_along(z_first, "sa", -1),
    )
    rounded = hopping_step(False, scalars, noise_parts, link_parts, (spinor,) + halos)
    H, S, C, RI, T, ROWS, L = rounded.shape
    rounded = rounded.reshape(H, S, C, RI, T, 2, ROWS // 2, L)
    own_part = intersection_part(rounded, vectors)
    partner_part = intersection_part(rounded, partner_vectors)
    lower_half = jnp.where(section_index == 0, own_part, partner_part)
    upper_half = jnp.where(section_index == 0, partner_part, own_part)
    partial_value = jnp.concatenate([lower_half, upper_half], axis=4)
    return reduce_scatter_sa(partial_value)


def solution(mesh):
    in_specs = (
        P(None, None, None, None, "ta", "sa", None),
        P("sec", None, None, "ta", "sa", None),
        P(),
        P("ta", "sec", None, None, "sa", None),
    )
    out_specs = P("sec", None, None, "ta", "sa")
    return jax.shard_map(local_body, mesh=mesh, in_specs=in_specs, out_specs=out_specs, check_vma=False)
```

```python
import functools

import jax
import jax.numpy as jnp
from jax import lax
from jax.experimental import pallas as pl
from jax.experimental.pallas import tpu as pltpu
from jax.sharding import PartitionSpec as P


NX = 32
TDIL = 4
INTERPRET = False


kappa_hop = 0.12
GAMMA_PERM = ((3, 2, 1, 0), (3, 2, 1, 0), (2, 3, 0, 1), (2, 3, 0, 1))
GAMMA_REAL = ((0, 0, 0, 0), (-1, 1, 1, -1), (0, 0, 0, 0), (1, 1, 1, 1))
GAMMA_IMAG = ((1, 1, -1, -1), (0, 0, 0, 0), (1, -1, -1, 1), (0, 0, 0, 0))


def passed_along(value, axis, steps):
    count = lax.axis_size(axis)
    pairs = [(source, (source + steps) % count) for source in range(count)]
    return lax.ppermute(value, axis, pairs)


def from_partner(x, axis, stride):
    return lax.ppermute(x, axis, [(i, i ^ 1 << stride) for i in range(lax.axis_size(axis))])


def times_phase(re, im, cr, ci):
    if ci == 0:
        if cr == 1:
            return re, im
        return -re, -im
    if ci == 1:
        return -im, re
    return im, -re


def hop_kernel(first, R, *refs):
    (smask_ref, tmask_ref, sign_ref, noise_ref, tup_ref, nthi_ref, zup_ref, nzhi_ref, u_ref) = refs[:9]
    rest = refs[9:]
    if first:
        out_ref, tfirst_ref, tlast_ref, zfirst_ref, zlast_ref = rest[:5]
        scratch = rest[5:]
    else:
        psi_ref, tlo_ref, thi_ref, zlo_ref, zhi_ref = rest[:5]
        out_ref = rest[5]
        scratch = rest[6:]
    pad_ref, src_ref, zlo_s, zhi_s, u8, ut8, uz8 = scratch
    S, C, RI, T, ROWS, L = src_ref.shape
    Z = ROWS // 2
    K = noise_ref.shape[3]
    span = T // K
    h = pl.program_id(0)
    lower = pl.ds(0, Z)
    upper = pl.ds(Z, Z)

    @pl.when(h == 0)
    def _():
        for a in range(3):
            for b in range(3):
                for ri in range(RI):
                    edge = (a * 3 + b) * RI + ri
                    for half in (lower, upper):
                        ut8[a, b, ri, 0, half] = tup_ref[R * 6 + edge]
                        ut8[a, b, ri, pl.ds(1, T), half] = u_ref[3, a, b, ri]
                        for t in range(T):
                            uz8[a, b, ri, t, half] = jnp.broadcast_to(zup_ref[R * 6 * K + edge * T + t], (Z, L))
                        for mu in range(4):
                            u8[mu, a, b, ri, :, half] = u_ref[mu, a, b, ri]

    for s in range(S):
        for c in range(C):
            for ri in range(RI):
                for g, half in ((0, lower), (1, upper)):
                    r = 2 * h + g
                    fs = smask_ref[r * S + s]
                    for t in range(T):
                        src_ref[s, c, ri, t, half] = noise_ref[g, c, ri, t // span] * (
                            fs * tmask_ref[r * (T + 2) + t + 1])
                    if first:
                        pad_ref[s, c, ri, 0, half] = tup_ref[(r * 3 + c) * RI + ri] * (
                            fs * tmask_ref[r * (T + 2)] * sign_ref[0])
                        pad_ref[s, c, ri, T + 1, half] = nthi_ref[g, c, ri, 0] * (
                            fs * tmask_ref[r * (T + 2) + T + 1] * sign_ref[1])
                        for t in range(T):
                            f = fs * tmask_ref[r * (T + 2) + t + 1]
                            zlo_s[s, c, ri, t, half] = jnp.broadcast_to(
                                zup_ref[((r * 3 + c) * RI + ri) * K + t // span] * f, (Z, L))
                            zhi_s[s, c, ri, t, half] = jnp.broadcast_to(nzhi_ref[g, c, ri, t // span] * f, (Z, L))
                    else:
                        for t in range(T):
                            if s < 2:
                                zlo_s[s, c, ri, t, half] = jnp.broadcast_to(zlo_ref[s, c, ri, t, pl.ds(g, 1)], (Z, L))
                                zhi_s[s, c, ri, t, half] = jnp.broadcast_to(zhi_ref[s, c, ri, t, pl.ds(g, 1)], (Z, L))
                            else:
                                zlo_s[s, c, ri, t, half] = jnp.zeros((Z, L), jnp.float32)
                                zhi_s[s, c, ri, t, half] = jnp.zeros((Z, L), jnp.float32)
                if first:
                    pad_ref[s, c, ri, pl.ds(1, T)] = src_ref[s, c, ri]
                else:
                    pad_ref[s, c, ri, pl.ds(1, T)] = psi_ref[s, c, ri]
                    if s < 2:
                        pad_ref[s, c, ri, pl.ds(0, 1)] = tlo_ref[s, c, ri].astype(jnp.float32) * sign_ref[0]
                        pad_ref[s, c, ri, pl.ds(T + 1, 1)] = thi_ref[s, c, ri].astype(jnp.float32) * sign_ref[1]
                    else:
                        pad_ref[s, c, ri, pl.ds(0, 1)] = jnp.zeros((1, ROWS, L), jnp.float32)
                        pad_ref[s, c, ri, pl.ds(T + 1, 1)] = jnp.zeros((1, ROWS, L), jnp.float32)
    xpos = lax.broadcasted_iota(jnp.int32, (ROWS, L), 1) % NX
    zpos = lax.broadcasted_iota(jnp.int32, (ROWS, L), 0) % Z
    x_last = xpos == NX - 1
    x_first = xpos == 0
    z_last = zpos == Z - 1
    z_first = zpos == 0

    def x_back(v):
        return jnp.where(x_first, pltpu.roll(v, L - NX + 1, axis=1), pltpu.roll(v, 1, axis=1))

    def body(t, carry):
        acc = [[[None, None] for _ in range(3)] for _ in range(4)]

        def shifted(s, c, ri, mu, stride):
            if mu == 3:
                return pad_ref[s, c, ri, t + 1 + stride]
            v = pad_ref[s, c, ri, t + 1]
            if mu == 2:
                if stride == 1:
                    return jnp.where(z_last, zhi_s[s, c, ri, t], pltpu.roll(v, ROWS - 1, axis=0))
                return jnp.where(z_first, zlo_s[s, c, ri, t], pltpu.roll(v, 1, axis=0))
            if mu == 1:
                return pltpu.roll(v, (L - NX) if stride == 1 else NX, axis=1)
            if stride == 1:
                return jnp.where(x_last, pltpu.roll(v, NX - 1, axis=1), pltpu.roll(v, L - 1, axis=1))
            return x_back(v)

        def back_link(mu, a, b, ri):
            if mu == 3:
                return ut8[a, b, ri, t]
            v = u8[mu, a, b, ri, t]
            if mu == 2:
                return jnp.where(z_first, uz8[a, b, ri, t], pltpu.roll(v, 1, axis=0))
            if mu == 1:
                return pltpu.roll(v, NX, axis=1)
            return x_back(v)

        for mu in range(4):
            perm = GAMMA_PERM[mu]
            heads = [0, 1]
            for stride in (1, -1):
                orient = -1 if stride == 1 else 1
                half = []
                for s in heads:
                    p = perm[s]
                    cr, ci = orient * GAMMA_REAL[mu][s], orient * GAMMA_IMAG[mu][s]
                    colours = []
                    for c in range(3):
                        sre = shifted(s, c, 0, mu, stride)
                        sim = shifted(s, c, 1, mu, stride)
                        pre, pim = times_phase(shifted(p, c, 0, mu, stride), shifted(p, c, 1, mu, stride), cr, ci)
                        colours.append((sre + pre, sim + pim))
                    half.append(colours)
                if stride == 1:
                    links = [[(u8[mu, a, b, 0, t], u8[mu, a, b, 1, t]) for b in range(3)] for a in range(3)]
                else:
                    links = [[(back_link(mu, b, a, 0), back_link(mu, b, a, 1)) for b in range(3)] for a in range(3)]
                for k, s in enumerate(heads):
                    p = perm[s]
                    cpr, cpi = orient * GAMMA_REAL[mu][p], orient * GAMMA_IMAG[mu][p]
                    for a in range(3):
                        sum_re = None
                        sum_im = None
                        for b in range(3):
                            hre, him = half[k][b]
                            lre, lim = links[a][b]
                            if stride == 1:
                                tre = lre * hre - lim * him
                                tim = lre * him + lim * hre
                            else:
                                tre = lre * hre + lim * him
                                tim = lre * him - lim * hre
                            sum_re = tre if sum_re is None else sum_re + tre
                            sum_im = tim if sum_im is None else sum_im + tim
                        for row, (vre, vim) in ((s, (sum_re, sum_im)), (p, times_phase(sum_re, sum_im, cpr, cpi))):
                            if acc[row][a][0] is None:
                                acc[row][a] = [vre, vim]
                            else:
                                acc[row][a] = [acc[row][a][0] + vre, acc[row][a][1] + vim]
        for s in range(4):
            for c in range(3):
                for ri in range(2):
                    psi = pad_ref[s, c, ri, t + 1]
                    src = src_ref[s, c, ri, t]
                    residual = src - (psi - kappa_hop * acc[s][c][ri])
                    value = psi + residual
                    if first:
                        out_ref[s, c, ri, t] = value
                    else:
                        for g in range(2):
                            out_ref[s, c, ri, t, g] = value[g * Z:(g + 1) * Z].astype(out_ref.dtype)
        return carry

    lax.fori_loop(0, T, body, 0)
    if first:
        for mu, stride, target, pick in (
            (3, 1, tfirst_ref, lambda s, c, ri: out_ref[s, c, ri, pl.ds(0, 1)]),
            (3, -1, tlast_ref, lambda s, c, ri: out_ref[s, c, ri, pl.ds(T - 1, 1)]),
        ):
            for k, (re, im) in enumerate(half_spinor(pick, mu, stride)):
                for c in range(C):
                    target[k, c, 0] = re[c].astype(target.dtype)
                    target[k, c, 1] = im[c].astype(target.dtype)
        for g in range(2):
            for mu, stride, target, row in ((2, 1, zfirst_ref, g * Z), (2, -1, zlast_ref, g * Z + Z - 1)):
                pick = lambda s, c, ri: out_ref[s, c, ri, :, pl.ds(row, 1), :]
                for k, (re, im) in enumerate(half_spinor(pick, mu, stride)):
                    for c in range(C):
                        target[k, c, 0, :, pl.ds(g, 1), :] = re[c]
                        target[k, c, 1, :, pl.ds(g, 1), :] = im[c]


def half_spinor(pick, mu, stride):
    orient = -1 if stride == 1 else 1
    rows = []
    for s in (0, 1):
        p = GAMMA_PERM[mu][s]
        cr, ci = orient * GAMMA_REAL[mu][s], orient * GAMMA_IMAG[mu][s]
        res, ims = [], []
        for c in range(3):
            pre, pim = times_phase(pick(p, c, 0), pick(p, c, 1), cr, ci)
            res.append(pick(s, c, 0) + pre)
            ims.append(pick(s, c, 1) + pim)
        rows.append((res, ims))
    return rows


def hopping_step(first, scalars, noise_parts, link_parts, spinor_parts):
    R, C, RI, K, Z, L = noise_parts[0].shape
    T = link_parts[0].shape[4]
    tup, zup = noise_parts[1], noise_parts[3]
    S = 4
    H = R // 2
    ROWS = 2 * Z
    index = lambda h: (h,) + (0,) * 6
    index6 = lambda h: (h,) + (0,) * 5
    whole = lambda x: pl.BlockSpec(x.shape, lambda h: (0,) * x.ndim)
    smem = pl.BlockSpec(memory_space=pltpu.SMEM)
    site_block = pl.BlockSpec((None, S, C, RI, T, ROWS, L), index)
    t_block = pl.BlockSpec((None, 2, C, RI, 1, ROWS, L), index)
    z_block = pl.BlockSpec((None, 2, C, RI, T, 2, L), index)
    noise_specs = [
        pl.BlockSpec((2, C, RI, K, Z, L), index6),
        whole(tup),
        pl.BlockSpec((2, C, RI, 1, Z, L), index6),
        whole(zup),
        pl.BlockSpec((2, C, RI, K, 1, L), index6),
    ]
    in_specs = [smem, smem, smem] + noise_specs + [whole(x) for x in link_parts]
    site_shape = (H, S, C, RI, T, ROWS, L)
    if first:
        t_shape = jax.ShapeDtypeStruct((H, 2, C, RI, 1, ROWS, L), jnp.bfloat16)
        z_shape = jax.ShapeDtypeStruct((H, 2, C, RI, T, 2, L), jnp.float32)
        out_shape = [jax.ShapeDtypeStruct(site_shape, jnp.float32), t_shape, t_shape, z_shape, z_shape]
        out_specs = [site_block, t_block, t_block, z_block, z_block]
    else:
        in_specs += [site_block, t_block, t_block, z_block, z_block]
        out_shape = jax.ShapeDtypeStruct((H, S, C, RI, T, 2, Z, L), jnp.bfloat16)
        out_specs = pl.BlockSpec((None, S, C, RI, T, 2, Z, L), lambda h: (h,) + (0,) * 7)
    scratch = [
        pltpu.VMEM((S, C, RI, T + 2, ROWS, L), jnp.float32),
        pltpu.VMEM((S, C, RI, T, ROWS, L), jnp.float32),
        pltpu.VMEM((S, C, RI, T, ROWS, L), jnp.float32),
        pltpu.VMEM((S, C, RI, T, ROWS, L), jnp.float32),
        pltpu.VMEM((4, 3, 3, RI, T, ROWS, L), jnp.float32),
        pltpu.VMEM((3, 3, RI, T + 1, ROWS, L), jnp.float32),
        pltpu.VMEM((3, 3, RI, T, ROWS, L), jnp.float32),
    ]
    return pl.pallas_call(
        functools.partial(hop_kernel, first, R),
        grid=(H,),
        in_specs=in_specs,
        out_specs=out_specs,
        out_shape=out_shape,
        scratch_shapes=scratch,
        compiler_params=pltpu.CompilerParams(dimension_semantics=("arbitrary",)),
        interpret=INTERPRET,
    )(*scalars, *noise_parts, *link_parts, *spinor_parts)


def reduce_scatter_sa(partial_value):
    n = lax.axis_size("sa")
    if n & (n - 1):
        return lax.psum_scatter(partial_value, "sa", scatter_dimension=4, tiled=True)
    lead = partial_value.shape[:-1]
    width = partial_value.shape[-1] // n
    x = jnp.moveaxis(partial_value.reshape(lead + (n, width)), -2, 0)
    me = lax.axis_index("sa")
    d = n // 2
    while d >= 1:
        upper_mine = (me // d) % 2 == 1
        keep = jnp.where(upper_mine, x[d:], x[:d])
        send = jnp.where(upper_mine, x[:d], x[d:])
        x = keep + lax.ppermute(send, "sa", [(j, j ^ d) for j in range(n)])
        d //= 2
    return x[0]


def intersection_part(rounded, vector_piece):
    products = jnp.einsum(
        "tvcazs,hqcbtgzs->hgqabtv", vector_piece, rounded, preferred_element_type=jnp.float32
    )
    products = products.reshape((-1,) + products.shape[2:])
    real_part = products[:, :, 0, 0] + products[:, :, 1, 1]
    imag_part = products[:, :, 0, 1] - products[:, :, 1, 0]
    return jnp.stack([real_part, imag_part], axis=2)


def local_body(gauge_links, noise_slabs, offsets, vectors):
    partner_vectors = from_partner(vectors, "sec", 0)
    batch_rows = noise_slabs.shape[0]
    slab_length = gauge_links.shape[4]
    Z = gauge_links.shape[5]
    K = noise_slabs.shape[3]
    section_index = lax.axis_index("sec")
    slab_index = lax.axis_index("ta")
    slab_count = lax.axis_size("ta")
    lower_sign = jnp.where(slab_index == 0, -1.0, 1.0).astype(jnp.float32)
    upper_sign = jnp.where(slab_index == slab_count - 1, -1.0, 1.0).astype(jnp.float32)
    signs = jnp.stack([lower_sign, upper_sign])
    t_start = slab_index * slab_length
    own_offsets = lax.dynamic_slice_in_dim(offsets, section_index * batch_rows, batch_rows)
    rhs_index = section_index * batch_rows + jnp.arange(batch_rows)
    spin_mask = (jnp.arange(4)[None, :] == rhs_index[:, None] % 4).astype(jnp.float32)
    times = t_start - 1 + jnp.arange(slab_length + 2)
    time_mask = (times[None, :] % TDIL == own_offsets[:, None]).astype(jnp.float32)
    scalars = (spin_mask.reshape(-1), time_mask.reshape(-1), signs)
    L = noise_slabs.shape[-1]
    t_up = jnp.concatenate([
        noise_slabs[:, :, :, K - 1].reshape(-1, Z, L),
        gauge_links[3, :, :, :, slab_length - 1].reshape(-1, Z, L),
    ])
    z_up = jnp.concatenate([
        noise_slabs[:, :, :, :, Z - 1].reshape(-1, 1, L),
        gauge_links[2, :, :, :, :, Z - 1].reshape(-1, 1, L),
    ])
    noise_parts = (
        noise_slabs,
        passed_along(t_up, "ta", 1),
        passed_along(noise_slabs[:, :, :, :1], "ta", -1),
        passed_along(z_up, "sa", 1),
        passed_along(noise_slabs[:, :, :, :, :1], "sa", -1),
    )
    link_parts = (gauge_links,)
    spinor, t_first, t_last, z_first, z_last = hopping_step(True, scalars, noise_parts, link_parts, ())
    halos = (
        passed_along(t_last, "ta", 1),
        passed_along(t_first, "ta", -1),
        passed_along(z_last, "sa", 1),
        passed_along(z_first, "sa", -1),
    )
    rounded = hopping_step(False, scalars, noise_parts, link_parts, (spinor,) + halos)
    own_part = intersection_part(rounded, vectors)
    partner_part = intersection_part(rounded, partner_vectors)
    lower_half = jnp.where(section_index == 0, own_part, partner_part)
    upper_half = jnp.where(section_index == 0, partner_part, own_part)
    partial_value = jnp.concatenate([lower_half, upper_half], axis=4)
    return reduce_scatter_sa(partial_value)


def solution(mesh):
    in_specs = (
        P(None, None, None, None, "ta", "sa", None),
        P("sec", None, None, "ta", "sa", None),
        P(),
        P("ta", "sec", None, None, "sa", None),
    )
    out_specs = P("sec", None, None, "ta", "sa")
    return jax.shard_map(local_body, mesh=mesh, in_specs=in_specs, out_specs=out_specs, check_vma=False)
```

```python
import functools

import jax
import jax.numpy as jnp
from jax import lax
from jax.experimental import pallas as pl
from jax.experimental.pallas import tpu as pltpu
from jax.sharding import PartitionSpec as P


NX = 32
TDIL = 4
INTERPRET = False


kappa_hop = 0.12
GAMMA_PERM = ((3, 2, 1, 0), (3, 2, 1, 0), (2, 3, 0, 1), (2, 3, 0, 1))
GAMMA_REAL = ((0, 0, 0, 0), (-1, 1, 1, -1), (0, 0, 0, 0), (1, 1, 1, 1))
GAMMA_IMAG = ((1, 1, -1, -1), (0, 0, 0, 0), (1, -1, -1, 1), (0, 0, 0, 0))


def passed_along(value, axis, steps):
    count = lax.axis_size(axis)
    pairs = [(source, (source + steps) % count) for source in range(count)]
    return lax.ppermute(value, axis, pairs)


def from_partner(x, axis, stride):
    return lax.ppermute(x, axis, [(i, i ^ 1 << stride) for i in range(lax.axis_size(axis))])


def times_phase(re, im, cr, ci):
    if ci == 0:
        if cr == 1:
            return re, im
        return -re, -im
    if ci == 1:
        return -im, re
    return im, -re


def hop_kernel(first, *refs):
    (smask_ref, tmask_ref, sign_ref, noise_ref, ntlo_ref, nthi_ref, nzlo_ref, nzhi_ref,
     u_ref, utedge_ref, uzedge_ref) = refs[:11]
    rest = refs[11:]
    if first:
        out_ref, tfirst_ref, tlast_ref, zfirst_ref, zlast_ref = rest[:5]
        scratch = rest[5:]
    else:
        psi_ref, tlo_ref, thi_ref, zlo_ref, zhi_ref = rest[:5]
        out_ref = rest[5]
        scratch = rest[6:]
    pad_ref, src_ref, zlo_s, zhi_s, u8, ut8, uz8 = scratch
    S, C, RI, T, ROWS, L = src_ref.shape
    Z = ROWS // 2
    K = noise_ref.shape[3]
    span = T // K
    h = pl.program_id(0)
    lower = pl.ds(0, Z)
    upper = pl.ds(Z, Z)

    @pl.when(h == 0)
    def _():
        for a in range(3):
            for b in range(3):
                for ri in range(RI):
                    for half in (lower, upper):
                        ut8[a, b, ri, pl.ds(0, 1), half] = utedge_ref[a, b, ri]
                        ut8[a, b, ri, pl.ds(1, T), half] = u_ref[3, a, b, ri]
                        for t in range(T):
                            uz8[a, b, ri, t, half] = jnp.broadcast_to(uzedge_ref[a, b, ri, t], (Z, L))
                        for mu in range(4):
                            u8[mu, a, b, ri, :, half] = u_ref[mu, a, b, ri]

    for s in range(S):
        for c in range(C):
            for ri in range(RI):
                for g, half in ((0, lower), (1, upper)):
                    r = 2 * h + g
                    fs = smask_ref[r * S + s]
                    for t in range(T):
                        src_ref[s, c, ri, t, half] = noise_ref[g, c, ri, t // span] * (
                            fs * tmask_ref[r * (T + 2) + t + 1])
                    if first:
                        pad_ref[s, c, ri, 0, half] = ntlo_ref[g, c, ri, 0] * (
                            fs * tmask_ref[r * (T + 2)] * sign_ref[0])
                        pad_ref[s, c, ri, T + 1, half] = nthi_ref[g, c, ri, 0] * (
                            fs * tmask_ref[r * (T + 2) + T + 1] * sign_ref[1])
                        for t in range(T):
                            f = fs * tmask_ref[r * (T + 2) + t + 1]
                            zlo_s[s, c, ri, t, half] = jnp.broadcast_to(nzlo_ref[g, c, ri, t // span] * f, (Z, L))
                            zhi_s[s, c, ri, t, half] = jnp.broadcast_to(nzhi_ref[g, c, ri, t // span] * f, (Z, L))
                    else:
                        for t in range(T):
                            if s < 2:
                                zlo_s[s, c, ri, t, half] = jnp.broadcast_to(zlo_ref[s, c, ri, t, pl.ds(g, 1)], (Z, L))
                                zhi_s[s, c, ri, t, half] = jnp.broadcast_to(zhi_ref[s, c, ri, t, pl.ds(g, 1)], (Z, L))
                            else:
                                zlo_s[s, c, ri, t, half] = jnp.zeros((Z, L), jnp.float32)
                                zhi_s[s, c, ri, t, half] = jnp.zeros((Z, L), jnp.float32)
                if first:
                    pad_ref[s, c, ri, pl.ds(1, T)] = src_ref[s, c, ri]
                else:
                    pad_ref[s, c, ri, pl.ds(1, T)] = psi_ref[s, c, ri]
                    if s < 2:
                        pad_ref[s, c, ri, pl.ds(0, 1)] = tlo_ref[s, c, ri].astype(jnp.float32) * sign_ref[0]
                        pad_ref[s, c, ri, pl.ds(T + 1, 1)] = thi_ref[s, c, ri].astype(jnp.float32) * sign_ref[1]
                    else:
                        pad_ref[s, c, ri, pl.ds(0, 1)] = jnp.zeros((1, ROWS, L), jnp.float32)
                        pad_ref[s, c, ri, pl.ds(T + 1, 1)] = jnp.zeros((1, ROWS, L), jnp.float32)
    xpos = lax.broadcasted_iota(jnp.int32, (ROWS, L), 1) % NX
    zpos = lax.broadcasted_iota(jnp.int32, (ROWS, L), 0) % Z
    x_last = xpos == NX - 1
    x_first = xpos == 0
    z_last = zpos == Z - 1
    z_first = zpos == 0

    def x_back(v):
        return jnp.where(x_first, pltpu.roll(v, L - NX + 1, axis=1), pltpu.roll(v, 1, axis=1))

    def body(t, carry):
        acc = [[[None, None] for _ in range(3)] for _ in range(4)]

        def shifted(s, c, ri, mu, stride):
            if mu == 3:
                return pad_ref[s, c, ri, t + 1 + stride]
            v = pad_ref[s, c, ri, t + 1]
            if mu == 2:
                if stride == 1:
                    return jnp.where(z_last, zhi_s[s, c, ri, t], pltpu.roll(v, ROWS - 1, axis=0))
                return jnp.where(z_first, zlo_s[s, c, ri, t], pltpu.roll(v, 1, axis=0))
            if mu == 1:
                return pltpu.roll(v, (L - NX) if stride == 1 else NX, axis=1)
            if stride == 1:
                return jnp.where(x_last, pltpu.roll(v, NX - 1, axis=1), pltpu.roll(v, L - 1, axis=1))
            return x_back(v)

        def back_link(mu, a, b, ri):
            if mu == 3:
                return ut8[a, b, ri, t]
            v = u8[mu, a, b, ri, t]
            if mu == 2:
                return jnp.where(z_first, uz8[a, b, ri, t], pltpu.roll(v, 1, axis=0))
            if mu == 1:
                return pltpu.roll(v, NX, axis=1)
            return x_back(v)

        for mu in range(4):
            perm = GAMMA_PERM[mu]
            heads = [0, 1]
            for stride in (1, -1):
                orient = -1 if stride == 1 else 1
                half = []
                for s in heads:
                    p = perm[s]
                    cr, ci = orient * GAMMA_REAL[mu][s], orient * GAMMA_IMAG[mu][s]
                    colours = []
                    for c in range(3):
                        sre = shifted(s, c, 0, mu, stride)
                        sim = shifted(s, c, 1, mu, stride)
                        pre, pim = times_phase(shifted(p, c, 0, mu, stride), shifted(p, c, 1, mu, stride), cr, ci)
                        colours.append((sre + pre, sim + pim))
                    half.append(colours)
                if stride == 1:
                    links = [[(u8[mu, a, b, 0, t], u8[mu, a, b, 1, t]) for b in range(3)] for a in range(3)]
                else:
                    links = [[(back_link(mu, b, a, 0), back_link(mu, b, a, 1)) for b in range(3)] for a in range(3)]
                for k, s in enumerate(heads):
                    p = perm[s]
                    cpr, cpi = orient * GAMMA_REAL[mu][p], orient * GAMMA_IMAG[mu][p]
                    for a in range(3):
                        sum_re = None
                        sum_im = None
                        for b in range(3):
                            hre, him = half[k][b]
                            lre, lim = links[a][b]
                            if stride == 1:
                                tre = lre * hre - lim * him
                                tim = lre * him + lim * hre
                            else:
                                tre = lre * hre + lim * him
                                tim = lre * him - lim * hre
                            sum_re = tre if sum_re is None else sum_re + tre
                            sum_im = tim if sum_im is None else sum_im + tim
                        for row, (vre, vim) in ((s, (sum_re, sum_im)), (p, times_phase(sum_re, sum_im, cpr, cpi))):
                            if acc[row][a][0] is None:
                                acc[row][a] = [vre, vim]
                            else:
                                acc[row][a] = [acc[row][a][0] + vre, acc[row][a][1] + vim]
        for s in range(4):
            for c in range(3):
                for ri in range(2):
                    psi = pad_ref[s, c, ri, t + 1]
                    src = src_ref[s, c, ri, t]
                    residual = src - (psi - kappa_hop * acc[s][c][ri])
                    value = psi + residual
                    if first:
                        out_ref[s, c, ri, t] = value
                    else:
                        for g in range(2):
                            out_ref[s, c, ri, t, g] = value[g * Z:(g + 1) * Z].astype(out_ref.dtype)
        return carry

    lax.fori_loop(0, T, body, 0)
    if first:
        for mu, stride, target, pick in (
            (3, 1, tfirst_ref, lambda s, c, ri: out_ref[s, c, ri, pl.ds(0, 1)]),
            (3, -1, tlast_ref, lambda s, c, ri: out_ref[s, c, ri, pl.ds(T - 1, 1)]),
        ):
            for k, (re, im) in enumerate(half_spinor(pick, mu, stride)):
                for c in range(C):
                    target[k, c, 0] = re[c].astype(target.dtype)
                    target[k, c, 1] = im[c].astype(target.dtype)
        for g in range(2):
            for mu, stride, target, row in ((2, 1, zfirst_ref, g * Z), (2, -1, zlast_ref, g * Z + Z - 1)):
                pick = lambda s, c, ri: out_ref[s, c, ri, :, pl.ds(row, 1), :]
                for k, (re, im) in enumerate(half_spinor(pick, mu, stride)):
                    for c in range(C):
                        target[k, c, 0, :, pl.ds(g, 1), :] = re[c]
                        target[k, c, 1, :, pl.ds(g, 1), :] = im[c]


def half_spinor(pick, mu, stride):
    orient = -1 if stride == 1 else 1
    rows = []
    for s in (0, 1):
        p = GAMMA_PERM[mu][s]
        cr, ci = orient * GAMMA_REAL[mu][s], orient * GAMMA_IMAG[mu][s]
        res, ims = [], []
        for c in range(3):
            pre, pim = times_phase(pick(p, c, 0), pick(p, c, 1), cr, ci)
            res.append(pick(s, c, 0) + pre)
            ims.append(pick(s, c, 1) + pim)
        rows.append((res, ims))
    return rows


def hopping_step(first, scalars, noise_parts, link_parts, spinor_parts):
    R, C, RI, K, Z, L = noise_parts[0].shape
    T = link_parts[0].shape[4]
    S = 4
    H = R // 2
    ROWS = 2 * Z
    index = lambda h: (h,) + (0,) * 6
    index6 = lambda h: (h,) + (0,) * 5
    whole = lambda x: pl.BlockSpec(x.shape, lambda h: (0,) * x.ndim)
    smem = pl.BlockSpec(memory_space=pltpu.SMEM)
    site_block = pl.BlockSpec((None, S, C, RI, T, ROWS, L), index)
    t_block = pl.BlockSpec((None, 2, C, RI, 1, ROWS, L), index)
    z_block = pl.BlockSpec((None, 2, C, RI, T, 2, L), index)
    noise_specs = [
        pl.BlockSpec((2, C, RI, K, Z, L), index6),
        pl.BlockSpec((2, C, RI, 1, Z, L), index6),
        pl.BlockSpec((2, C, RI, 1, Z, L), index6),
        pl.BlockSpec((2, C, RI, K, 1, L), index6),
        pl.BlockSpec((2, C, RI, K, 1, L), index6),
    ]
    in_specs = [smem, smem, smem] + noise_specs + [whole(x) for x in link_parts]
    site_shape = (H, S, C, RI, T, ROWS, L)
    if first:
        t_shape = jax.ShapeDtypeStruct((H, 2, C, RI, 1, ROWS, L), jnp.bfloat16)
        z_shape = jax.ShapeDtypeStruct((H, 2, C, RI, T, 2, L), jnp.float32)
        out_shape = [jax.ShapeDtypeStruct(site_shape, jnp.float32), t_shape, t_shape, z_shape, z_shape]
        out_specs = [site_block, t_block, t_block, z_block, z_block]
    else:
        in_specs += [site_block, t_block, t_block, z_block, z_block]
        out_shape = jax.ShapeDtypeStruct((H, S, C, RI, T, 2, Z, L), jnp.bfloat16)
        out_specs = pl.BlockSpec((None, S, C, RI, T, 2, Z, L), lambda h: (h,) + (0,) * 7)
    scratch = [
        pltpu.VMEM((S, C, RI, T + 2, ROWS, L), jnp.float32),
        pltpu.VMEM((S, C, RI, T, ROWS, L), jnp.float32),
        pltpu.VMEM((S, C, RI, T, ROWS, L), jnp.float32),
        pltpu.VMEM((S, C, RI, T, ROWS, L), jnp.float32),
        pltpu.VMEM((4, 3, 3, RI, T, ROWS, L), jnp.float32),
        pltpu.VMEM((3, 3, RI, T + 1, ROWS, L), jnp.float32),
        pltpu.VMEM((3, 3, RI, T, ROWS, L), jnp.float32),
    ]
    return pl.pallas_call(
        functools.partial(hop_kernel, first),
        grid=(H,),
        in_specs=in_specs,
        out_specs=out_specs,
        out_shape=out_shape,
        scratch_shapes=scratch,
        compiler_params=pltpu.CompilerParams(dimension_semantics=("arbitrary",)),
        interpret=INTERPRET,
    )(*scalars, *noise_parts, *link_parts, *spinor_parts)


def reduce_scatter_sa(partial_value):
    n = lax.axis_size("sa")
    if n & (n - 1):
        return lax.psum_scatter(partial_value, "sa", scatter_dimension=4, tiled=True)
    lead = partial_value.shape[:-1]
    width = partial_value.shape[-1] // n
    x = jnp.moveaxis(partial_value.reshape(lead + (n, width)), -2, 0)
    me = lax.axis_index("sa")
    d = n // 2
    while d >= 1:
        upper_mine = (me // d) % 2 == 1
        keep = jnp.where(upper_mine, x[d:], x[:d])
        send = jnp.where(upper_mine, x[:d], x[d:])
        x = keep + lax.ppermute(send, "sa", [(j, j ^ d) for j in range(n)])
        d //= 2
    return x[0]


def intersection_part(rounded, vector_piece):
    products = jnp.einsum(
        "tvcazs,hqcbtgzs->hgqabtv", vector_piece, rounded, preferred_element_type=jnp.float32
    )
    products = products.reshape((-1,) + products.shape[2:])
    real_part = products[:, :, 0, 0] + products[:, :, 1, 1]
    imag_part = products[:, :, 0, 1] - products[:, :, 1, 0]
    return jnp.stack([real_part, imag_part], axis=2)


def local_body(gauge_links, noise_slabs, offsets, vectors):
    partner_vectors = from_partner(vectors, "sec", 0)
    batch_rows = noise_slabs.shape[0]
    slab_length = gauge_links.shape[4]
    Z = gauge_links.shape[5]
    K = noise_slabs.shape[3]
    section_index = lax.axis_index("sec")
    slab_index = lax.axis_index("ta")
    slab_count = lax.axis_size("ta")
    lower_sign = jnp.where(slab_index == 0, -1.0, 1.0).astype(jnp.float32)
    upper_sign = jnp.where(slab_index == slab_count - 1, -1.0, 1.0).astype(jnp.float32)
    signs = jnp.stack([lower_sign, upper_sign])
    t_start = slab_index * slab_length
    own_offsets = lax.dynamic_slice_in_dim(offsets, section_index * batch_rows, batch_rows)
    rhs_index = section_index * batch_rows + jnp.arange(batch_rows)
    spin_mask = (jnp.arange(4)[None, :] == rhs_index[:, None] % 4).astype(jnp.float32)
    times = t_start - 1 + jnp.arange(slab_length + 2)
    time_mask = (times[None, :] % TDIL == own_offsets[:, None]).astype(jnp.float32)
    scalars = (spin_mask.reshape(-1), time_mask.reshape(-1), signs)
    noise_parts = (
        noise_slabs,
        passed_along(noise_slabs[:, :, :, K - 1:], "ta", 1),
        passed_along(noise_slabs[:, :, :, :1], "ta", -1),
        passed_along(noise_slabs[:, :, :, :, Z - 1:], "sa", 1),
        passed_along(noise_slabs[:, :, :, :, :1], "sa", -1),
    )
    link_parts = (
        gauge_links,
        passed_along(gauge_links[3, :, :, :, -1:, :, :], "ta", 1),
        passed_along(gauge_links[2, :, :, :, :, -1:, :], "sa", 1),
    )
    spinor, t_first, t_last, z_first, z_last = hopping_step(True, scalars, noise_parts, link_parts, ())
    halos = (
        passed_along(t_last, "ta", 1),
        passed_along(t_first, "ta", -1),
        passed_along(z_last, "sa", 1),
        passed_along(z_first, "sa", -1),
    )
    rounded = hopping_step(False, scalars, noise_parts, link_parts, (spinor,) + halos)
    own_part = intersection_part(rounded, vectors)
    partner_part = intersection_part(rounded, partner_vectors)
    lower_half = jnp.where(section_index == 0, own_part, partner_part)
    upper_half = jnp.where(section_index == 0, partner_part, own_part)
    partial_value = jnp.concatenate([lower_half, upper_half], axis=4)
    return reduce_scatter_sa(partial_value)


def solution(mesh):
    in_specs = (
        P(None, None, None, None, "ta", "sa", None),
        P("sec", None, None, "ta", "sa", None),
        P(),
        P("ta", "sec", None, None, "sa", None),
    )
    out_specs = P("sec", None, None, "ta", "sa")
    return jax.shard_map(local_body, mesh=mesh, in_specs=in_specs, out_specs=out_specs, check_vma=False)
```

```python
import functools

import jax
import jax.numpy as jnp
from jax import lax
from jax.experimental import pallas as pl
from jax.experimental.pallas import tpu as pltpu
from jax.sharding import PartitionSpec as P


NX = 32
TDIL = 4
INTERPRET = False


kappa_hop = 0.12
GAMMA_PERM = ((3, 2, 1, 0), (3, 2, 1, 0), (2, 3, 0, 1), (2, 3, 0, 1))
GAMMA_REAL = ((0, 0, 0, 0), (-1, 1, 1, -1), (0, 0, 0, 0), (1, 1, 1, 1))
GAMMA_IMAG = ((1, 1, -1, -1), (0, 0, 0, 0), (1, -1, -1, 1), (0, 0, 0, 0))


def passed_along(value, axis, steps):
    count = lax.axis_size(axis)
    pairs = [(source, (source + steps) % count) for source in range(count)]
    return lax.ppermute(value, axis, pairs)


def from_partner(x, axis, stride):
    return lax.ppermute(x, axis, [(i, i ^ 1 << stride) for i in range(lax.axis_size(axis))])


def times_phase(re, im, cr, ci):
    if ci == 0:
        if cr == 1:
            return re, im
        return -re, -im
    if ci == 1:
        return -im, re
    return im, -re


def hop_kernel(first, *refs):
    (smask_ref, tmask_ref, sign_ref, noise_ref, ntlo_ref, nthi_ref, nzlo_ref, nzhi_ref,
     u_ref, utedge_ref, uzedge_ref) = refs[:11]
    rest = refs[11:]
    if first:
        out_ref, tfirst_ref, tlast_ref, zfirst_ref, zlast_ref = rest[:5]
        scratch = rest[5:]
    else:
        psi_ref, tlo_ref, thi_ref, zlo_ref, zhi_ref = rest[:5]
        out_ref = rest[5]
        scratch = rest[6:]
    pad_ref, src_ref, zlo_s, zhi_s, u8, ut8, uz8, acc_ref = scratch
    S, C, RI, T, ROWS, L = src_ref.shape
    Z = ROWS // 2
    K = noise_ref.shape[3]
    span = T // K
    h = pl.program_id(0)
    lower = pl.ds(0, Z)
    upper = pl.ds(Z, Z)

    @pl.when(h == 0)
    def _():
        for a in range(3):
            for b in range(3):
                for ri in range(RI):
                    for half in (lower, upper):
                        ut8[a, b, ri, pl.ds(0, 1), half] = utedge_ref[a, b, ri]
                        ut8[a, b, ri, pl.ds(1, T), half] = u_ref[3, a, b, ri]
                        for t in range(T):
                            uz8[a, b, ri, t, half] = jnp.broadcast_to(uzedge_ref[a, b, ri, t], (Z, L))
                        for mu in range(4):
                            u8[mu, a, b, ri, :, half] = u_ref[mu, a, b, ri]

    for s in range(S):
        for c in range(C):
            for ri in range(RI):
                for g, half in ((0, lower), (1, upper)):
                    r = 2 * h + g
                    fs = smask_ref[r * S + s]
                    for t in range(T):
                        src_ref[s, c, ri, t, half] = noise_ref[g, c, ri, t // span] * (
                            fs * tmask_ref[r * (T + 2) + t + 1])
                    if first:
                        pad_ref[s, c, ri, 0, half] = ntlo_ref[g, c, ri, 0] * (
                            fs * tmask_ref[r * (T + 2)] * sign_ref[0])
                        pad_ref[s, c, ri, T + 1, half] = nthi_ref[g, c, ri, 0] * (
                            fs * tmask_ref[r * (T + 2) + T + 1] * sign_ref[1])
                        for t in range(T):
                            f = fs * tmask_ref[r * (T + 2) + t + 1]
                            zlo_s[s, c, ri, t, half] = jnp.broadcast_to(nzlo_ref[g, c, ri, t // span] * f, (Z, L))
                            zhi_s[s, c, ri, t, half] = jnp.broadcast_to(nzhi_ref[g, c, ri, t // span] * f, (Z, L))
                    else:
                        for t in range(T):
                            if s < 2:
                                zlo_s[s, c, ri, t, half] = jnp.broadcast_to(zlo_ref[s, c, ri, t, pl.ds(g, 1)], (Z, L))
                                zhi_s[s, c, ri, t, half] = jnp.broadcast_to(zhi_ref[s, c, ri, t, pl.ds(g, 1)], (Z, L))
                            else:
                                zlo_s[s, c, ri, t, half] = jnp.zeros((Z, L), jnp.float32)
                                zhi_s[s, c, ri, t, half] = jnp.zeros((Z, L), jnp.float32)
                if first:
                    pad_ref[s, c, ri, pl.ds(1, T)] = src_ref[s, c, ri]
                else:
                    pad_ref[s, c, ri, pl.ds(1, T)] = psi_ref[s, c, ri]
                    if s < 2:
                        pad_ref[s, c, ri, pl.ds(0, 1)] = tlo_ref[s, c, ri].astype(jnp.float32) * sign_ref[0]
                        pad_ref[s, c, ri, pl.ds(T + 1, 1)] = thi_ref[s, c, ri].astype(jnp.float32) * sign_ref[1]
                    else:
                        pad_ref[s, c, ri, pl.ds(0, 1)] = jnp.zeros((1, ROWS, L), jnp.float32)
                        pad_ref[s, c, ri, pl.ds(T + 1, 1)] = jnp.zeros((1, ROWS, L), jnp.float32)
    xpos = lax.broadcasted_iota(jnp.int32, (ROWS, L), 1) % NX
    zpos = lax.broadcasted_iota(jnp.int32, (ROWS, L), 0) % Z
    x_last = xpos == NX - 1
    x_first = xpos == 0
    z_last = zpos == Z - 1
    z_first = zpos == 0

    def x_back(v):
        return jnp.where(x_first, pltpu.roll(v, L - NX + 1, axis=1), pltpu.roll(v, 1, axis=1))

    def body(t, carry):
        started = [[[False, False] for _ in range(3)] for _ in range(4)]

        def accumulate(row, a, ri, value):
            if started[row][a][ri]:
                acc_ref[row, a, ri] = acc_ref[row, a, ri] + value
            else:
                acc_ref[row, a, ri] = value
                started[row][a][ri] = True

        def shifted(s, c, ri, mu, stride):
            if mu == 3:
                return pad_ref[s, c, ri, t + 1 + stride]
            v = pad_ref[s, c, ri, t + 1]
            if mu == 2:
                if stride == 1:
                    return jnp.where(z_last, zhi_s[s, c, ri, t], pltpu.roll(v, ROWS - 1, axis=0))
                return jnp.where(z_first, zlo_s[s, c, ri, t], pltpu.roll(v, 1, axis=0))
            if mu == 1:
                return pltpu.roll(v, (L - NX) if stride == 1 else NX, axis=1)
            if stride == 1:
                return jnp.where(x_last, pltpu.roll(v, NX - 1, axis=1), pltpu.roll(v, L - 1, axis=1))
            return x_back(v)

        def back_link(mu, a, b, ri):
            if mu == 3:
                return ut8[a, b, ri, t]
            v = u8[mu, a, b, ri, t]
            if mu == 2:
                return jnp.where(z_first, uz8[a, b, ri, t], pltpu.roll(v, 1, axis=0))
            if mu == 1:
                return pltpu.roll(v, NX, axis=1)
            return x_back(v)

        for mu in range(4):
            perm = GAMMA_PERM[mu]
            heads = [0, 1]
            for stride in (1, -1):
                orient = -1 if stride == 1 else 1
                half = []
                for s in heads:
                    p = perm[s]
                    cr, ci = orient * GAMMA_REAL[mu][s], orient * GAMMA_IMAG[mu][s]
                    colours = []
                    for c in range(3):
                        sre = shifted(s, c, 0, mu, stride)
                        sim = shifted(s, c, 1, mu, stride)
                        pre, pim = times_phase(shifted(p, c, 0, mu, stride), shifted(p, c, 1, mu, stride), cr, ci)
                        colours.append((sre + pre, sim + pim))
                    half.append(colours)
                if stride == 1:
                    links = [[(u8[mu, a, b, 0, t], u8[mu, a, b, 1, t]) for b in range(3)] for a in range(3)]
                else:
                    links = [[(back_link(mu, b, a, 0), back_link(mu, b, a, 1)) for b in range(3)] for a in range(3)]
                for k, s in enumerate(heads):
                    p = perm[s]
                    cpr, cpi = orient * GAMMA_REAL[mu][p], orient * GAMMA_IMAG[mu][p]
                    for a in range(3):
                        sum_re = None
                        sum_im = None
                        for b in range(3):
                            hre, him = half[k][b]
                            lre, lim = links[a][b]
                            if stride == 1:
                                tre = lre * hre - lim * him
                                tim = lre * him + lim * hre
                            else:
                                tre = lre * hre + lim * him
                                tim = lre * him - lim * hre
                            sum_re = tre if sum_re is None else sum_re + tre
                            sum_im = tim if sum_im is None else sum_im + tim
                        for row, (vre, vim) in ((s, (sum_re, sum_im)), (p, times_phase(sum_re, sum_im, cpr, cpi))):
                            accumulate(row, a, 0, vre)
                            accumulate(row, a, 1, vim)
        for s in range(4):
            for c in range(3):
                for ri in range(2):
                    psi = pad_ref[s, c, ri, t + 1]
                    src = src_ref[s, c, ri, t]
                    residual = src - (psi - kappa_hop * acc_ref[s, c, ri])
                    value = psi + residual
                    if first:
                        out_ref[s, c, ri, t] = value
                    else:
                        for g in range(2):
                            out_ref[s, c, ri, t, g] = value[g * Z:(g + 1) * Z].astype(out_ref.dtype)
        return carry

    lax.fori_loop(0, T, body, 0)
    if first:
        for mu, stride, target, pick in (
            (3, 1, tfirst_ref, lambda s, c, ri: out_ref[s, c, ri, pl.ds(0, 1)]),
            (3, -1, tlast_ref, lambda s, c, ri: out_ref[s, c, ri, pl.ds(T - 1, 1)]),
        ):
            for k, (re, im) in enumerate(half_spinor(pick, mu, stride)):
                for c in range(C):
                    target[k, c, 0] = re[c].astype(target.dtype)
                    target[k, c, 1] = im[c].astype(target.dtype)
        for g in range(2):
            for mu, stride, target, row in ((2, 1, zfirst_ref, g * Z), (2, -1, zlast_ref, g * Z + Z - 1)):
                pick = lambda s, c, ri: out_ref[s, c, ri, :, pl.ds(row, 1), :]
                for k, (re, im) in enumerate(half_spinor(pick, mu, stride)):
                    for c in range(C):
                        target[k, c, 0, :, pl.ds(g, 1), :] = re[c]
                        target[k, c, 1, :, pl.ds(g, 1), :] = im[c]


def half_spinor(pick, mu, stride):
    orient = -1 if stride == 1 else 1
    rows = []
    for s in (0, 1):
        p = GAMMA_PERM[mu][s]
        cr, ci = orient * GAMMA_REAL[mu][s], orient * GAMMA_IMAG[mu][s]
        res, ims = [], []
        for c in range(3):
            pre, pim = times_phase(pick(p, c, 0), pick(p, c, 1), cr, ci)
            res.append(pick(s, c, 0) + pre)
            ims.append(pick(s, c, 1) + pim)
        rows.append((res, ims))
    return rows


def hopping_step(first, scalars, noise_parts, link_parts, spinor_parts):
    R, C, RI, K, Z, L = noise_parts[0].shape
    T = link_parts[0].shape[4]
    S = 4
    H = R // 2
    ROWS = 2 * Z
    index = lambda h: (h,) + (0,) * 6
    index6 = lambda h: (h,) + (0,) * 5
    whole = lambda x: pl.BlockSpec(x.shape, lambda h: (0,) * x.ndim)
    smem = pl.BlockSpec(memory_space=pltpu.SMEM)
    site_block = pl.BlockSpec((None, S, C, RI, T, ROWS, L), index)
    t_block = pl.BlockSpec((None, 2, C, RI, 1, ROWS, L), index)
    z_block = pl.BlockSpec((None, 2, C, RI, T, 2, L), index)
    noise_specs = [
        pl.BlockSpec((2, C, RI, K, Z, L), index6),
        pl.BlockSpec((2, C, RI, 1, Z, L), index6),
        pl.BlockSpec((2, C, RI, 1, Z, L), index6),
        pl.BlockSpec((2, C, RI, K, 1, L), index6),
        pl.BlockSpec((2, C, RI, K, 1, L), index6),
    ]
    in_specs = [smem, smem, smem] + noise_specs + [whole(x) for x in link_parts]
    site_shape = (H, S, C, RI, T, ROWS, L)
    if first:
        t_shape = jax.ShapeDtypeStruct((H, 2, C, RI, 1, ROWS, L), jnp.bfloat16)
        z_shape = jax.ShapeDtypeStruct((H, 2, C, RI, T, 2, L), jnp.float32)
        out_shape = [jax.ShapeDtypeStruct(site_shape, jnp.float32), t_shape, t_shape, z_shape, z_shape]
        out_specs = [site_block, t_block, t_block, z_block, z_block]
    else:
        in_specs += [site_block, t_block, t_block, z_block, z_block]
        out_shape = jax.ShapeDtypeStruct((H, S, C, RI, T, 2, Z, L), jnp.bfloat16)
        out_specs = pl.BlockSpec((None, S, C, RI, T, 2, Z, L), lambda h: (h,) + (0,) * 7)
    scratch = [
        pltpu.VMEM((S, C, RI, T + 2, ROWS, L), jnp.float32),
        pltpu.VMEM((S, C, RI, T, ROWS, L), jnp.float32),
        pltpu.VMEM((S, C, RI, T, ROWS, L), jnp.float32),
        pltpu.VMEM((S, C, RI, T, ROWS, L), jnp.float32),
        pltpu.VMEM((4, 3, 3, RI, T, ROWS, L), jnp.float32),
        pltpu.VMEM((3, 3, RI, T + 1, ROWS, L), jnp.float32),
        pltpu.VMEM((3, 3, RI, T, ROWS, L), jnp.float32),
        pltpu.VMEM((S, C, RI, ROWS, L), jnp.float32),
    ]
    return pl.pallas_call(
        functools.partial(hop_kernel, first),
        grid=(H,),
        in_specs=in_specs,
        out_specs=out_specs,
        out_shape=out_shape,
        scratch_shapes=scratch,
        compiler_params=pltpu.CompilerParams(dimension_semantics=("arbitrary",)),
        interpret=INTERPRET,
    )(*scalars, *noise_parts, *link_parts, *spinor_parts)


def reduce_scatter_sa(partial_value):
    n = lax.axis_size("sa")
    if n & (n - 1):
        return lax.psum_scatter(partial_value, "sa", scatter_dimension=4, tiled=True)
    lead = partial_value.shape[:-1]
    width = partial_value.shape[-1] // n
    x = jnp.moveaxis(partial_value.reshape(lead + (n, width)), -2, 0)
    me = lax.axis_index("sa")
    d = 1
    while d < n:
        x = x.reshape((x.shape[0] // 2, 2) + x.shape[1:])
        odd = (me // d) % 2 == 1
        keep = jnp.where(odd, x[:, 1], x[:, 0])
        send = jnp.where(odd, x[:, 0], x[:, 1])
        x = keep + lax.ppermute(send, "sa", [(j, j ^ d) for j in range(n)])
        d *= 2
    return x[0]


def intersection_part(rounded, vector_piece):
    products = jnp.einsum(
        "tvcazs,hqcbtgzs->hgqabtv", vector_piece, rounded, preferred_element_type=jnp.float32
    )
    products = products.reshape((-1,) + products.shape[2:])
    real_part = products[:, :, 0, 0] + products[:, :, 1, 1]
    imag_part = products[:, :, 0, 1] - products[:, :, 1, 0]
    return jnp.stack([real_part, imag_part], axis=2)


def local_body(gauge_links, noise_slabs, offsets, vectors):
    partner_vectors = from_partner(vectors, "sec", 0)
    batch_rows = noise_slabs.shape[0]
    slab_length = gauge_links.shape[4]
    Z = gauge_links.shape[5]
    K = noise_slabs.shape[3]
    section_index = lax.axis_index("sec")
    slab_index = lax.axis_index("ta")
    slab_count = lax.axis_size("ta")
    lower_sign = jnp.where(slab_index == 0, -1.0, 1.0).astype(jnp.float32)
    upper_sign = jnp.where(slab_index == slab_count - 1, -1.0, 1.0).astype(jnp.float32)
    signs = jnp.stack([lower_sign, upper_sign])
    t_start = slab_index * slab_length
    own_offsets = lax.dynamic_slice_in_dim(offsets, section_index * batch_rows, batch_rows)
    rhs_index = section_index * batch_rows + jnp.arange(batch_rows)
    spin_mask = (jnp.arange(4)[None, :] == rhs_index[:, None] % 4).astype(jnp.float32)
    times = t_start - 1 + jnp.arange(slab_length + 2)
    time_mask = (times[None, :] % TDIL == own_offsets[:, None]).astype(jnp.float32)
    scalars = (spin_mask.reshape(-1), time_mask.reshape(-1), signs)
    noise_parts = (
        noise_slabs,
        passed_along(noise_slabs[:, :, :, K - 1:], "ta", 1),
        passed_along(noise_slabs[:, :, :, :1], "ta", -1),
        passed_along(noise_slabs[:, :, :, :, Z - 1:], "sa", 1),
        passed_along(noise_slabs[:, :, :, :, :1], "sa", -1),
    )
    link_parts = (
        gauge_links,
        passed_along(gauge_links[3, :, :, :, -1:, :, :], "ta", 1),
        passed_along(gauge_links[2, :, :, :, :, -1:, :], "sa", 1),
    )
    spinor, t_first, t_last, z_first, z_last = hopping_step(True, scalars, noise_parts, link_parts, ())
    halos = (
        passed_along(t_last, "ta", 1),
        passed_along(t_first, "ta", -1),
        passed_along(z_last, "sa", 1),
        passed_along(z_first, "sa", -1),
    )
    rounded = hopping_step(False, scalars, noise_parts, link_parts, (spinor,) + halos)
    own_part = intersection_part(rounded, vectors)
    partner_part = intersection_part(rounded, partner_vectors)
    lower_half = jnp.where(section_index == 0, own_part, partner_part)
    upper_half = jnp.where(section_index == 0, partner_part, own_part)
    partial_value = jnp.concatenate([lower_half, upper_half], axis=4)
    return reduce_scatter_sa(partial_value)


def solution(mesh):
    in_specs = (
        P(None, None, None, None, "ta", "sa", None),
        P("sec", None, None, "ta", "sa", None),
        P(),
        P("ta", "sec", None, None, "sa", None),
    )
    out_specs = P("sec", None, None, "ta", "sa")
    return jax.shard_map(local_body, mesh=mesh, in_specs=in_specs, out_specs=out_specs, check_vma=False)
```

```python
import functools

import jax
import jax.numpy as jnp
from jax import lax
from jax.experimental import pallas as pl
from jax.experimental.pallas import tpu as pltpu
from jax.sharding import PartitionSpec as P


NX = 32
TDIL = 4
INTERPRET = False


kappa_hop = 0.12
GAMMA_PERM = ((3, 2, 1, 0), (3, 2, 1, 0), (2, 3, 0, 1), (2, 3, 0, 1))
GAMMA_REAL = ((0, 0, 0, 0), (-1, 1, 1, -1), (0, 0, 0, 0), (1, 1, 1, 1))
GAMMA_IMAG = ((1, 1, -1, -1), (0, 0, 0, 0), (1, -1, -1, 1), (0, 0, 0, 0))


def passed_along(value, axis, steps):
    count = lax.axis_size(axis)
    pairs = [(source, (source + steps) % count) for source in range(count)]
    return lax.ppermute(value, axis, pairs)


def from_partner(x, axis, stride):
    return lax.ppermute(x, axis, [(i, i ^ 1 << stride) for i in range(lax.axis_size(axis))])


def times_phase(re, im, cr, ci):
    if ci == 0:
        if cr == 1:
            return re, im
        return -re, -im
    if ci == 1:
        return -im, re
    return im, -re


def hop_kernel(first, *refs):
    (scal_ref, noise_ref, ntlo_ref, nthi_ref, nzlo_ref, nzhi_ref, u_ref, utedge_ref, uzedge_ref) = refs[:9]
    rest = refs[9:]
    if first:
        out_ref, tfirst_ref, tlast_ref, zfirst_ref, zlast_ref = rest[:5]
        scratch = rest[5:]
    else:
        psi_ref, tlo_ref, thi_ref, zlo_ref, zhi_ref = rest[:5]
        out_ref = rest[5]
        scratch = rest[6:]
    pad_ref, src_ref, zlo_s, zhi_s, u8, ut8, uz8 = scratch
    S, C, RI, T, ROWS, L = src_ref.shape
    Z = ROWS // 2
    K = noise_ref.shape[3]
    span = T // K
    h = pl.program_id(0)
    R = 2 * pl.num_programs(0)
    smask = lambda i: scal_ref[i]
    tmask = lambda i: scal_ref[R * S + i]
    sign = lambda i: scal_ref[R * S + R * (T + 2) + i]
    lower = pl.ds(0, Z)
    upper = pl.ds(Z, Z)

    @pl.when(h == 0)
    def _():
        for a in range(3):
            for b in range(3):
                for ri in range(RI):
                    for half in (lower, upper):
                        ut8[a, b, ri, pl.ds(0, 1), half] = utedge_ref[a, b, ri]
                        ut8[a, b, ri, pl.ds(1, T), half] = u_ref[3, a, b, ri]
                        for t in range(T):
                            uz8[a, b, ri, t, half] = jnp.broadcast_to(uzedge_ref[a, b, ri, t], (Z, L))
                        for mu in range(4):
                            u8[mu, a, b, ri, :, half] = u_ref[mu, a, b, ri]

    for s in range(S):
        for c in range(C):
            for ri in range(RI):
                for g, half in ((0, lower), (1, upper)):
                    r = 2 * h + g
                    fs = smask(r * S + s)
                    for t in range(T):
                        src_ref[s, c, ri, t, half] = noise_ref[g, c, ri, t // span] * (
                            fs * tmask(r * (T + 2) + t + 1))
                    if first:
                        pad_ref[s, c, ri, 0, half] = ntlo_ref[g, c, ri, 0] * (
                            fs * tmask(r * (T + 2)) * sign(0))
                        pad_ref[s, c, ri, T + 1, half] = nthi_ref[g, c, ri, 0] * (
                            fs * tmask(r * (T + 2) + T + 1) * sign(1))
                        for t in range(T):
                            f = fs * tmask(r * (T + 2) + t + 1)
                            zlo_s[s, c, ri, t, half] = jnp.broadcast_to(nzlo_ref[g, c, ri, t // span] * f, (Z, L))
                            zhi_s[s, c, ri, t, half] = jnp.broadcast_to(nzhi_ref[g, c, ri, t // span] * f, (Z, L))
                    else:
                        for t in range(T):
                            if s < 2:
                                zlo_s[s, c, ri, t, half] = jnp.broadcast_to(zlo_ref[s, c, ri, t, pl.ds(g, 1)], (Z, L))
                                zhi_s[s, c, ri, t, half] = jnp.broadcast_to(zhi_ref[s, c, ri, t, pl.ds(g, 1)], (Z, L))
                            else:
                                zlo_s[s, c, ri, t, half] = jnp.zeros((Z, L), jnp.float32)
                                zhi_s[s, c, ri, t, half] = jnp.zeros((Z, L), jnp.float32)
                if first:
                    pad_ref[s, c, ri, pl.ds(1, T)] = src_ref[s, c, ri]
                else:
                    pad_ref[s, c, ri, pl.ds(1, T)] = psi_ref[s, c, ri]
                    if s < 2:
                        pad_ref[s, c, ri, pl.ds(0, 1)] = tlo_ref[s, c, ri].astype(jnp.float32) * sign(0)
                        pad_ref[s, c, ri, pl.ds(T + 1, 1)] = thi_ref[s, c, ri].astype(jnp.float32) * sign(1)
                    else:
                        pad_ref[s, c, ri, pl.ds(0, 1)] = jnp.zeros((1, ROWS, L), jnp.float32)
                        pad_ref[s, c, ri, pl.ds(T + 1, 1)] = jnp.zeros((1, ROWS, L), jnp.float32)
    xpos = lax.broadcasted_iota(jnp.int32, (ROWS, L), 1) % NX
    zpos = lax.broadcasted_iota(jnp.int32, (ROWS, L), 0) % Z
    x_last = xpos == NX - 1
    x_first = xpos == 0
    z_last = zpos == Z - 1
    z_first = zpos == 0

    def x_back(v):
        return jnp.where(x_first, pltpu.roll(v, L - NX + 1, axis=1), pltpu.roll(v, 1, axis=1))

    def body(t, carry):
        acc = [[[None, None] for _ in range(3)] for _ in range(4)]

        def shifted(s, c, ri, mu, stride):
            if mu == 3:
                return pad_ref[s, c, ri, t + 1 + stride]
            v = pad_ref[s, c, ri, t + 1]
            if mu == 2:
                if stride == 1:
                    return jnp.where(z_last, zhi_s[s, c, ri, t], pltpu.roll(v, ROWS - 1, axis=0))
                return jnp.where(z_first, zlo_s[s, c, ri, t], pltpu.roll(v, 1, axis=0))
            if mu == 1:
                return pltpu.roll(v, (L - NX) if stride == 1 else NX, axis=1)
            if stride == 1:
                return jnp.where(x_last, pltpu.roll(v, NX - 1, axis=1), pltpu.roll(v, L - 1, axis=1))
            return x_back(v)

        def back_link(mu, a, b, ri):
            if mu == 3:
                return ut8[a, b, ri, t]
            v = u8[mu, a, b, ri, t]
            if mu == 2:
                return jnp.where(z_first, uz8[a, b, ri, t], pltpu.roll(v, 1, axis=0))
            if mu == 1:
                return pltpu.roll(v, NX, axis=1)
            return x_back(v)

        for mu in range(4):
            perm = GAMMA_PERM[mu]
            heads = [0, 1]
            for stride in (1, -1):
                orient = -1 if stride == 1 else 1
                half = []
                for s in heads:
                    p = perm[s]
                    cr, ci = orient * GAMMA_REAL[mu][s], orient * GAMMA_IMAG[mu][s]
                    colours = []
                    for c in range(3):
                        sre = shifted(s, c, 0, mu, stride)
                        sim = shifted(s, c, 1, mu, stride)
                        pre, pim = times_phase(shifted(p, c, 0, mu, stride), shifted(p, c, 1, mu, stride), cr, ci)
                        colours.append((sre + pre, sim + pim))
                    half.append(colours)
                if stride == 1:
                    links = [[(u8[mu, a, b, 0, t], u8[mu, a, b, 1, t]) for b in range(3)] for a in range(3)]
                else:
                    links = [[(back_link(mu, b, a, 0), back_link(mu, b, a, 1)) for b in range(3)] for a in range(3)]
                for k, s in enumerate(heads):
                    p = perm[s]
                    cpr, cpi = orient * GAMMA_REAL[mu][p], orient * GAMMA_IMAG[mu][p]
                    for a in range(3):
                        sum_re = None
                        sum_im = None
                        for b in range(3):
                            hre, him = half[k][b]
                            lre, lim = links[a][b]
                            if stride == 1:
                                tre = lre * hre - lim * him
                                tim = lre * him + lim * hre
                            else:
                                tre = lre * hre + lim * him
                                tim = lre * him - lim * hre
                            sum_re = tre if sum_re is None else sum_re + tre
                            sum_im = tim if sum_im is None else sum_im + tim
                        for row, (vre, vim) in ((s, (sum_re, sum_im)), (p, times_phase(sum_re, sum_im, cpr, cpi))):
                            if acc[row][a][0] is None:
                                acc[row][a] = [vre, vim]
                            else:
                                acc[row][a] = [acc[row][a][0] + vre, acc[row][a][1] + vim]
        for s in range(4):
            for c in range(3):
                for ri in range(2):
                    psi = pad_ref[s, c, ri, t + 1]
                    src = src_ref[s, c, ri, t]
                    residual = src - (psi - kappa_hop * acc[s][c][ri])
                    value = psi + residual
                    if first:
                        out_ref[s, c, ri, t] = value
                    else:
                        for g in range(2):
                            out_ref[s, c, ri, t, g] = value[g * Z:(g + 1) * Z].astype(out_ref.dtype)
        return carry

    lax.fori_loop(0, T, body, 0)
    if first:
        for mu, stride, target, pick in (
            (3, 1, tfirst_ref, lambda s, c, ri: out_ref[s, c, ri, pl.ds(0, 1)]),
            (3, -1, tlast_ref, lambda s, c, ri: out_ref[s, c, ri, pl.ds(T - 1, 1)]),
        ):
            for k, (re, im) in enumerate(half_spinor(pick, mu, stride)):
                for c in range(C):
                    target[k, c, 0] = re[c].astype(target.dtype)
                    target[k, c, 1] = im[c].astype(target.dtype)
        for g in range(2):
            for mu, stride, target, row in ((2, 1, zfirst_ref, g * Z), (2, -1, zlast_ref, g * Z + Z - 1)):
                pick = lambda s, c, ri: out_ref[s, c, ri, :, pl.ds(row, 1), :]
                for k, (re, im) in enumerate(half_spinor(pick, mu, stride)):
                    for c in range(C):
                        target[k, c, 0, :, pl.ds(g, 1), :] = re[c]
                        target[k, c, 1, :, pl.ds(g, 1), :] = im[c]


def half_spinor(pick, mu, stride):
    orient = -1 if stride == 1 else 1
    rows = []
    for s in (0, 1):
        p = GAMMA_PERM[mu][s]
        cr, ci = orient * GAMMA_REAL[mu][s], orient * GAMMA_IMAG[mu][s]
        res, ims = [], []
        for c in range(3):
            pre, pim = times_phase(pick(p, c, 0), pick(p, c, 1), cr, ci)
            res.append(pick(s, c, 0) + pre)
            ims.append(pick(s, c, 1) + pim)
        rows.append((res, ims))
    return rows


def hopping_step(first, scalars, noise_parts, link_parts, spinor_parts):
    R, C, RI, K, Z, L = noise_parts[0].shape
    T = link_parts[0].shape[4]
    S = 4
    H = R // 2
    ROWS = 2 * Z
    index = lambda h: (h,) + (0,) * 6
    index6 = lambda h: (h,) + (0,) * 5
    whole = lambda x: pl.BlockSpec(x.shape, lambda h: (0,) * x.ndim)
    smem = pl.BlockSpec(memory_space=pltpu.SMEM)
    site_block = pl.BlockSpec((None, S, C, RI, T, ROWS, L), index)
    t_block = pl.BlockSpec((None, 2, C, RI, 1, ROWS, L), index)
    z_block = pl.BlockSpec((None, 2, C, RI, T, 2, L), index)
    noise_specs = [
        pl.BlockSpec((2, C, RI, K, Z, L), index6),
        pl.BlockSpec((2, C, RI, 1, Z, L), index6),
        pl.BlockSpec((2, C, RI, 1, Z, L), index6),
        pl.BlockSpec((2, C, RI, K, 1, L), index6),
        pl.BlockSpec((2, C, RI, K, 1, L), index6),
    ]
    in_specs = [smem] + noise_specs + [whole(x) for x in link_parts]
    site_shape = (H, S, C, RI, T, ROWS, L)
    if first:
        t_shape = jax.ShapeDtypeStruct((H, 2, C, RI, 1, ROWS, L), jnp.bfloat16)
        z_shape = jax.ShapeDtypeStruct((H, 2, C, RI, T, 2, L), jnp.float32)
        out_shape = [jax.ShapeDtypeStruct(site_shape, jnp.float32), t_shape, t_shape, z_shape, z_shape]
        out_specs = [site_block, t_block, t_block, z_block, z_block]
    else:
        in_specs += [site_block, t_block, t_block, z_block, z_block]
        out_shape = jax.ShapeDtypeStruct((H, S, C, RI, T, 2, Z, L), jnp.bfloat16)
        out_specs = pl.BlockSpec((None, S, C, RI, T, 2, Z, L), lambda h: (h,) + (0,) * 7)
    scratch = [
        pltpu.VMEM((S, C, RI, T + 2, ROWS, L), jnp.float32),
        pltpu.VMEM((S, C, RI, T, ROWS, L), jnp.float32),
        pltpu.VMEM((S, C, RI, T, ROWS, L), jnp.float32),
        pltpu.VMEM((S, C, RI, T, ROWS, L), jnp.float32),
        pltpu.VMEM((4, 3, 3, RI, T, ROWS, L), jnp.float32),
        pltpu.VMEM((3, 3, RI, T + 1, ROWS, L), jnp.float32),
        pltpu.VMEM((3, 3, RI, T, ROWS, L), jnp.float32),
    ]
    return pl.pallas_call(
        functools.partial(hop_kernel, first),
        grid=(H,),
        in_specs=in_specs,
        out_specs=out_specs,
        out_shape=out_shape,
        scratch_shapes=scratch,
        compiler_params=pltpu.CompilerParams(dimension_semantics=("arbitrary",)),
        interpret=INTERPRET,
    )(*scalars, *noise_parts, *link_parts, *spinor_parts)


def reduce_scatter_sa(partial_value):
    n = lax.axis_size("sa")
    if n & (n - 1):
        return lax.psum_scatter(partial_value, "sa", scatter_dimension=4, tiled=True)
    lead = partial_value.shape[:-1]
    width = partial_value.shape[-1] // n
    x = jnp.moveaxis(partial_value.reshape(lead + (n, width)), -2, 0)
    me = lax.axis_index("sa")
    d = 1
    while d < n:
        x = x.reshape((x.shape[0] // 2, 2) + x.shape[1:])
        odd = (me // d) % 2 == 1
        keep = jnp.where(odd, x[:, 1], x[:, 0])
        send = jnp.where(odd, x[:, 0], x[:, 1])
        x = keep + lax.ppermute(send, "sa", [(j, j ^ d) for j in range(n)])
        d *= 2
    return x[0]


def intersection_part(rounded, vector_piece):
    products = jnp.einsum(
        "tvcazs,hqcbtgzs->hgqabtv", vector_piece, rounded, preferred_element_type=jnp.float32
    )
    products = products.reshape((-1,) + products.shape[2:])
    real_part = products[:, :, 0, 0] + products[:, :, 1, 1]
    imag_part = products[:, :, 0, 1] - products[:, :, 1, 0]
    return jnp.stack([real_part, imag_part], axis=2)


def local_body(gauge_links, noise_slabs, offsets, vectors):
    partner_vectors = from_partner(vectors, "sec", 0)
    batch_rows = noise_slabs.shape[0]
    slab_length = gauge_links.shape[4]
    Z = gauge_links.shape[5]
    K = noise_slabs.shape[3]
    section_index = lax.axis_index("sec")
    slab_index = lax.axis_index("ta")
    slab_count = lax.axis_size("ta")
    lower_sign = jnp.where(slab_index == 0, -1.0, 1.0).astype(jnp.float32)
    upper_sign = jnp.where(slab_index == slab_count - 1, -1.0, 1.0).astype(jnp.float32)
    signs = jnp.stack([lower_sign, upper_sign])
    t_start = slab_index * slab_length
    own_offsets = lax.dynamic_slice_in_dim(offsets, section_index * batch_rows, batch_rows)
    rhs_index = section_index * batch_rows + jnp.arange(batch_rows)
    spin_mask = (jnp.arange(4)[None, :] == rhs_index[:, None] % 4).astype(jnp.float32)
    times = t_start - 1 + jnp.arange(slab_length + 2)
    time_mask = (times[None, :] % TDIL == own_offsets[:, None]).astype(jnp.float32)
    scalars = (jnp.concatenate([spin_mask.reshape(-1), time_mask.reshape(-1), signs]),)
    noise_parts = (
        noise_slabs,
        passed_along(noise_slabs[:, :, :, K - 1:], "ta", 1),
        passed_along(noise_slabs[:, :, :, :1], "ta", -1),
        passed_along(noise_slabs[:, :, :, :, Z - 1:], "sa", 1),
        passed_along(noise_slabs[:, :, :, :, :1], "sa", -1),
    )
    link_parts = (
        gauge_links,
        passed_along(gauge_links[3, :, :, :, -1:, :, :], "ta", 1),
        passed_along(gauge_links[2, :, :, :, :, -1:, :], "sa", 1),
    )
    spinor, t_first, t_last, z_first, z_last = hopping_step(True, scalars, noise_parts, link_parts, ())
    halos = (
        passed_along(t_last, "ta", 1),
        passed_along(t_first, "ta", -1),
        passed_along(z_last, "sa", 1),
        passed_along(z_first, "sa", -1),
    )
    rounded = hopping_step(False, scalars, noise_parts, link_parts, (spinor,) + halos)
    own_part = intersection_part(rounded, vectors)
    partner_part = intersection_part(rounded, partner_vectors)
    lower_half = jnp.where(section_index == 0, own_part, partner_part)
    upper_half = jnp.where(section_index == 0, partner_part, own_part)
    partial_value = jnp.concatenate([lower_half, upper_half], axis=4)
    return reduce_scatter_sa(partial_value)


def solution(mesh):
    in_specs = (
        P(None, None, None, None, "ta", "sa", None),
        P("sec", None, None, "ta", "sa", None),
        P(),
        P("ta", "sec", None, None, "sa", None),
    )
    out_specs = P("sec", None, None, "ta", "sa")
    return jax.shard_map(local_body, mesh=mesh, in_specs=in_specs, out_specs=out_specs, check_vma=False)
```

```python
import functools

import jax
import jax.numpy as jnp
from jax import lax
from jax.experimental import pallas as pl
from jax.experimental.pallas import tpu as pltpu
from jax.sharding import PartitionSpec as P


NX = 32
TDIL = 4
INTERPRET = False


kappa_hop = 0.12
GAMMA_PERM = ((3, 2, 1, 0), (3, 2, 1, 0), (2, 3, 0, 1), (2, 3, 0, 1))
GAMMA_REAL = ((0, 0, 0, 0), (-1, 1, 1, -1), (0, 0, 0, 0), (1, 1, 1, 1))
GAMMA_IMAG = ((1, 1, -1, -1), (0, 0, 0, 0), (1, -1, -1, 1), (0, 0, 0, 0))


def passed_along(value, axis, steps):
    count = lax.axis_size(axis)
    pairs = [(source, (source + steps) % count) for source in range(count)]
    return lax.ppermute(value, axis, pairs)


def from_partner(x, axis, stride):
    return lax.ppermute(x, axis, [(i, i ^ 1 << stride) for i in range(lax.axis_size(axis))])


def times_phase(re, im, cr, ci):
    if ci == 0:
        if cr == 1:
            return re, im
        return -re, -im
    if ci == 1:
        return -im, re
    return im, -re


def hop_kernel(first, *refs):
    (scal_ref, noise_ref, ntlo_ref, nthi_ref, nzlo_ref, nzhi_ref, u_ref, utedge_ref, uzedge_ref) = refs[:9]
    rest = refs[9:]
    if first:
        out_ref, tfirst_ref, tlast_ref, zfirst_ref, zlast_ref = rest[:5]
        scratch = rest[5:]
    else:
        psi_ref, tlo_ref, thi_ref, zlo_ref, zhi_ref = rest[:5]
        out_ref = rest[5]
        scratch = rest[6:]
    pad_ref, src_ref, zlo_s, zhi_s, u8, ut8, uz8 = scratch
    S, C, RI, T, ROWS, L = src_ref.shape
    Z = ROWS // 2
    K = noise_ref.shape[3]
    span = T // K
    h = pl.program_id(0)
    R = 2 * pl.num_programs(0)
    smask = lambda i: scal_ref[i]
    tmask = lambda i: scal_ref[R * S + i]
    sign = lambda i: scal_ref[R * S + R * (T + 2) + i]
    lower = pl.ds(0, Z)
    upper = pl.ds(Z, Z)

    @pl.when(h == 0)
    def _():
        for a in range(3):
            for b in range(3):
                for ri in range(RI):
                    for half in (lower, upper):
                        ut8[a, b, ri, pl.ds(0, 1), half] = utedge_ref[a, b, ri].astype(jnp.float32)
                        ut8[a, b, ri, pl.ds(1, T), half] = u_ref[3, a, b, ri]
                        for t in range(T):
                            uz8[a, b, ri, t, half] = jnp.broadcast_to(uzedge_ref[a, b, ri, t], (Z, L))
                        for mu in range(4):
                            u8[mu, a, b, ri, :, half] = u_ref[mu, a, b, ri]

    for s in range(S):
        for c in range(C):
            for ri in range(RI):
                for g, half in ((0, lower), (1, upper)):
                    r = 2 * h + g
                    fs = smask(r * S + s)
                    for t in range(T):
                        src_ref[s, c, ri, t, half] = noise_ref[g, c, ri, t // span] * (
                            fs * tmask(r * (T + 2) + t + 1))
                    if first:
                        pad_ref[s, c, ri, 0, half] = ntlo_ref[g, c, ri, 0].astype(jnp.float32) * (
                            fs * tmask(r * (T + 2)) * sign(0))
                        pad_ref[s, c, ri, T + 1, half] = nthi_ref[g, c, ri, 0].astype(jnp.float32) * (
                            fs * tmask(r * (T + 2) + T + 1) * sign(1))
                        for t in range(T):
                            f = fs * tmask(r * (T + 2) + t + 1)
                            zlo_s[s, c, ri, t, half] = jnp.broadcast_to(nzlo_ref[g, c, ri, t // span] * f, (Z, L))
                            zhi_s[s, c, ri, t, half] = jnp.broadcast_to(nzhi_ref[g, c, ri, t // span] * f, (Z, L))
                    else:
                        for t in range(T):
                            if s < 2:
                                zlo_s[s, c, ri, t, half] = jnp.broadcast_to(zlo_ref[s, c, ri, t, pl.ds(g, 1)], (Z, L))
                                zhi_s[s, c, ri, t, half] = jnp.broadcast_to(zhi_ref[s, c, ri, t, pl.ds(g, 1)], (Z, L))
                            else:
                                zlo_s[s, c, ri, t, half] = jnp.zeros((Z, L), jnp.float32)
                                zhi_s[s, c, ri, t, half] = jnp.zeros((Z, L), jnp.float32)
                if first:
                    pad_ref[s, c, ri, pl.ds(1, T)] = src_ref[s, c, ri]
                else:
                    pad_ref[s, c, ri, pl.ds(1, T)] = psi_ref[s, c, ri]
                    if s < 2:
                        pad_ref[s, c, ri, pl.ds(0, 1)] = tlo_ref[s, c, ri].astype(jnp.float32) * sign(0)
                        pad_ref[s, c, ri, pl.ds(T + 1, 1)] = thi_ref[s, c, ri].astype(jnp.float32) * sign(1)
                    else:
                        pad_ref[s, c, ri, pl.ds(0, 1)] = jnp.zeros((1, ROWS, L), jnp.float32)
                        pad_ref[s, c, ri, pl.ds(T + 1, 1)] = jnp.zeros((1, ROWS, L), jnp.float32)
    xpos = lax.broadcasted_iota(jnp.int32, (ROWS, L), 1) % NX
    zpos = lax.broadcasted_iota(jnp.int32, (ROWS, L), 0) % Z
    x_last = xpos == NX - 1
    x_first = xpos == 0
    z_last = zpos == Z - 1
    z_first = zpos == 0

    def x_back(v):
        return jnp.where(x_first, pltpu.roll(v, L - NX + 1, axis=1), pltpu.roll(v, 1, axis=1))

    def body(t, carry):
        acc = [[[None, None] for _ in range(3)] for _ in range(4)]

        def shifted(s, c, ri, mu, stride):
            if mu == 3:
                return pad_ref[s, c, ri, t + 1 + stride]
            v = pad_ref[s, c, ri, t + 1]
            if mu == 2:
                if stride == 1:
                    return jnp.where(z_last, zhi_s[s, c, ri, t], pltpu.roll(v, ROWS - 1, axis=0))
                return jnp.where(z_first, zlo_s[s, c, ri, t], pltpu.roll(v, 1, axis=0))
            if mu == 1:
                return pltpu.roll(v, (L - NX) if stride == 1 else NX, axis=1)
            if stride == 1:
                return jnp.where(x_last, pltpu.roll(v, NX - 1, axis=1), pltpu.roll(v, L - 1, axis=1))
            return x_back(v)

        def back_link(mu, a, b, ri):
            if mu == 3:
                return ut8[a, b, ri, t]
            v = u8[mu, a, b, ri, t]
            if mu == 2:
                return jnp.where(z_first, uz8[a, b, ri, t], pltpu.roll(v, 1, axis=0))
            if mu == 1:
                return pltpu.roll(v, NX, axis=1)
            return x_back(v)

        for mu in range(4):
            perm = GAMMA_PERM[mu]
            heads = [0, 1]
            for stride in (1, -1):
                orient = -1 if stride == 1 else 1
                half = []
                for s in heads:
                    p = perm[s]
                    cr, ci = orient * GAMMA_REAL[mu][s], orient * GAMMA_IMAG[mu][s]
                    colours = []
                    for c in range(3):
                        sre = shifted(s, c, 0, mu, stride)
                        sim = shifted(s, c, 1, mu, stride)
                        pre, pim = times_phase(shifted(p, c, 0, mu, stride), shifted(p, c, 1, mu, stride), cr, ci)
                        colours.append((sre + pre, sim + pim))
                    half.append(colours)
                if stride == 1:
                    links = [[(u8[mu, a, b, 0, t], u8[mu, a, b, 1, t]) for b in range(3)] for a in range(3)]
                else:
                    links = [[(back_link(mu, b, a, 0), back_link(mu, b, a, 1)) for b in range(3)] for a in range(3)]
                for k, s in enumerate(heads):
                    p = perm[s]
                    cpr, cpi = orient * GAMMA_REAL[mu][p], orient * GAMMA_IMAG[mu][p]
                    for a in range(3):
                        sum_re = None
                        sum_im = None
                        for b in range(3):
                            hre, him = half[k][b]
                            lre, lim = links[a][b]
                            if stride == 1:
                                tre = lre * hre - lim * him
                                tim = lre * him + lim * hre
                            else:
                                tre = lre * hre + lim * him
                                tim = lre * him - lim * hre
                            sum_re = tre if sum_re is None else sum_re + tre
                            sum_im = tim if sum_im is None else sum_im + tim
                        for row, (vre, vim) in ((s, (sum_re, sum_im)), (p, times_phase(sum_re, sum_im, cpr, cpi))):
                            if acc[row][a][0] is None:
                                acc[row][a] = [vre, vim]
                            else:
                                acc[row][a] = [acc[row][a][0] + vre, acc[row][a][1] + vim]
        for s in range(4):
            for c in range(3):
                for ri in range(2):
                    psi = pad_ref[s, c, ri, t + 1]
                    src = src_ref[s, c, ri, t]
                    residual = src - (psi - kappa_hop * acc[s][c][ri])
                    value = psi + residual
                    if first:
                        out_ref[s, c, ri, t] = value
                    else:
                        for g in range(2):
                            out_ref[s, c, ri, t, g] = value[g * Z:(g + 1) * Z].astype(out_ref.dtype)
        return carry

    lax.fori_loop(0, T, body, 0)
    if first:
        for mu, stride, target, pick in (
            (3, 1, tfirst_ref, lambda s, c, ri: out_ref[s, c, ri, pl.ds(0, 1)]),
            (3, -1, tlast_ref, lambda s, c, ri: out_ref[s, c, ri, pl.ds(T - 1, 1)]),
        ):
            for k, (re, im) in enumerate(half_spinor(pick, mu, stride)):
                for c in range(C):
                    target[k, c, 0] = re[c].astype(target.dtype)
                    target[k, c, 1] = im[c].astype(target.dtype)
        for g in range(2):
            for mu, stride, target, row in ((2, 1, zfirst_ref, g * Z), (2, -1, zlast_ref, g * Z + Z - 1)):
                pick = lambda s, c, ri: out_ref[s, c, ri, :, pl.ds(row, 1), :]
                for k, (re, im) in enumerate(half_spinor(pick, mu, stride)):
                    for c in range(C):
                        target[k, c, 0, :, pl.ds(g, 1), :] = re[c]
                        target[k, c, 1, :, pl.ds(g, 1), :] = im[c]


def half_spinor(pick, mu, stride):
    orient = -1 if stride == 1 else 1
    rows = []
    for s in (0, 1):
        p = GAMMA_PERM[mu][s]
        cr, ci = orient * GAMMA_REAL[mu][s], orient * GAMMA_IMAG[mu][s]
        res, ims = [], []
        for c in range(3):
            pre, pim = times_phase(pick(p, c, 0), pick(p, c, 1), cr, ci)
            res.append(pick(s, c, 0) + pre)
            ims.append(pick(s, c, 1) + pim)
        rows.append((res, ims))
    return rows


def hopping_step(first, scalars, noise_parts, link_parts, spinor_parts):
    R, C, RI, K, Z, L = noise_parts[0].shape
    T = link_parts[0].shape[4]
    S = 4
    H = R // 2
    ROWS = 2 * Z
    index = lambda h: (h,) + (0,) * 6
    index6 = lambda h: (h,) + (0,) * 5
    whole = lambda x: pl.BlockSpec(x.shape, lambda h: (0,) * x.ndim)
    smem = pl.BlockSpec(memory_space=pltpu.SMEM)
    site_block = pl.BlockSpec((None, S, C, RI, T, ROWS, L), index)
    t_block = pl.BlockSpec((None, 2, C, RI, 1, ROWS, L), index)
    z_block = pl.BlockSpec((None, 2, C, RI, T, 2, L), index)
    noise_specs = [
        pl.BlockSpec((2, C, RI, K, Z, L), index6),
        pl.BlockSpec((2, C, RI, 1, Z, L), index6),
        pl.BlockSpec((2, C, RI, 1, Z, L), index6),
        pl.BlockSpec((2, C, RI, K, 1, L), index6),
        pl.BlockSpec((2, C, RI, K, 1, L), index6),
    ]
    in_specs = [smem] + noise_specs + [whole(x) for x in link_parts]
    site_shape = (H, S, C, RI, T, ROWS, L)
    if first:
        t_shape = jax.ShapeDtypeStruct((H, 2, C, RI, 1, ROWS, L), jnp.bfloat16)
        z_shape = jax.ShapeDtypeStruct((H, 2, C, RI, T, 2, L), jnp.float32)
        out_shape = [jax.ShapeDtypeStruct(site_shape, jnp.float32), t_shape, t_shape, z_shape, z_shape]
        out_specs = [site_block, t_block, t_block, z_block, z_block]
    else:
        in_specs += [site_block, t_block, t_block, z_block, z_block]
        out_shape = jax.ShapeDtypeStruct((H, S, C, RI, T, 2, Z, L), jnp.bfloat16)
        out_specs = pl.BlockSpec((None, S, C, RI, T, 2, Z, L), lambda h: (h,) + (0,) * 7)
    scratch = [
        pltpu.VMEM((S, C, RI, T + 2, ROWS, L), jnp.float32),
        pltpu.VMEM((S, C, RI, T, ROWS, L), jnp.float32),
        pltpu.VMEM((S, C, RI, T, ROWS, L), jnp.float32),
        pltpu.VMEM((S, C, RI, T, ROWS, L), jnp.float32),
        pltpu.VMEM((4, 3, 3, RI, T, ROWS, L), jnp.float32),
        pltpu.VMEM((3, 3, RI, T + 1, ROWS, L), jnp.float32),
        pltpu.VMEM((3, 3, RI, T, ROWS, L), jnp.float32),
    ]
    return pl.pallas_call(
        functools.partial(hop_kernel, first),
        grid=(H,),
        in_specs=in_specs,
        out_specs=out_specs,
        out_shape=out_shape,
        scratch_shapes=scratch,
        compiler_params=pltpu.CompilerParams(dimension_semantics=("arbitrary",)),
        interpret=INTERPRET,
    )(*scalars, *noise_parts, *link_parts, *spinor_parts)


def reduce_scatter_sa(partial_value):
    n = lax.axis_size("sa")
    if n & (n - 1):
        return lax.psum_scatter(partial_value, "sa", scatter_dimension=4, tiled=True)
    lead = partial_value.shape[:-1]
    width = partial_value.shape[-1] // n
    x = jnp.moveaxis(partial_value.reshape(lead + (n, width)), -2, 0)
    me = lax.axis_index("sa")
    d = 1
    while d < n:
        x = x.reshape((x.shape[0] // 2, 2) + x.shape[1:])
        odd = (me // d) % 2 == 1
        keep = jnp.where(odd, x[:, 1], x[:, 0])
        send = jnp.where(odd, x[:, 0], x[:, 1])
        x = keep + lax.ppermute(send, "sa", [(j, j ^ d) for j in range(n)])
        d *= 2
    return x[0]


def intersection_part(rounded, vector_piece):
    products = jnp.einsum(
        "tvcazs,hqcbtgzs->hgqabtv", vector_piece, rounded, preferred_element_type=jnp.float32
    )
    products = products.reshape((-1,) + products.shape[2:])
    real_part = products[:, :, 0, 0] + products[:, :, 1, 1]
    imag_part = products[:, :, 0, 1] - products[:, :, 1, 0]
    return jnp.stack([real_part, imag_part], axis=2)


def local_body(gauge_links, noise_slabs, offsets, vectors):
    partner_vectors = from_partner(vectors, "sec", 0)
    batch_rows = noise_slabs.shape[0]
    slab_length = gauge_links.shape[4]
    Z = gauge_links.shape[5]
    K = noise_slabs.shape[3]
    section_index = lax.axis_index("sec")
    slab_index = lax.axis_index("ta")
    slab_count = lax.axis_size("ta")
    lower_sign = jnp.where(slab_index == 0, -1.0, 1.0).astype(jnp.float32)
    upper_sign = jnp.where(slab_index == slab_count - 1, -1.0, 1.0).astype(jnp.float32)
    signs = jnp.stack([lower_sign, upper_sign])
    t_start = slab_index * slab_length
    own_offsets = lax.dynamic_slice_in_dim(offsets, section_index * batch_rows, batch_rows)
    rhs_index = section_index * batch_rows + jnp.arange(batch_rows)
    spin_mask = (jnp.arange(4)[None, :] == rhs_index[:, None] % 4).astype(jnp.float32)
    times = t_start - 1 + jnp.arange(slab_length + 2)
    time_mask = (times[None, :] % TDIL == own_offsets[:, None]).astype(jnp.float32)
    scalars = (jnp.concatenate([spin_mask.reshape(-1), time_mask.reshape(-1), signs]),)
    noise_parts = (
        noise_slabs,
        passed_along(noise_slabs[:, :, :, K - 1:].astype(jnp.bfloat16), "ta", 1),
        passed_along(noise_slabs[:, :, :, :1].astype(jnp.bfloat16), "ta", -1),
        passed_along(noise_slabs[:, :, :, :, Z - 1:], "sa", 1),
        passed_along(noise_slabs[:, :, :, :, :1], "sa", -1),
    )
    link_parts = (
        gauge_links,
        passed_along(gauge_links[3, :, :, :, -1:, :, :].astype(jnp.bfloat16), "ta", 1),
        passed_along(gauge_links[2, :, :, :, :, -1:, :], "sa", 1),
    )
    spinor, t_first, t_last, z_first, z_last = hopping_step(True, scalars, noise_parts, link_parts, ())
    halos = (
        passed_along(t_last, "ta", 1),
        passed_along(t_first, "ta", -1),
        passed_along(z_last, "sa", 1),
        passed_along(z_first, "sa", -1),
    )
    rounded = hopping_step(False, scalars, noise_parts, link_parts, (spinor,) + halos)
    own_part = intersection_part(rounded, vectors)
    partner_part = intersection_part(rounded, partner_vectors)
    lower_half = jnp.where(section_index == 0, own_part, partner_part)
    upper_half = jnp.where(section_index == 0, partner_part, own_part)
    partial_value = jnp.concatenate([lower_half, upper_half], axis=4)
    return reduce_scatter_sa(partial_value)


def solution(mesh):
    in_specs = (
        P(None, None, None, None, "ta", "sa", None),
        P("sec", None, None, "ta", "sa", None),
        P(),
        P("ta", "sec", None, None, "sa", None),
    )
    out_specs = P("sec", None, None, "ta", "sa")
    return jax.shard_map(local_body, mesh=mesh, in_specs=in_specs, out_specs=out_specs, check_vma=False)
```

```python
import functools

import jax
import jax.numpy as jnp
from jax import lax
from jax.experimental import pallas as pl
from jax.experimental.pallas import tpu as pltpu
from jax.sharding import PartitionSpec as P


NX = 32
TDIL = 4
INTERPRET = False


kappa_hop = 0.12
GAMMA_PERM = ((3, 2, 1, 0), (3, 2, 1, 0), (2, 3, 0, 1), (2, 3, 0, 1))
GAMMA_REAL = ((0, 0, 0, 0), (-1, 1, 1, -1), (0, 0, 0, 0), (1, 1, 1, 1))
GAMMA_IMAG = ((1, 1, -1, -1), (0, 0, 0, 0), (1, -1, -1, 1), (0, 0, 0, 0))


def passed_along(value, axis, steps):
    count = lax.axis_size(axis)
    pairs = [(source, (source + steps) % count) for source in range(count)]
    return lax.ppermute(value, axis, pairs)


def from_partner(x, axis, stride):
    return lax.ppermute(x, axis, [(i, i ^ 1 << stride) for i in range(lax.axis_size(axis))])


def times_phase(re, im, cr, ci):
    if ci == 0:
        if cr == 1:
            return re, im
        return -re, -im
    if ci == 1:
        return -im, re
    return im, -re


def add_phase(are, aim, re, im, cr, ci):
    if ci == 0:
        if cr == 1:
            return are + re, aim + im
        return are - re, aim - im
    if ci == 1:
        return are - im, aim + re
    return are + im, aim - re


def hop_kernel(first, *refs):
    (scal_ref, noise_ref, ntlo_ref, nthi_ref, nzlo_ref, nzhi_ref, u_ref, utedge_ref, uzedge_ref) = refs[:9]
    rest = refs[9:]
    if first:
        out_ref, tfirst_ref, tlast_ref, zfirst_ref, zlast_ref = rest[:5]
        scratch = rest[5:]
    else:
        psi_ref, tlo_ref, thi_ref, zlo_ref, zhi_ref = rest[:5]
        out_ref = rest[5]
        scratch = rest[6:]
    pad_ref, src_ref, zlo_s, zhi_s, u8, ut8, uz8 = scratch
    S, C, RI, T, ROWS, L = src_ref.shape
    Z = ROWS // 2
    K = noise_ref.shape[3]
    span = T // K
    h = pl.program_id(0)
    R = 2 * pl.num_programs(0)
    smask = lambda i: scal_ref[i]
    tmask = lambda i: scal_ref[R * S + i]
    sign = lambda i: scal_ref[R * S + R * (T + 2) + i]
    lower = pl.ds(0, Z)
    upper = pl.ds(Z, Z)

    @pl.when(h == 0)
    def _():
        for a in range(3):
            for b in range(3):
                for ri in range(RI):
                    for half in (lower, upper):
                        ut8[a, b, ri, pl.ds(0, 1), half] = utedge_ref[a, b, ri]
                        ut8[a, b, ri, pl.ds(1, T), half] = u_ref[3, a, b, ri]
                        for t in range(T):
                            uz8[a, b, ri, t, half] = jnp.broadcast_to(uzedge_ref[a, b, ri, t], (Z, L))
                        for mu in range(4):
                            u8[mu, a, b, ri, :, half] = u_ref[mu, a, b, ri]

    for s in range(S):
        for c in range(C):
            for ri in range(RI):
                for g, half in ((0, lower), (1, upper)):
                    r = 2 * h + g
                    fs = smask(r * S + s)
                    for t in range(T):
                        src_ref[s, c, ri, t, half] = noise_ref[g, c, ri, t // span] * (
                            fs * tmask(r * (T + 2) + t + 1))
                    if first:
                        pad_ref[s, c, ri, 0, half] = ntlo_ref[g, c, ri, 0] * (
                            fs * tmask(r * (T + 2)) * sign(0))
                        pad_ref[s, c, ri, T + 1, half] = nthi_ref[g, c, ri, 0] * (
                            fs * tmask(r * (T + 2) + T + 1) * sign(1))
                        for t in range(T):
                            f = fs * tmask(r * (T + 2) + t + 1)
                            zlo_s[s, c, ri, t, half] = jnp.broadcast_to(nzlo_ref[g, c, ri, t // span] * f, (Z, L))
                            zhi_s[s, c, ri, t, half] = jnp.broadcast_to(nzhi_ref[g, c, ri, t // span] * f, (Z, L))
                    else:
                        for t in range(T):
                            if s < 2:
                                zlo_s[s, c, ri, t, half] = jnp.broadcast_to(zlo_ref[s, c, ri, t, pl.ds(g, 1)], (Z, L))
                                zhi_s[s, c, ri, t, half] = jnp.broadcast_to(zhi_ref[s, c, ri, t, pl.ds(g, 1)], (Z, L))
                            else:
                                zlo_s[s, c, ri, t, half] = jnp.zeros((Z, L), jnp.float32)
                                zhi_s[s, c, ri, t, half] = jnp.zeros((Z, L), jnp.float32)
                if first:
                    pad_ref[s, c, ri, pl.ds(1, T)] = src_ref[s, c, ri]
                else:
                    pad_ref[s, c, ri, pl.ds(1, T)] = psi_ref[s, c, ri]
                    if s < 2:
                        pad_ref[s, c, ri, pl.ds(0, 1)] = tlo_ref[s, c, ri].astype(jnp.float32) * sign(0)
                        pad_ref[s, c, ri, pl.ds(T + 1, 1)] = thi_ref[s, c, ri].astype(jnp.float32) * sign(1)
                    else:
                        pad_ref[s, c, ri, pl.ds(0, 1)] = jnp.zeros((1, ROWS, L), jnp.float32)
                        pad_ref[s, c, ri, pl.ds(T + 1, 1)] = jnp.zeros((1, ROWS, L), jnp.float32)
    xpos = lax.broadcasted_iota(jnp.int32, (ROWS, L), 1) % NX
    zpos = lax.broadcasted_iota(jnp.int32, (ROWS, L), 0) % Z
    x_last = xpos == NX - 1
    x_first = xpos == 0
    z_last = zpos == Z - 1
    z_first = zpos == 0

    def x_back(v):
        return jnp.where(x_first, pltpu.roll(v, L - NX + 1, axis=1), pltpu.roll(v, 1, axis=1))

    def body(t, carry):
        acc = [[[None, None] for _ in range(3)] for _ in range(4)]

        def shifted(s, c, ri, mu, stride):
            if mu == 3:
                return pad_ref[s, c, ri, t + 1 + stride]
            v = pad_ref[s, c, ri, t + 1]
            if mu == 2:
                if stride == 1:
                    return jnp.where(z_last, zhi_s[s, c, ri, t], pltpu.roll(v, ROWS - 1, axis=0))
                return jnp.where(z_first, zlo_s[s, c, ri, t], pltpu.roll(v, 1, axis=0))
            if mu == 1:
                return pltpu.roll(v, (L - NX) if stride == 1 else NX, axis=1)
            if stride == 1:
                return jnp.where(x_last, pltpu.roll(v, NX - 1, axis=1), pltpu.roll(v, L - 1, axis=1))
            return x_back(v)

        def back_link(mu, a, b, ri):
            if mu == 3:
                return ut8[a, b, ri, t]
            v = u8[mu, a, b, ri, t]
            if mu == 2:
                return jnp.where(z_first, uz8[a, b, ri, t], pltpu.roll(v, 1, axis=0))
            if mu == 1:
                return pltpu.roll(v, NX, axis=1)
            return x_back(v)

        for mu in range(4):
            perm = GAMMA_PERM[mu]
            heads = [0, 1]
            for stride in (1, -1):
                orient = -1 if stride == 1 else 1
                half = []
                for s in heads:
                    p = perm[s]
                    cr, ci = orient * GAMMA_REAL[mu][s], orient * GAMMA_IMAG[mu][s]
                    colours = []
                    for c in range(3):
                        sre = shifted(s, c, 0, mu, stride)
                        sim = shifted(s, c, 1, mu, stride)
                        colours.append(add_phase(sre, sim, shifted(p, c, 0, mu, stride), shifted(p, c, 1, mu, stride), cr, ci))
                    half.append(colours)
                if stride == 1:
                    links = [[(u8[mu, a, b, 0, t], u8[mu, a, b, 1, t]) for b in range(3)] for a in range(3)]
                else:
                    links = [[(back_link(mu, b, a, 0), back_link(mu, b, a, 1)) for b in range(3)] for a in range(3)]
                for k, s in enumerate(heads):
                    p = perm[s]
                    cpr, cpi = orient * GAMMA_REAL[mu][p], orient * GAMMA_IMAG[mu][p]
                    for a in range(3):
                        sum_re = None
                        sum_im = None
                        for b in range(3):
                            hre, him = half[k][b]
                            lre, lim = links[a][b]
                            if stride == 1:
                                tre = lre * hre - lim * him
                                tim = lre * him + lim * hre
                            else:
                                tre = lre * hre + lim * him
                                tim = lre * him - lim * hre
                            sum_re = tre if sum_re is None else sum_re + tre
                            sum_im = tim if sum_im is None else sum_im + tim
                        if acc[s][a][0] is None:
                            acc[s][a] = [sum_re, sum_im]
                        else:
                            acc[s][a] = [acc[s][a][0] + sum_re, acc[s][a][1] + sum_im]
                        if acc[p][a][0] is None:
                            acc[p][a] = list(times_phase(sum_re, sum_im, cpr, cpi))
                        else:
                            acc[p][a] = list(add_phase(acc[p][a][0], acc[p][a][1], sum_re, sum_im, cpr, cpi))
        for s in range(4):
            for c in range(3):
                for ri in range(2):
                    psi = pad_ref[s, c, ri, t + 1]
                    src = src_ref[s, c, ri, t]
                    residual = src - (psi - kappa_hop * acc[s][c][ri])
                    value = psi + residual
                    if first:
                        out_ref[s, c, ri, t] = value
                    else:
                        for g in range(2):
                            out_ref[s, c, ri, t, g] = value[g * Z:(g + 1) * Z].astype(out_ref.dtype)
        return carry

    lax.fori_loop(0, T, body, 0)
    if first:
        for mu, stride, target, pick in (
            (3, 1, tfirst_ref, lambda s, c, ri: out_ref[s, c, ri, pl.ds(0, 1)]),
            (3, -1, tlast_ref, lambda s, c, ri: out_ref[s, c, ri, pl.ds(T - 1, 1)]),
        ):
            for k, (re, im) in enumerate(half_spinor(pick, mu, stride)):
                for c in range(C):
                    target[k, c, 0] = re[c].astype(target.dtype)
                    target[k, c, 1] = im[c].astype(target.dtype)
        for g in range(2):
            for mu, stride, target, row in ((2, 1, zfirst_ref, g * Z), (2, -1, zlast_ref, g * Z + Z - 1)):
                pick = lambda s, c, ri: out_ref[s, c, ri, :, pl.ds(row, 1), :]
                for k, (re, im) in enumerate(half_spinor(pick, mu, stride)):
                    for c in range(C):
                        target[k, c, 0, :, pl.ds(g, 1), :] = re[c]
                        target[k, c, 1, :, pl.ds(g, 1), :] = im[c]


def half_spinor(pick, mu, stride):
    orient = -1 if stride == 1 else 1
    rows = []
    for s in (0, 1):
        p = GAMMA_PERM[mu][s]
        cr, ci = orient * GAMMA_REAL[mu][s], orient * GAMMA_IMAG[mu][s]
        res, ims = [], []
        for c in range(3):
            pre, pim = times_phase(pick(p, c, 0), pick(p, c, 1), cr, ci)
            res.append(pick(s, c, 0) + pre)
            ims.append(pick(s, c, 1) + pim)
        rows.append((res, ims))
    return rows


def hopping_step(first, scalars, noise_parts, link_parts, spinor_parts):
    R, C, RI, K, Z, L = noise_parts[0].shape
    T = link_parts[0].shape[4]
    S = 4
    H = R // 2
    ROWS = 2 * Z
    index = lambda h: (h,) + (0,) * 6
    index6 = lambda h: (h,) + (0,) * 5
    whole = lambda x: pl.BlockSpec(x.shape, lambda h: (0,) * x.ndim)
    smem = pl.BlockSpec(memory_space=pltpu.SMEM)
    site_block = pl.BlockSpec((None, S, C, RI, T, ROWS, L), index)
    t_block = pl.BlockSpec((None, 2, C, RI, 1, ROWS, L), index)
    z_block = pl.BlockSpec((None, 2, C, RI, T, 2, L), index)
    noise_specs = [
        pl.BlockSpec((2, C, RI, K, Z, L), index6),
        pl.BlockSpec((2, C, RI, 1, Z, L), index6),
        pl.BlockSpec((2, C, RI, 1, Z, L), index6),
        pl.BlockSpec((2, C, RI, K, 1, L), index6),
        pl.BlockSpec((2, C, RI, K, 1, L), index6),
    ]
    in_specs = [smem] + noise_specs + [whole(x) for x in link_parts]
    site_shape = (H, S, C, RI, T, ROWS, L)
    if first:
        t_shape = jax.ShapeDtypeStruct((H, 2, C, RI, 1, ROWS, L), jnp.bfloat16)
        z_shape = jax.ShapeDtypeStruct((H, 2, C, RI, T, 2, L), jnp.float32)
        out_shape = [jax.ShapeDtypeStruct(site_shape, jnp.float32), t_shape, t_shape, z_shape, z_shape]
        out_specs = [site_block, t_block, t_block, z_block, z_block]
    else:
        in_specs += [site_block, t_block, t_block, z_block, z_block]
        out_shape = jax.ShapeDtypeStruct((H, S, C, RI, T, 2, Z, L), jnp.bfloat16)
        out_specs = pl.BlockSpec((None, S, C, RI, T, 2, Z, L), lambda h: (h,) + (0,) * 7)
    scratch = [
        pltpu.VMEM((S, C, RI, T + 2, ROWS, L), jnp.float32),
        pltpu.VMEM((S, C, RI, T, ROWS, L), jnp.float32),
        pltpu.VMEM((S, C, RI, T, ROWS, L), jnp.float32),
        pltpu.VMEM((S, C, RI, T, ROWS, L), jnp.float32),
        pltpu.VMEM((4, 3, 3, RI, T, ROWS, L), jnp.float32),
        pltpu.VMEM((3, 3, RI, T + 1, ROWS, L), jnp.float32),
        pltpu.VMEM((3, 3, RI, T, ROWS, L), jnp.float32),
    ]
    return pl.pallas_call(
        functools.partial(hop_kernel, first),
        grid=(H,),
        in_specs=in_specs,
        out_specs=out_specs,
        out_shape=out_shape,
        scratch_shapes=scratch,
        compiler_params=pltpu.CompilerParams(dimension_semantics=("arbitrary",)),
        interpret=INTERPRET,
    )(*scalars, *noise_parts, *link_parts, *spinor_parts)


def reduce_scatter_sa(partial_value):
    n = lax.axis_size("sa")
    if n & (n - 1):
        return lax.psum_scatter(partial_value, "sa", scatter_dimension=4, tiled=True)
    lead = partial_value.shape[:-1]
    width = partial_value.shape[-1] // n
    x = jnp.moveaxis(partial_value.reshape(lead + (n, width)), -2, 0)
    me = lax.axis_index("sa")
    d = 1
    while d < n:
        x = x.reshape((x.shape[0] // 2, 2) + x.shape[1:])
        odd = (me // d) % 2 == 1
        keep = jnp.where(odd, x[:, 1], x[:, 0])
        send = jnp.where(odd, x[:, 0], x[:, 1])
        x = keep + lax.ppermute(send, "sa", [(j, j ^ d) for j in range(n)])
        d *= 2
    return x[0]


def intersection_part(rounded, vector_piece):
    products = jnp.einsum(
        "tvcazs,hqcbtgzs->hgqabtv", vector_piece, rounded, preferred_element_type=jnp.float32
    )
    products = products.reshape((-1,) + products.shape[2:])
    real_part = products[:, :, 0, 0] + products[:, :, 1, 1]
    imag_part = products[:, :, 0, 1] - products[:, :, 1, 0]
    return jnp.stack([real_part, imag_part], axis=2)


def local_body(gauge_links, noise_slabs, offsets, vectors):
    partner_vectors = from_partner(vectors, "sec", 0)
    batch_rows = noise_slabs.shape[0]
    slab_length = gauge_links.shape[4]
    Z = gauge_links.shape[5]
    K = noise_slabs.shape[3]
    section_index = lax.axis_index("sec")
    slab_index = lax.axis_index("ta")
    slab_count = lax.axis_size("ta")
    lower_sign = jnp.where(slab_index == 0, -1.0, 1.0).astype(jnp.float32)
    upper_sign = jnp.where(slab_index == slab_count - 1, -1.0, 1.0).astype(jnp.float32)
    signs = jnp.stack([lower_sign, upper_sign])
    t_start = slab_index * slab_length
    own_offsets = lax.dynamic_slice_in_dim(offsets, section_index * batch_rows, batch_rows)
    rhs_index = section_index * batch_rows + jnp.arange(batch_rows)
    spin_mask = (jnp.arange(4)[None, :] == rhs_index[:, None] % 4).astype(jnp.float32)
    times = t_start - 1 + jnp.arange(slab_length + 2)
    time_mask = (times[None, :] % TDIL == own_offsets[:, None]).astype(jnp.float32)
    scalars = (jnp.concatenate([spin_mask.reshape(-1), time_mask.reshape(-1), signs]),)
    noise_parts = (
        noise_slabs,
        passed_along(noise_slabs[:, :, :, K - 1:], "ta", 1),
        passed_along(noise_slabs[:, :, :, :1], "ta", -1),
        passed_along(noise_slabs[:, :, :, :, Z - 1:], "sa", 1),
        passed_along(noise_slabs[:, :, :, :, :1], "sa", -1),
    )
    link_parts = (
        gauge_links,
        passed_along(gauge_links[3, :, :, :, -1:, :, :], "ta", 1),
        passed_along(gauge_links[2, :, :, :, :, -1:, :], "sa", 1),
    )
    spinor, t_first, t_last, z_first, z_last = hopping_step(True, scalars, noise_parts, link_parts, ())
    halos = (
        passed_along(t_last, "ta", 1),
        passed_along(t_first, "ta", -1),
        passed_along(z_last, "sa", 1),
        passed_along(z_first, "sa", -1),
    )
    rounded = hopping_step(False, scalars, noise_parts, link_parts, (spinor,) + halos)
    own_part = intersection_part(rounded, vectors)
    partner_part = intersection_part(rounded, partner_vectors)
    lower_half = jnp.where(section_index == 0, own_part, partner_part)
    upper_half = jnp.where(section_index == 0, partner_part, own_part)
    partial_value = jnp.concatenate([lower_half, upper_half], axis=4)
    return reduce_scatter_sa(partial_value)


def solution(mesh):
    in_specs = (
        P(None, None, None, None, "ta", "sa", None),
        P("sec", None, None, "ta", "sa", None),
        P(),
        P("ta", "sec", None, None, "sa", None),
    )
    out_specs = P("sec", None, None, "ta", "sa")
    return jax.shard_map(local_body, mesh=mesh, in_specs=in_specs, out_specs=out_specs, check_vma=False)
```

```python
import functools

import jax
import jax.numpy as jnp
from jax import lax
from jax.experimental import pallas as pl
from jax.experimental.pallas import tpu as pltpu
from jax.sharding import PartitionSpec as P


NX = 32
TDIL = 4
INTERPRET = False


kappa_hop = 0.12
GAMMA_PERM = ((3, 2, 1, 0), (3, 2, 1, 0), (2, 3, 0, 1), (2, 3, 0, 1))
GAMMA_REAL = ((0, 0, 0, 0), (-1, 1, 1, -1), (0, 0, 0, 0), (1, 1, 1, 1))
GAMMA_IMAG = ((1, 1, -1, -1), (0, 0, 0, 0), (1, -1, -1, 1), (0, 0, 0, 0))


def passed_along(value, axis, steps):
    count = lax.axis_size(axis)
    pairs = [(source, (source + steps) % count) for source in range(count)]
    return lax.ppermute(value, axis, pairs)


def from_partner(x, axis, stride):
    return lax.ppermute(x, axis, [(i, i ^ 1 << stride) for i in range(lax.axis_size(axis))])


def times_phase(re, im, cr, ci):
    if ci == 0:
        if cr == 1:
            return re, im
        return -re, -im
    if ci == 1:
        return -im, re
    return im, -re


def add_phase(are, aim, re, im, cr, ci):
    if ci == 0:
        if cr == 1:
            return are + re, aim + im
        return are - re, aim - im
    if ci == 1:
        return are - im, aim + re
    return are + im, aim - re


def hop_kernel(first, *refs):
    (scal_ref, noise_ref, ntlo_ref, nthi_ref, nzlo_ref, nzhi_ref, u_ref, utedge_ref, uzedge_ref) = refs[:9]
    rest = refs[9:]
    if first:
        out_ref, tfirst_ref, tlast_ref, zfirst_ref, zlast_ref = rest[:5]
        scratch = rest[5:]
    else:
        psi_ref, tlo_ref, thi_ref, zlo_ref, zhi_ref = rest[:5]
        out_ref = rest[5]
        scratch = rest[6:]
    pad_ref, src_ref, zlo_s, zhi_s, u8, ut8, uz8 = scratch
    S, C, RI, T, ROWS, L = src_ref.shape
    Z = ROWS // 2
    K = noise_ref.shape[3]
    span = T // K
    h = pl.program_id(0)
    R = 2 * pl.num_programs(0)
    smask = lambda i: scal_ref[i]
    tmask = lambda i: scal_ref[R * S + i]
    sign = lambda i: scal_ref[R * S + R * (T + 2) + i]
    lower = pl.ds(0, Z)
    upper = pl.ds(Z, Z)

    @pl.when(h == 0)
    def _():
        for a in range(3):
            for b in range(3):
                for ri in range(RI):
                    for half in (lower, upper):
                        ut8[a, b, ri, pl.ds(0, 1), half] = utedge_ref[a, b, ri]
                        ut8[a, b, ri, pl.ds(1, T), half] = u_ref[3, a, b, ri]
                        for t in range(T):
                            uz8[a, b, ri, t, half] = jnp.broadcast_to(uzedge_ref[a, b, ri, t], (Z, L))
                        for mu in range(4):
                            u8[mu, a, b, ri, :, half] = u_ref[mu, a, b, ri]

    for s in range(S):
        for c in range(C):
            for ri in range(RI):
                for g, half in ((0, lower), (1, upper)):
                    r = 2 * h + g
                    fs = smask(r * S + s)
                    for t in range(T):
                        src_ref[s, c, ri, t, half] = noise_ref[g, c, ri, t // span] * (
                            fs * tmask(r * (T + 2) + t + 1))
                    if first:
                        pad_ref[s, c, ri, 0, half] = ntlo_ref[g, c, ri, 0] * (
                            fs * tmask(r * (T + 2)) * sign(0))
                        pad_ref[s, c, ri, T + 1, half] = nthi_ref[g, c, ri, 0] * (
                            fs * tmask(r * (T + 2) + T + 1) * sign(1))
                        for t in range(T):
                            f = fs * tmask(r * (T + 2) + t + 1)
                            zlo_s[s, c, ri, t, half] = jnp.broadcast_to(nzlo_ref[g, c, ri, t // span] * f, (Z, L))
                            zhi_s[s, c, ri, t, half] = jnp.broadcast_to(nzhi_ref[g, c, ri, t // span] * f, (Z, L))
                    else:
                        for t in range(T):
                            if s < 2:
                                zlo_s[s, c, ri, t, half] = jnp.broadcast_to(zlo_ref[s, c, ri, t, pl.ds(g, 1)], (Z, L))
                                zhi_s[s, c, ri, t, half] = jnp.broadcast_to(zhi_ref[s, c, ri, t, pl.ds(g, 1)], (Z, L))
                            else:
                                zlo_s[s, c, ri, t, half] = jnp.zeros((Z, L), jnp.float32)
                                zhi_s[s, c, ri, t, half] = jnp.zeros((Z, L), jnp.float32)
                if first:
                    pad_ref[s, c, ri, pl.ds(1, T)] = src_ref[s, c, ri]
                else:
                    pad_ref[s, c, ri, pl.ds(1, T)] = psi_ref[s, c, ri]
                    if s < 2:
                        pad_ref[s, c, ri, pl.ds(0, 1)] = tlo_ref[s, c, ri].astype(jnp.float32) * sign(0)
                        pad_ref[s, c, ri, pl.ds(T + 1, 1)] = thi_ref[s, c, ri].astype(jnp.float32) * sign(1)
                    else:
                        pad_ref[s, c, ri, pl.ds(0, 1)] = jnp.zeros((1, ROWS, L), jnp.float32)
                        pad_ref[s, c, ri, pl.ds(T + 1, 1)] = jnp.zeros((1, ROWS, L), jnp.float32)
    xpos = lax.broadcasted_iota(jnp.int32, (ROWS, L), 1) % NX
    zpos = lax.broadcasted_iota(jnp.int32, (ROWS, L), 0) % Z
    x_last = xpos == NX - 1
    x_first = xpos == 0
    z_last = zpos == Z - 1
    z_first = zpos == 0

    def x_back(v):
        return jnp.where(x_first, pltpu.roll(v, L - NX + 1, axis=1), pltpu.roll(v, 1, axis=1))

    def body(t, carry):
        acc = [[[None, None] for _ in range(3)] for _ in range(4)]

        def shifted(s, c, ri, mu, stride):
            if mu == 3:
                return pad_ref[s, c, ri, t + 1 + stride]
            v = pad_ref[s, c, ri, t + 1]
            if mu == 2:
                if stride == 1:
                    return jnp.where(z_last, zhi_s[s, c, ri, t], pltpu.roll(v, ROWS - 1, axis=0))
                return jnp.where(z_first, zlo_s[s, c, ri, t], pltpu.roll(v, 1, axis=0))
            if mu == 1:
                return pltpu.roll(v, (L - NX) if stride == 1 else NX, axis=1)
            if stride == 1:
                return jnp.where(x_last, pltpu.roll(v, NX - 1, axis=1), pltpu.roll(v, L - 1, axis=1))
            return x_back(v)

        def back_link(mu, a, b, ri):
            if mu == 3:
                return ut8[a, b, ri, t]
            v = u8[mu, a, b, ri, t]
            if mu == 2:
                return jnp.where(z_first, uz8[a, b, ri, t], pltpu.roll(v, 1, axis=0))
            if mu == 1:
                return pltpu.roll(v, NX, axis=1)
            return x_back(v)

        for mu in range(4):
            perm = GAMMA_PERM[mu]
            heads = [0, 1]
            for stride in (1, -1):
                orient = -1 if stride == 1 else 1
                half = []
                for s in heads:
                    p = perm[s]
                    cr, ci = orient * GAMMA_REAL[mu][s], orient * GAMMA_IMAG[mu][s]
                    colours = []
                    for c in range(3):
                        sre = shifted(s, c, 0, mu, stride)
                        sim = shifted(s, c, 1, mu, stride)
                        colours.append(add_phase(sre, sim, shifted(p, c, 0, mu, stride), shifted(p, c, 1, mu, stride), cr, ci))
                    half.append(colours)
                if stride == 1:
                    links = [[(u8[mu, a, b, 0, t], u8[mu, a, b, 1, t]) for b in range(3)] for a in range(3)]
                else:
                    links = [[(back_link(mu, b, a, 0), back_link(mu, b, a, 1)) for b in range(3)] for a in range(3)]
                for k, s in enumerate(heads):
                    p = perm[s]
                    cpr, cpi = orient * GAMMA_REAL[mu][p], orient * GAMMA_IMAG[mu][p]
                    for a in range(3):
                        sum_re = None
                        sum_im = None
                        for b in range(3):
                            hre, him = half[k][b]
                            lre, lim = links[a][b]
                            if stride == 1:
                                tre = lre * hre - lim * him
                                tim = lre * him + lim * hre
                            else:
                                tre = lre * hre + lim * him
                                tim = lre * him - lim * hre
                            sum_re = tre if sum_re is None else sum_re + tre
                            sum_im = tim if sum_im is None else sum_im + tim
                        if acc[s][a][0] is None:
                            acc[s][a] = [sum_re, sum_im]
                        else:
                            acc[s][a] = [acc[s][a][0] + sum_re, acc[s][a][1] + sum_im]
                        if acc[p][a][0] is None:
                            acc[p][a] = list(times_phase(sum_re, sum_im, cpr, cpi))
                        else:
                            acc[p][a] = list(add_phase(acc[p][a][0], acc[p][a][1], sum_re, sum_im, cpr, cpi))
        for s in range(4):
            for c in range(3):
                for ri in range(2):
                    psi = pad_ref[s, c, ri, t + 1]
                    src = src_ref[s, c, ri, t]
                    residual = src - (psi - kappa_hop * acc[s][c][ri])
                    value = psi + residual
                    if first:
                        out_ref[s, c, ri, t] = value
                    else:
                        for g in range(2):
                            out_ref[s, c, ri, t, g] = value[g * Z:(g + 1) * Z].astype(out_ref.dtype)
        return carry

    lax.fori_loop(0, T, body, 0)
    if first:
        for mu, stride, target, pick in (
            (3, 1, tfirst_ref, lambda s, c, ri: out_ref[s, c, ri, pl.ds(0, 1)]),
            (3, -1, tlast_ref, lambda s, c, ri: out_ref[s, c, ri, pl.ds(T - 1, 1)]),
        ):
            for k, (re, im) in enumerate(half_spinor(pick, mu, stride)):
                for c in range(C):
                    target[k, c, 0] = re[c].astype(target.dtype)
                    target[k, c, 1] = im[c].astype(target.dtype)
        for g in range(2):
            for mu, stride, target, row in ((2, 1, zfirst_ref, g * Z), (2, -1, zlast_ref, g * Z + Z - 1)):
                pick = lambda s, c, ri: out_ref[s, c, ri, :, pl.ds(row, 1), :]
                for k, (re, im) in enumerate(half_spinor(pick, mu, stride)):
                    for c in range(C):
                        target[k, c, 0, :, pl.ds(g, 1), :] = re[c]
                        target[k, c, 1, :, pl.ds(g, 1), :] = im[c]


def half_spinor(pick, mu, stride):
    orient = -1 if stride == 1 else 1
    rows = []
    for s in (0, 1):
        p = GAMMA_PERM[mu][s]
        cr, ci = orient * GAMMA_REAL[mu][s], orient * GAMMA_IMAG[mu][s]
        res, ims = [], []
        for c in range(3):
            pre, pim = times_phase(pick(p, c, 0), pick(p, c, 1), cr, ci)
            res.append(pick(s, c, 0) + pre)
            ims.append(pick(s, c, 1) + pim)
        rows.append((res, ims))
    return rows


def hopping_step(first, scalars, noise_parts, link_parts, spinor_parts):
    R, C, RI, K, Z, L = noise_parts[0].shape
    T = link_parts[0].shape[4]
    S = 4
    H = R // 2
    ROWS = 2 * Z
    index = lambda h: (h,) + (0,) * 6
    index6 = lambda h: (h,) + (0,) * 5
    whole = lambda x: pl.BlockSpec(x.shape, lambda h: (0,) * x.ndim)
    smem = pl.BlockSpec(memory_space=pltpu.SMEM)
    site_block = pl.BlockSpec((None, S, C, RI, T, ROWS, L), index)
    t_block = pl.BlockSpec((None, 2, C, RI, 1, ROWS, L), index)
    z_block = pl.BlockSpec((None, 2, C, RI, T, 2, L), index)
    noise_specs = [
        pl.BlockSpec((2, C, RI, K, Z, L), index6),
        pl.BlockSpec((2, C, RI, 1, Z, L), index6),
        pl.BlockSpec((2, C, RI, 1, Z, L), index6),
        pl.BlockSpec((2, C, RI, K, 1, L), index6),
        pl.BlockSpec((2, C, RI, K, 1, L), index6),
    ]
    in_specs = [smem] + noise_specs + [whole(x) for x in link_parts]
    site_shape = (H, S, C, RI, T, ROWS, L)
    if first:
        t_shape = jax.ShapeDtypeStruct((H, 2, C, RI, 1, ROWS, L), jnp.bfloat16)
        z_shape = jax.ShapeDtypeStruct((H, 2, C, RI, T, 2, L), jnp.float32)
        out_shape = [jax.ShapeDtypeStruct(site_shape, jnp.float32), t_shape, t_shape, z_shape, z_shape]
        out_specs = [site_block, t_block, t_block, z_block, z_block]
    else:
        in_specs += [site_block, t_block, t_block, z_block, z_block]
        out_shape = jax.ShapeDtypeStruct((H, S, C, RI, T, 2, Z, L), jnp.bfloat16)
        out_specs = pl.BlockSpec((None, S, C, RI, T, 2, Z, L), lambda h: (h,) + (0,) * 7)
    scratch = [
        pltpu.VMEM((S, C, RI, T + 2, ROWS, L), jnp.float32),
        pltpu.VMEM((S, C, RI, T, ROWS, L), jnp.float32),
        pltpu.VMEM((S, C, RI, T, ROWS, L), jnp.float32),
        pltpu.VMEM((S, C, RI, T, ROWS, L), jnp.float32),
        pltpu.VMEM((4, 3, 3, RI, T, ROWS, L), jnp.float32),
        pltpu.VMEM((3, 3, RI, T + 1, ROWS, L), jnp.float32),
        pltpu.VMEM((3, 3, RI, T, ROWS, L), jnp.float32),
    ]
    return pl.pallas_call(
        functools.partial(hop_kernel, first),
        grid=(H,),
        in_specs=in_specs,
        out_specs=out_specs,
        out_shape=out_shape,
        scratch_shapes=scratch,
        compiler_params=pltpu.CompilerParams(dimension_semantics=("arbitrary",)),
        interpret=INTERPRET,
    )(*scalars, *noise_parts, *link_parts, *spinor_parts)


def reduce_scatter_sa(partial_value):
    n = lax.axis_size("sa")
    if n & (n - 1):
        return lax.psum_scatter(partial_value, "sa", scatter_dimension=4, tiled=True)
    lead = partial_value.shape[:-1]
    width = partial_value.shape[-1] // n
    x = jnp.moveaxis(partial_value.reshape(lead + (n, width)), -2, 0)
    me = lax.axis_index("sa")
    d = 1
    while d < n:
        x = x.reshape((x.shape[0] // 2, 2) + x.shape[1:])
        odd = (me // d) % 2 == 1
        keep = jnp.where(odd, x[:, 1], x[:, 0])
        send = jnp.where(odd, x[:, 0], x[:, 1])
        x = keep + lax.ppermute(send, "sa", [(j, j ^ d) for j in range(n)])
        d *= 2
    return x[0]


def intersection_part(rounded, vector_piece):
    products = jnp.einsum(
        "tvcazs,hqcbtgzs->hgqabtv", vector_piece, rounded, preferred_element_type=jnp.float32
    )
    products = products.reshape((-1,) + products.shape[2:])
    real_part = products[:, :, 0, 0] + products[:, :, 1, 1]
    imag_part = products[:, :, 0, 1] - products[:, :, 1, 0]
    return jnp.stack([real_part, imag_part], axis=2)


def local_body(gauge_links, noise_slabs, offsets, vectors):
    partner_vectors = from_partner(vectors, "sec", 0)
    batch_rows = noise_slabs.shape[0]
    slab_length = gauge_links.shape[4]
    Z = gauge_links.shape[5]
    K = noise_slabs.shape[3]
    section_index = lax.axis_index("sec")
    slab_index = lax.axis_index("ta")
    slab_count = lax.axis_size("ta")
    lower_sign = jnp.where(slab_index == 0, -1.0, 1.0).astype(jnp.float32)
    upper_sign = jnp.where(slab_index == slab_count - 1, -1.0, 1.0).astype(jnp.float32)
    signs = jnp.stack([lower_sign, upper_sign])
    t_start = slab_index * slab_length
    own_offsets = lax.dynamic_slice_in_dim(offsets, section_index * batch_rows, batch_rows)
    rhs_index = section_index * batch_rows + jnp.arange(batch_rows)
    spin_mask = (jnp.arange(4)[None, :] == rhs_index[:, None] % 4).astype(jnp.float32)
    times = t_start - 1 + jnp.arange(slab_length + 2)
    time_mask = (times[None, :] % TDIL == own_offsets[:, None]).astype(jnp.float32)
    scalars = (jnp.concatenate([spin_mask.reshape(-1), time_mask.reshape(-1), signs]),)
    noise_parts = (
        noise_slabs,
        passed_along(noise_slabs[:, :, :, K - 1:], "ta", 1),
        passed_along(noise_slabs[:, :, :, :1], "ta", -1),
        passed_along(noise_slabs[:, :, :, :, Z - 1:], "sa", 1),
        passed_along(noise_slabs[:, :, :, :, :1], "sa", -1),
    )
    link_parts = (
        gauge_links,
        passed_along(gauge_links[3, :, :, :, -1:, :, :], "ta", 1),
        passed_along(gauge_links[2, :, :, :, :, -1:, :], "sa", 1),
    )
    spinor, t_first, t_last, z_first, z_last = hopping_step(True, scalars, noise_parts, link_parts, ())
    halos = (
        passed_along(t_last, "ta", 1),
        passed_along(t_first, "ta", -1),
        passed_along(z_last, "sa", 1),
        passed_along(z_first, "sa", -1),
    )
    rounded = hopping_step(False, scalars, noise_parts, link_parts, (spinor,) + halos)
    first_half = jnp.where(section_index == 0, vectors, partner_vectors)
    second_half = jnp.where(section_index == 0, partner_vectors, vectors)
    partial_value = intersection_part(rounded, jnp.concatenate([first_half, second_half], axis=1))
    return reduce_scatter_sa(partial_value)


def solution(mesh):
    in_specs = (
        P(None, None, None, None, "ta", "sa", None),
        P("sec", None, None, "ta", "sa", None),
        P(),
        P("ta", "sec", None, None, "sa", None),
    )
    out_specs = P("sec", None, None, "ta", "sa")
    return jax.shard_map(local_body, mesh=mesh, in_specs=in_specs, out_specs=out_specs, check_vma=False)
```

```python
import functools

import jax
import jax.numpy as jnp
from jax import lax
from jax.experimental import pallas as pl
from jax.experimental.pallas import tpu as pltpu
from jax.sharding import PartitionSpec as P


NX = 32
TDIL = 4
INTERPRET = False


kappa_hop = 0.12
GAMMA_PERM = ((3, 2, 1, 0), (3, 2, 1, 0), (2, 3, 0, 1), (2, 3, 0, 1))
GAMMA_REAL = ((0, 0, 0, 0), (-1, 1, 1, -1), (0, 0, 0, 0), (1, 1, 1, 1))
GAMMA_IMAG = ((1, 1, -1, -1), (0, 0, 0, 0), (1, -1, -1, 1), (0, 0, 0, 0))


def passed_along(value, axis, steps):
    count = lax.axis_size(axis)
    pairs = [(source, (source + steps) % count) for source in range(count)]
    return lax.ppermute(value, axis, pairs)


def from_partner(x, axis, stride):
    return lax.ppermute(x, axis, [(i, i ^ 1 << stride) for i in range(lax.axis_size(axis))])


def times_phase(re, im, cr, ci):
    if ci == 0:
        if cr == 1:
            return re, im
        return -re, -im
    if ci == 1:
        return -im, re
    return im, -re


def add_phase(are, aim, re, im, cr, ci):
    if ci == 0:
        if cr == 1:
            return are + re, aim + im
        return are - re, aim - im
    if ci == 1:
        return are - im, aim + re
    return are + im, aim - re


def hop_kernel(first, *refs):
    (scal_ref, noise_ref, ntlo_ref, nthi_ref, nzlo_ref, nzhi_ref, u_ref, utedge_ref, uzedge_ref) = refs[:9]
    rest = refs[9:]
    if first:
        out_ref, tfirst_ref, tlast_ref, zfirst_ref, zlast_ref = rest[:5]
        scratch = rest[5:]
    else:
        psi_ref, tlo_ref, thi_ref, zlo_ref, zhi_ref = rest[:5]
        out_ref = rest[5]
        scratch = rest[6:]
    pad_ref, src_ref, zlo_s, zhi_s, u8, ut8, uz8 = scratch
    S, C, RI, T, ROWS, L = src_ref.shape
    Z = ROWS // 2
    K = noise_ref.shape[3]
    span = T // K
    h = pl.program_id(0)
    R = 2 * pl.num_programs(0)
    smask = lambda i: scal_ref[i]
    tmask = lambda i: scal_ref[R * S + i]
    sign = lambda i: scal_ref[R * S + R * (T + 2) + i]
    lower = pl.ds(0, Z)
    upper = pl.ds(Z, Z)

    @pl.when(h == 0)
    def _():
        for a in range(3):
            for b in range(3):
                for ri in range(RI):
                    for half in (lower, upper):
                        ut8[a, b, ri, pl.ds(0, 1), half] = utedge_ref[a, b, ri]
                        ut8[a, b, ri, pl.ds(1, T), half] = u_ref[3, a, b, ri]
                        for t in range(T):
                            uz8[a, b, ri, t, half] = jnp.broadcast_to(uzedge_ref[a, b, ri, t], (Z, L))
                        for mu in range(4):
                            u8[mu, a, b, ri, :, half] = u_ref[mu, a, b, ri]

    for s in range(S):
        for c in range(C):
            for ri in range(RI):
                for g, half in ((0, lower), (1, upper)):
                    r = 2 * h + g
                    fs = smask(r * S + s)
                    for t in range(T):
                        src_ref[s, c, ri, t, half] = noise_ref[g, c, ri, t // span] * (
                            fs * tmask(r * (T + 2) + t + 1))
                    if first:
                        pad_ref[s, c, ri, 0, half] = ntlo_ref[g, c, ri, 0] * (
                            fs * tmask(r * (T + 2)) * sign(0))
                        pad_ref[s, c, ri, T + 1, half] = nthi_ref[g, c, ri, 0] * (
                            fs * tmask(r * (T + 2) + T + 1) * sign(1))
                        for t in range(T):
                            f = fs * tmask(r * (T + 2) + t + 1)
                            zlo_s[s, c, ri, t, half] = jnp.broadcast_to(nzlo_ref[g, c, ri, t // span] * f, (Z, L))
                            zhi_s[s, c, ri, t, half] = jnp.broadcast_to(nzhi_ref[g, c, ri, t // span] * f, (Z, L))
                    else:
                        for t in range(T):
                            if s < 2:
                                zlo_s[s, c, ri, t, half] = jnp.broadcast_to(zlo_ref[s, c, ri, t, pl.ds(g, 1)], (Z, L))
                                zhi_s[s, c, ri, t, half] = jnp.broadcast_to(zhi_ref[s, c, ri, t, pl.ds(g, 1)], (Z, L))
                            else:
                                zlo_s[s, c, ri, t, half] = jnp.zeros((Z, L), jnp.float32)
                                zhi_s[s, c, ri, t, half] = jnp.zeros((Z, L), jnp.float32)
                if first:
                    pad_ref[s, c, ri, pl.ds(1, T)] = src_ref[s, c, ri]
                else:
                    pad_ref[s, c, ri, pl.ds(1, T)] = psi_ref[s, c, ri]
                    if s < 2:
                        pad_ref[s, c, ri, pl.ds(0, 1)] = tlo_ref[s, c, ri].astype(jnp.float32) * sign(0)
                        pad_ref[s, c, ri, pl.ds(T + 1, 1)] = thi_ref[s, c, ri].astype(jnp.float32) * sign(1)
                    else:
                        pad_ref[s, c, ri, pl.ds(0, 1)] = jnp.zeros((1, ROWS, L), jnp.float32)
                        pad_ref[s, c, ri, pl.ds(T + 1, 1)] = jnp.zeros((1, ROWS, L), jnp.float32)
    xpos = lax.broadcasted_iota(jnp.int32, (ROWS, L), 1) % NX
    zpos = lax.broadcasted_iota(jnp.int32, (ROWS, L), 0) % Z
    x_last = xpos == NX - 1
    x_first = xpos == 0
    z_last = zpos == Z - 1
    z_first = zpos == 0

    def x_back(v):
        return jnp.where(x_first, pltpu.roll(v, L - NX + 1, axis=1), pltpu.roll(v, 1, axis=1))

    def body(t, carry):
        acc = [[[None, None] for _ in range(3)] for _ in range(4)]

        def shifted(s, c, ri, mu, stride):
            if mu == 3:
                return pad_ref[s, c, ri, t + 1 + stride]
            v = pad_ref[s, c, ri, t + 1]
            if mu == 2:
                if stride == 1:
                    return jnp.where(z_last, zhi_s[s, c, ri, t], pltpu.roll(v, ROWS - 1, axis=0))
                return jnp.where(z_first, zlo_s[s, c, ri, t], pltpu.roll(v, 1, axis=0))
            if mu == 1:
                return pltpu.roll(v, (L - NX) if stride == 1 else NX, axis=1)
            if stride == 1:
                return jnp.where(x_last, pltpu.roll(v, NX - 1, axis=1), pltpu.roll(v, L - 1, axis=1))
            return x_back(v)

        def back_link(mu, a, b, ri):
            if mu == 3:
                return ut8[a, b, ri, t]
            v = u8[mu, a, b, ri, t]
            if mu == 2:
                return jnp.where(z_first, uz8[a, b, ri, t], pltpu.roll(v, 1, axis=0))
            if mu == 1:
                return pltpu.roll(v, NX, axis=1)
            return x_back(v)

        for mu in range(4):
            perm = GAMMA_PERM[mu]
            heads = [0, 1]
            for stride in (1, -1):
                orient = -1 if stride == 1 else 1
                half = []
                for s in heads:
                    p = perm[s]
                    cr, ci = orient * GAMMA_REAL[mu][s], orient * GAMMA_IMAG[mu][s]
                    colours = []
                    for c in range(3):
                        sre = shifted(s, c, 0, mu, stride)
                        sim = shifted(s, c, 1, mu, stride)
                        colours.append(add_phase(sre, sim, shifted(p, c, 0, mu, stride), shifted(p, c, 1, mu, stride), cr, ci))
                    half.append(colours)
                if stride == 1:
                    links = [[(u8[mu, a, b, 0, t], u8[mu, a, b, 1, t]) for b in range(3)] for a in range(3)]
                else:
                    links = [[(back_link(mu, b, a, 0), back_link(mu, b, a, 1)) for b in range(3)] for a in range(3)]
                for k, s in enumerate(heads):
                    p = perm[s]
                    cpr, cpi = orient * GAMMA_REAL[mu][p], orient * GAMMA_IMAG[mu][p]
                    for a in range(3):
                        sum_re = None
                        sum_im = None
                        for b in range(3):
                            hre, him = half[k][b]
                            lre, lim = links[a][b]
                            if stride == 1:
                                tre = lre * hre - lim * him
                                tim = lre * him + lim * hre
                            else:
                                tre = lre * hre + lim * him
                                tim = lre * him - lim * hre
                            sum_re = tre if sum_re is None else sum_re + tre
                            sum_im = tim if sum_im is None else sum_im + tim
                        if acc[s][a][0] is None:
                            acc[s][a] = [sum_re, sum_im]
                        else:
                            acc[s][a] = [acc[s][a][0] + sum_re, acc[s][a][1] + sum_im]
                        if acc[p][a][0] is None:
                            acc[p][a] = list(times_phase(sum_re, sum_im, cpr, cpi))
                        else:
                            acc[p][a] = list(add_phase(acc[p][a][0], acc[p][a][1], sum_re, sum_im, cpr, cpi))
        for s in range(4):
            for c in range(3):
                for ri in range(2):
                    psi = pad_ref[s, c, ri, t + 1]
                    src = src_ref[s, c, ri, t]
                    residual = src - (psi - kappa_hop * acc[s][c][ri])
                    value = psi + residual
                    if first:
                        out_ref[s, c, ri, t] = value
                    else:
                        for g in range(2):
                            out_ref[s, c, ri, t, g] = value[g * Z:(g + 1) * Z].astype(out_ref.dtype)
        return carry

    lax.fori_loop(0, T, body, 0)
    if first:
        for mu, stride, target, pick in (
            (3, 1, tfirst_ref, lambda s, c, ri: out_ref[s, c, ri, pl.ds(0, 1)]),
            (3, -1, tlast_ref, lambda s, c, ri: out_ref[s, c, ri, pl.ds(T - 1, 1)]),
        ):
            for k, (re, im) in enumerate(half_spinor(pick, mu, stride)):
                for c in range(C):
                    target[k, c, 0] = re[c].astype(target.dtype)
                    target[k, c, 1] = im[c].astype(target.dtype)
        for g in range(2):
            for mu, stride, target, row in ((2, 1, zfirst_ref, g * Z), (2, -1, zlast_ref, g * Z + Z - 1)):
                pick = lambda s, c, ri: out_ref[s, c, ri, :, pl.ds(row, 1), :]
                for k, (re, im) in enumerate(half_spinor(pick, mu, stride)):
                    for c in range(C):
                        target[k, c, 0, :, pl.ds(g, 1), :] = re[c]
                        target[k, c, 1, :, pl.ds(g, 1), :] = im[c]


def half_spinor(pick, mu, stride):
    orient = -1 if stride == 1 else 1
    rows = []
    for s in (0, 1):
        p = GAMMA_PERM[mu][s]
        cr, ci = orient * GAMMA_REAL[mu][s], orient * GAMMA_IMAG[mu][s]
        res, ims = [], []
        for c in range(3):
            pre, pim = times_phase(pick(p, c, 0), pick(p, c, 1), cr, ci)
            res.append(pick(s, c, 0) + pre)
            ims.append(pick(s, c, 1) + pim)
        rows.append((res, ims))
    return rows


def hopping_step(first, scalars, noise_parts, link_parts, spinor_parts):
    R, C, RI, K, Z, L = noise_parts[0].shape
    T = link_parts[0].shape[4]
    S = 4
    H = R // 2
    ROWS = 2 * Z
    index = lambda h: (h,) + (0,) * 6
    index6 = lambda h: (h,) + (0,) * 5
    whole = lambda x: pl.BlockSpec(x.shape, lambda h: (0,) * x.ndim)
    smem = pl.BlockSpec(memory_space=pltpu.SMEM)
    site_block = pl.BlockSpec((None, S, C, RI, T, ROWS, L), index)
    t_block = pl.BlockSpec((None, 2, C, RI, 1, ROWS, L), index)
    z_block = pl.BlockSpec((None, 2, C, RI, T, 2, L), index)
    noise_specs = [
        pl.BlockSpec((2, C, RI, K, Z, L), index6),
        pl.BlockSpec((2, C, RI, 1, Z, L), index6),
        pl.BlockSpec((2, C, RI, 1, Z, L), index6),
        pl.BlockSpec((2, C, RI, K, 1, L), index6),
        pl.BlockSpec((2, C, RI, K, 1, L), index6),
    ]
    in_specs = [smem] + noise_specs + [whole(x) for x in link_parts]
    site_shape = (H, S, C, RI, T, ROWS, L)
    if first:
        t_shape = jax.ShapeDtypeStruct((H, 2, C, RI, 1, ROWS, L), jnp.bfloat16)
        z_shape = jax.ShapeDtypeStruct((H, 2, C, RI, T, 2, L), jnp.float32)
        out_shape = [jax.ShapeDtypeStruct(site_shape, jnp.float32), t_shape, t_shape, z_shape, z_shape]
        out_specs = [site_block, t_block, t_block, z_block, z_block]
    else:
        in_specs += [site_block, t_block, t_block, z_block, z_block]
        out_shape = jax.ShapeDtypeStruct((H, S, C, RI, T, 2, Z, L), jnp.bfloat16)
        out_specs = pl.BlockSpec((None, S, C, RI, T, 2, Z, L), lambda h: (h,) + (0,) * 7)
    scratch = [
        pltpu.VMEM((S, C, RI, T + 2, ROWS, L), jnp.float32),
        pltpu.VMEM((S, C, RI, T, ROWS, L), jnp.float32),
        pltpu.VMEM((S, C, RI, T, ROWS, L), jnp.float32),
        pltpu.VMEM((S, C, RI, T, ROWS, L), jnp.float32),
        pltpu.VMEM((4, 3, 3, RI, T, ROWS, L), jnp.float32),
        pltpu.VMEM((3, 3, RI, T + 1, ROWS, L), jnp.float32),
        pltpu.VMEM((3, 3, RI, T, ROWS, L), jnp.float32),
    ]
    return pl.pallas_call(
        functools.partial(hop_kernel, first),
        grid=(H,),
        in_specs=in_specs,
        out_specs=out_specs,
        out_shape=out_shape,
        scratch_shapes=scratch,
        compiler_params=pltpu.CompilerParams(dimension_semantics=("arbitrary",)),
        interpret=INTERPRET,
    )(*scalars, *noise_parts, *link_parts, *spinor_parts)


def reduce_scatter_sa(partial_value):
    n = lax.axis_size("sa")
    if n & (n - 1):
        return lax.psum_scatter(partial_value, "sa", scatter_dimension=4, tiled=True)
    lead = partial_value.shape[:-1]
    width = partial_value.shape[-1] // n
    x = jnp.moveaxis(partial_value.reshape(lead + (n, width)), -2, 0)
    me = lax.axis_index("sa")
    d = 1
    while d < n:
        x = x.reshape((x.shape[0] // 2, 2) + x.shape[1:])
        odd = (me // d) % 2 == 1
        keep = jnp.where(odd, x[:, 1], x[:, 0])
        send = jnp.where(odd, x[:, 0], x[:, 1])
        x = keep + lax.ppermute(send, "sa", [(j, j ^ d) for j in range(n)])
        d *= 2
    return x[0]


def intersection_part(rounded, vector_piece):
    products = jnp.einsum(
        "tvcazs,hqcbtgzs->hgqabtv", vector_piece, rounded, preferred_element_type=jnp.float32
    )
    products = products.reshape((-1,) + products.shape[2:])
    real_part = products[:, :, 0, 0] + products[:, :, 1, 1]
    imag_part = products[:, :, 0, 1] - products[:, :, 1, 0]
    return jnp.stack([real_part, imag_part], axis=2)


def local_body(gauge_links, noise_slabs, offsets, vectors):
    partner_vectors = from_partner(vectors, "sec", 0)
    batch_rows = noise_slabs.shape[0]
    slab_length = gauge_links.shape[4]
    Z = gauge_links.shape[5]
    K = noise_slabs.shape[3]
    section_index = lax.axis_index("sec")
    slab_index = lax.axis_index("ta")
    slab_count = lax.axis_size("ta")
    lower_sign = jnp.where(slab_index == 0, -1.0, 1.0).astype(jnp.float32)
    upper_sign = jnp.where(slab_index == slab_count - 1, -1.0, 1.0).astype(jnp.float32)
    signs = jnp.stack([lower_sign, upper_sign])
    t_start = slab_index * slab_length
    own_offsets = lax.dynamic_slice_in_dim(offsets, section_index * batch_rows, batch_rows)
    rhs_index = section_index * batch_rows + jnp.arange(batch_rows)
    spin_mask = (jnp.arange(4)[None, :] == rhs_index[:, None] % 4).astype(jnp.float32)
    times = t_start - 1 + jnp.arange(slab_length + 2)
    time_mask = (times[None, :] % TDIL == own_offsets[:, None]).astype(jnp.float32)
    scalars = (jnp.concatenate([spin_mask.reshape(-1), time_mask.reshape(-1), signs]),)
    noise_parts = (
        noise_slabs,
        passed_along(noise_slabs[:, :, :, K - 1:], "ta", 1),
        passed_along(noise_slabs[:, :, :, :1], "ta", -1),
        passed_along(noise_slabs[:, :, :, :, Z - 1:], "sa", 1),
        passed_along(noise_slabs[:, :, :, :, :1], "sa", -1),
    )
    link_parts = (
        gauge_links,
        passed_along(gauge_links[3, :, :, :, -1:, :, :], "ta", 1),
        passed_along(gauge_links[2, :, :, :, :, -1:, :], "sa", 1),
    )
    spinor, t_first, t_last, z_first, z_last = hopping_step(True, scalars, noise_parts, link_parts, ())
    halos = (
        passed_along(t_last, "ta", 1),
        passed_along(t_first, "ta", -1),
        passed_along(z_last, "sa", 1),
        passed_along(z_first, "sa", -1),
    )
    rounded = hopping_step(False, scalars, noise_parts, link_parts, (spinor,) + halos)
    own_first = intersection_part(rounded, jnp.concatenate([vectors, partner_vectors], axis=1))
    half = vectors.shape[1]
    partial_value = jnp.where(section_index == 0, own_first, jnp.roll(own_first, half, axis=4))
    return reduce_scatter_sa(partial_value)


def solution(mesh):
    in_specs = (
        P(None, None, None, None, "ta", "sa", None),
        P("sec", None, None, "ta", "sa", None),
        P(),
        P("ta", "sec", None, None, "sa", None),
    )
    out_specs = P("sec", None, None, "ta", "sa")
    return jax.shard_map(local_body, mesh=mesh, in_specs=in_specs, out_specs=out_specs, check_vma=False)
```
